32 devices in a mesh: req: 16 (over z, y, x), tp: 2 (over core).
Axes of the slice: x: 2, y: 2, z: 4, core: 2. Of those that a mesh axis runs over, the one named last changes fastest.
Arguments:
- queries: bfloat16 [10240, 4096], P('req', 'tp'), may hold values from -60 to 60
- rotated_key_rows: bfloat16 [10240, 1024], P('req', 'tp'), may hold values from -9 to 9
- stream_value_rows: bfloat16 [10240, 1024], P('req', 'tp'), may hold values from -6 to 6
- out_weight: bfloat16 [4096, 8192], P('tp'), may hold values from -0.5 to 0.5
- short_pages: int32 [51], replicated, may hold values from 1 to 4, 128 in all
- short_fill: int32 [51], replicated, may hold values from 1 to 16
- stream_page_table: int32 [640], replicated, may hold values from 0 to 767, as said below
Outputs:
- mixed: bfloat16 [10240, 8192], P(('req', 'tp'))
- cache_pages: bfloat16 [2, 768, 16, 1024], P(None, 'req', None, 'tp')
The draws below stay inside these ranges and needn't reach their ends.
Inputs may be any that keep to these rules, and one draw needn't show every extreme that they name: `stream_page_table`: entries are distinct. Owner = entry // 48. Of the 40 pages of one block of the stream at most 3 have one owner; in every draw some owner gets 3 pages from every block.
All inputs are finite; a program needn't handle non-finite values.
Results may differ from the reference program's by a relative error of at most 0.0061.
Values may be sent and summed in bfloat16 or wider, within the bound.
No kernel may reach another device: no remote copies, remote signals or barrier semaphores. Data moves between devices by JAX's collectives and lax.ppermute only.
A program may use at most 192 MiB of HBM per device.

```python
import math
import jax
import jax.numpy as jnp
import numpy as np
from jax import lax

D = 8192
QUERY_HEADS = 32
KEY_VALUE_HEADS = 8
HEAD_SIZE = 128
LONG_DEV = 512
SHORT_DEV = 128
PAGE_ROWS = 16
MAXLEN = 64
BLOCK_TOKENS = 640
STREAM_ROWS = 10240
SPAGES = 128
NSHORT = 51
PPD = 40
CAPP = 3
OWNER_PAGES = 48
STREAM_PAGES = 640
N_REQ = 16
N_TP = 2


def query_key_pair(key):
    key_offset = jnp.clip(jax.random.normal(jax.random.fold_in(key, 21), (STREAM_ROWS, KEY_VALUE_HEADS * HEAD_SIZE), jnp.float32), -6.0, 6.0)
    query_base = 1.5 * jnp.clip(jax.random.normal(jax.random.fold_in(key, 22), (STREAM_ROWS, QUERY_HEADS * HEAD_SIZE), jnp.float32), -6.0, 6.0)
    return (query_base, key_offset)


def draw_queries(key, part):
    return query_key_pair(key)[0].astype(jnp.bfloat16)


def draw_rotated_key_rows(key, part):
    return query_key_pair(key)[1].astype(jnp.bfloat16)


def draw_stream_page_table(key, part):
    block_ids = jnp.arange(N_REQ, dtype=jnp.int32)
    orders = jax.vmap(lambda block_id: jax.random.permutation(jax.random.fold_in(key, block_id), N_REQ))(block_ids).astype(jnp.int32)
    starred = jax.random.randint(jax.random.fold_in(key, 999), (), 0, N_REQ).astype(jnp.int32)
    orders = jnp.where(orders == starred, orders[:, :1], orders)
    orders = orders.at[:, 0].set(starred)
    shuffles = jax.vmap(lambda block_id: jax.random.permutation(jax.random.fold_in(key, 3000 + block_id), PPD))(block_ids).astype(jnp.int32)
    owners = jnp.take_along_axis(orders, shuffles % N_REQ, axis=1)
    within = shuffles // N_REQ
    raw_slot = block_ids[:, None] * CAPP + within
    slot_orders = jax.vmap(lambda owner_id: jax.random.permutation(jax.random.fold_in(key, 7000 + owner_id), OWNER_PAGES))(block_ids).astype(jnp.int32)
    slot_ids = slot_orders[owners, raw_slot]
    return (owners * OWNER_PAGES + slot_ids).reshape(-1).astype(jnp.int32)


def with_ends(array, rng, least, largest):
    longest = array.shape.index(max(array.shape))
    spots = []
    for shift in (0, 1):
        where = [jax.random.randint(jax.random.fold_in(rng, axis), (), 0, length) for axis, length in enumerate(array.shape)]
        where[longest] = (where[longest] + shift) % array.shape[longest]
        spots.append(tuple(where))
    return array.at[spots[0]].set(least).at[spots[1]].set(largest)


def shard_levels(rng, shape, pieces, smallest, high):
    factor_of, own = 1.0, jax.random.fold_in(rng, 6)
    for axis_at, shards_of in pieces:
        heights = jnp.exp(jax.random.uniform(jax.random.fold_in(own, axis_at), (shards_of,), jnp.float32, smallest / len(pieces), high / len(pieces)))
        factor_of = factor_of * jnp.repeat(heights, shape[axis_at] // shards_of).reshape([-1 if axis == axis_at else 1 for axis in range(len(shape))])
    return factor_of


def length_profile(amount, total, reach, skew):
    portions = [(1 << 20) // math.isqrt(standing ** skew) + 1 for standing in range(2, amount + 1)]
    rest, given = total - reach - (amount - 1), [1] * (amount - 1)
    while rest > 0:
        free = [i for i in range(amount - 1) if given[i] < reach]
        whole, remaining = sum([portions[i] for i in free]), rest
        for i in free:
            extra = min(reach - given[i], max(1, remaining * portions[i] // whole), rest)
            given[i] = given[i] + extra
            rest = rest - extra
    return np.array([reach] + given)


def ragged(stream_key, count, total, reach, slope):
    if count == 2:
        one = jax.random.randint(stream_key, (), max(1, total - reach), min(reach, total - 1) + 1)
        return jnp.stack([one, total - one])
    tallies = jnp.asarray(length_profile(count, total, reach, slope), jnp.int32)
    couples = (count - 1) // 2
    source_of, taker = tallies[1:1 + 2 * couples:2], tallies[2:2 + 2 * couples:2]
    margin = jnp.minimum(source_of - 1, reach - taker)
    moved = jax.random.randint(jax.random.fold_in(stream_key, 1), (couples,), 0, 1 << 20) % (margin + 1)
    tallies = tallies.at[1:1 + 2 * couples:2].set(source_of - moved).at[2:2 + 2 * couples:2].set(taker + moved)
    return tallies[jax.random.permutation(jax.random.fold_in(stream_key, 2), count)]


def noise(key, shape, deviation, most, shards=(), kind=jnp.bfloat16):
    loudness = shard_levels(key, shape, shards, -0.22, 0.18) if shards else 1.0
    entries = jax.random.normal(key, shape, jnp.float32) * deviation * loudness
    return jnp.minimum(jnp.maximum(entries, -most), most).astype(kind)


def setup_inputs(seed: int = 0) -> dict:
    key_of = jax.random.split(jax.random.key(seed), 8)
    queries = draw_queries(jax.random.fold_in(key_of[7], 71), 0)
    rotated_key_rows = draw_rotated_key_rows(jax.random.fold_in(key_of[7], 71), 0)
    stream_value_rows = noise(key_of[2], (STREAM_ROWS, KEY_VALUE_HEADS * HEAD_SIZE), 1.0, 6.0, ((0, 16), (1, 2)))
    out_weight = noise(key_of[3], (QUERY_HEADS * HEAD_SIZE, D), HEAD_SIZE ** -0.5, 0.5, ((0, 2),))
    short_pages = ragged(key_of[4], NSHORT, SPAGES, MAXLEN // PAGE_ROWS, 1).astype(jnp.int32)
    short_fill = with_ends(jax.random.randint(key_of[5], (NSHORT,), 1, PAGE_ROWS + 1), jax.random.fold_in(key_of[5], 1), 1, PAGE_ROWS).astype(jnp.int32)
    stream_page_table = draw_stream_page_table(jax.random.fold_in(key_of[7], 71), 0)
    return dict(queries=queries, rotated_key_rows=rotated_key_rows, stream_value_rows=stream_value_rows, out_weight=out_weight, short_pages=short_pages, short_fill=short_fill, stream_page_table=stream_page_table)


NEGATIVE_FILL = -1e30


def stream_layout(short_pages, short_fill, req_count):
    token_id = jnp.arange(req_count * BLOCK_TOKENS, dtype=jnp.int32)
    device_block = token_id // BLOCK_TOKENS
    in_block = token_id % BLOCK_TOKENS
    is_long = in_block < LONG_DEV
    offset = jnp.where(is_long, 0, device_block * SHORT_DEV + in_block - LONG_DEV).astype(jnp.int32)
    page_id = offset // PAGE_ROWS
    page_ends = jnp.cumsum(short_pages).astype(jnp.int32)
    page_starts = (page_ends - short_pages).astype(jnp.int32)
    limits = (page_starts * PAGE_ROWS + (short_pages - 1) * PAGE_ROWS + short_fill).astype(jnp.int32)
    owner_hit = page_ends[None, :] <= page_id[:, None]
    prompt = jnp.sum(owner_hit.astype(jnp.int32), axis=1).astype(jnp.int32)
    select = jnp.arange(short_pages.shape[0], dtype=jnp.int32)[None, :] == prompt[:, None]
    begin_at = jnp.sum(jnp.where(select, page_starts[None, :], 0), axis=1).astype(jnp.int32) * PAGE_ROWS
    limit_at = jnp.sum(jnp.where(select, limits[None, :], 0), axis=1).astype(jnp.int32)
    segment = jnp.where(is_long, 0, prompt + 1).astype(jnp.int32)
    position = jnp.where(is_long, device_block * LONG_DEV + in_block, offset - begin_at).astype(jnp.int32)
    is_valid = is_long | (offset < limit_at)
    return segment, position, is_valid


def reference(queries, rotated_key_rows, stream_value_rows, out_weight, short_pages, short_fill, stream_page_table):
    segment, position, is_valid = stream_layout(short_pages, short_fill, N_REQ)
    query_group_size = QUERY_HEADS // KEY_VALUE_HEADS

    def block_attention(block_id):
        start_offset = block_id * BLOCK_TOKENS
        query_block = lax.dynamic_slice_in_dim(queries, start_offset, BLOCK_TOKENS, 0).astype(jnp.float32).reshape(BLOCK_TOKENS, KEY_VALUE_HEADS, query_group_size, HEAD_SIZE)
        q_seg = lax.dynamic_slice_in_dim(segment, start_offset, BLOCK_TOKENS, 0)
        q_pos = lax.dynamic_slice_in_dim(position, start_offset, BLOCK_TOKENS, 0)
        q_live = lax.dynamic_slice_in_dim(is_valid, start_offset, BLOCK_TOKENS, 0)

        def advance(step_id, carried):
            row_max, denom, weighted = carried
            leading_row = step_id * BLOCK_TOKENS
            key_portion = lax.dynamic_slice_in_dim(rotated_key_rows, leading_row, BLOCK_TOKENS, 0).astype(jnp.float32).reshape(BLOCK_TOKENS, KEY_VALUE_HEADS, HEAD_SIZE)
            value_portion = lax.dynamic_slice_in_dim(stream_value_rows, leading_row, BLOCK_TOKENS, 0).astype(jnp.float32).reshape(BLOCK_TOKENS, KEY_VALUE_HEADS, HEAD_SIZE)
            k_seg = lax.dynamic_slice_in_dim(segment, leading_row, BLOCK_TOKENS, 0)
            k_pos = lax.dynamic_slice_in_dim(position, leading_row, BLOCK_TOKENS, 0)
            k_live = lax.dynamic_slice_in_dim(is_valid, leading_row, BLOCK_TOKENS, 0)
            allowed = (q_seg[:, None] == k_seg[None, :]) & (k_pos[None, :] <= q_pos[:, None]) & k_live[None, :]
            scores = jnp.einsum("qhgd,khd->qhgk", query_block, key_portion) * (HEAD_SIZE ** -0.5)
            scores = jnp.where(allowed[:, None, None, :], scores, NEGATIVE_FILL)
            new_max = jnp.maximum(row_max, jnp.max(scores, axis=-1))
            factor = jnp.exp(row_max - new_max)
            weights = jnp.exp(scores - new_max[..., None])
            denom = denom * factor + jnp.sum(weights, axis=-1)
            rounded = lax.optimization_barrier(weights.astype(jnp.bfloat16)).astype(jnp.float32)
            weighted = weighted * factor[..., None] + jnp.einsum("qhgk,khd->qhgd", rounded, value_portion)
            return new_max, denom, weighted

        initial_state = (jnp.full((BLOCK_TOKENS, KEY_VALUE_HEADS, query_group_size), NEGATIVE_FILL, jnp.float32),
                       jnp.zeros((BLOCK_TOKENS, KEY_VALUE_HEADS, query_group_size), jnp.float32),
                       jnp.zeros((BLOCK_TOKENS, KEY_VALUE_HEADS, query_group_size, HEAD_SIZE), jnp.float32))
        row_max, denom, weighted = lax.fori_loop(0, block_id + 1, advance, initial_state)
        attended = weighted / denom[..., None]
        attended = jnp.where(q_live[:, None, None, None], attended, 0.0)
        return attended.reshape(BLOCK_TOKENS, QUERY_HEADS * HEAD_SIZE).astype(jnp.bfloat16)

    attended = lax.map(block_attention, jnp.arange(N_REQ, dtype=jnp.int32)).reshape(STREAM_ROWS, QUERY_HEADS * HEAD_SIZE)
    width = QUERY_HEADS * HEAD_SIZE // N_TP
    mixed = jnp.zeros((STREAM_ROWS, D), jnp.float32)
    for group_id in range(N_TP):
        partial_value = jnp.dot(attended[:, group_id * width:(group_id + 1) * width],
                          out_weight[group_id * width:(group_id + 1) * width],
                          preferred_element_type=jnp.float32)
        mixed = mixed + lax.optimization_barrier(partial_value.astype(jnp.bfloat16)).astype(jnp.float32)
    mixed = mixed.astype(jnp.bfloat16)
    stacked_pages = jnp.stack([rotated_key_rows, stream_value_rows])
    stacked_pages = jnp.where(is_valid[None, :, None], stacked_pages, jnp.zeros_like(stacked_pages))
    stacked_pages = stacked_pages.reshape(2, STREAM_PAGES, PAGE_ROWS, KEY_VALUE_HEADS * HEAD_SIZE)
    written_cache = jnp.zeros((2, N_REQ * OWNER_PAGES, PAGE_ROWS, KEY_VALUE_HEADS * HEAD_SIZE), jnp.bfloat16).at[:, stream_page_table].set(stacked_pages)
    return mixed, written_cache
```

```python
import functools

import jax
import jax.numpy as jnp
from jax import lax
from jax.experimental import pallas as pl
from jax.experimental.pallas import tpu as pltpu
from jax.sharding import PartitionSpec as P

HEAD_SIZE = 128
LONG_DEV = 512
SHORT_DEV = 128
PAGE_ROWS = 16
BLOCK_TOKENS = 640


NEGATIVE_FILL = -1e30


def short_layout(offset, short_pages, short_fill):
    page_id = offset // PAGE_ROWS
    page_ends = jnp.cumsum(short_pages)
    page_starts = page_ends - short_pages
    limits = page_starts * PAGE_ROWS + (short_pages - 1) * PAGE_ROWS + short_fill
    owner_hit = page_ends[None, :] <= page_id[:, None]
    prompt = jnp.sum(owner_hit.astype(jnp.int32), axis=1)
    select = jnp.arange(short_pages.shape[0], dtype=jnp.int32)[None, :] == prompt[:, None]
    begin_at = jnp.sum(jnp.where(select, page_starts[None, :], 0), axis=1) * PAGE_ROWS
    limit_at = jnp.sum(jnp.where(select, limits[None, :], 0), axis=1)
    return (prompt, offset - begin_at, offset < limit_at)


def flash_kernel(b_ref, q_ref, k_ref, v_ref, o_ref, m_sc, l_sc, acc_sc, *, group, tq, nb):
    i = pl.program_id(1)
    j = pl.program_id(2)
    b = b_ref[0]
    scale = HEAD_SIZE ** (-0.5)

    @pl.when(j == 0)
    def _init():
        m_sc[...] = jnp.full(m_sc.shape, NEGATIVE_FILL, jnp.float32)
        l_sc[...] = jnp.zeros(l_sc.shape, jnp.float32)
        acc_sc[...] = jnp.zeros(acc_sc.shape, jnp.float32)

    def step(masked):
        k = k_ref[...]
        v = v_ref[...]
        if masked:
            rows = i * tq + lax.broadcasted_iota(jnp.int32, (tq, k.shape[0]), 0)
            cols = lax.broadcasted_iota(jnp.int32, (tq, k.shape[0]), 1)
            allowed = cols <= rows
        for g in range(group):
            qg = q_ref[:, g * HEAD_SIZE:(g + 1) * HEAD_SIZE]
            s = lax.dot_general(
                qg, k, (((1,), (1,)), ((), ())), preferred_element_type=jnp.float32
            ) * scale
            if masked:
                s = jnp.where(allowed, s, NEGATIVE_FILL)
            m_prev = m_sc[g]
            m_new = jnp.maximum(m_prev, jnp.max(s, axis=1, keepdims=True))
            p = jnp.exp(s - m_new[:, :1])
            alpha = jnp.exp(m_prev - m_new)
            l_sc[g] = alpha * l_sc[g] + jnp.sum(p, axis=1, keepdims=True)
            acc_sc[g] = acc_sc[g] * alpha + lax.dot_general(
                p.astype(jnp.bfloat16), v, (((1,), (0,)), ((), ())),
                preferred_element_type=jnp.float32,
            )
            m_sc[g] = m_new

    @pl.when(j < b)
    def _full():
        step(False)

    @pl.when(j == b)
    def _diag():
        step(True)

    @pl.when(j == nb - 1)
    def _fin():
        for g in range(group):
            o_ref[:, g * HEAD_SIZE:(g + 1) * HEAD_SIZE] = (acc_sc[g] / l_sc[g]).astype(o_ref.dtype)


def long_attention(my_index, q_long, kv_long):
    rows, q_cols = q_long.shape
    kv_cols = kv_long.shape[1] // 2
    heads_kv = kv_cols // HEAD_SIZE
    group = q_cols // kv_cols
    nb = kv_long.shape[0] // LONG_DEV
    tq = LONG_DEV
    kernel = functools.partial(flash_kernel, group=group, tq=tq, nb=nb)
    grid_spec = pltpu.PrefetchScalarGridSpec(
        num_scalar_prefetch=1,
        grid=(heads_kv, rows // tq, nb),
        in_specs=[
            pl.BlockSpec((tq, group * HEAD_SIZE), lambda h, i, j, b: (i, h)),
            pl.BlockSpec((LONG_DEV, HEAD_SIZE), lambda h, i, j, b: (jnp.minimum(j, b[0]), h)),
            pl.BlockSpec(
                (LONG_DEV, HEAD_SIZE), lambda h, i, j, b: (jnp.minimum(j, b[0]), heads_kv + h)
            ),
        ],
        out_specs=pl.BlockSpec((tq, group * HEAD_SIZE), lambda h, i, j, b: (i, h)),
        scratch_shapes=[
            pltpu.VMEM((group, tq, HEAD_SIZE), jnp.float32),
            pltpu.VMEM((group, tq, HEAD_SIZE), jnp.float32),
            pltpu.VMEM((group, tq, HEAD_SIZE), jnp.float32),
        ],
    )
    b_arr = jnp.reshape(my_index, (1,)).astype(jnp.int32)
    return pl.pallas_call(
        kernel,
        grid_spec=grid_spec,
        out_shape=jax.ShapeDtypeStruct((rows, q_cols), jnp.bfloat16),
        compiler_params=pltpu.CompilerParams(
            dimension_semantics=("arbitrary", "arbitrary", "arbitrary")
        ),
    )(b_arr, q_long, kv_long, kv_long)


def short_attention(my_index, req_count, q_short, k_short, v_short, short_pages, short_fill):
    heads_kv = k_short.shape[1] // HEAD_SIZE
    group = q_short.shape[1] // k_short.shape[1]
    perm = [(s, s + 1) for s in range(req_count - 1)]
    k_prev = lax.ppermute(k_short, "req", perm)
    v_prev = lax.ppermute(v_short, "req", perm)
    own_off = my_index * SHORT_DEV + jnp.arange(SHORT_DEV, dtype=jnp.int32)
    key_off = (my_index - 1) * SHORT_DEV + jnp.arange(2 * SHORT_DEV, dtype=jnp.int32)
    q_seg, q_pos, q_live = short_layout(own_off, short_pages, short_fill)
    k_seg, k_pos, k_live = short_layout(key_off, short_pages, short_fill)
    k_live = k_live & (key_off >= 0)
    allowed = (q_seg[:, None] == k_seg[None, :]) & (k_pos[None, :] <= q_pos[:, None]) & k_live[None, :]
    keys = jnp.concatenate([k_prev, k_short]).reshape(2 * SHORT_DEV, heads_kv, HEAD_SIZE)
    values = jnp.concatenate([v_prev, v_short]).reshape(2 * SHORT_DEV, heads_kv, HEAD_SIZE)
    qs = q_short.reshape(SHORT_DEV, heads_kv, group, HEAD_SIZE)
    scores = jnp.einsum(
        "qhgd,khd->hgqk", qs, keys, preferred_element_type=jnp.float32
    ) * HEAD_SIZE ** (-0.5)
    scores = jnp.where(allowed[None, None], scores, NEGATIVE_FILL)
    row_max = jnp.max(scores, axis=-1, keepdims=True)
    weights = jnp.exp(scores - row_max)
    denom = jnp.sum(weights, axis=-1)
    weighted = jnp.einsum(
        "hgqk,khd->qhgd", weights.astype(jnp.bfloat16), values, preferred_element_type=jnp.float32
    )
    attended = weighted / jnp.transpose(denom, (2, 0, 1))[..., None]
    attended = jnp.where(q_live[:, None, None, None], attended, 0.0)
    return attended.reshape(SHORT_DEV, -1).astype(jnp.bfloat16)


def local(
    queries,
    rotated_key_rows,
    stream_value_rows,
    out_weight,
    short_pages,
    short_fill,
    stream_page_table,
):
    req_count = lax.axis_size("req")
    my_index = lax.axis_index("req")
    tok_rows = queries.shape[0]
    kv_long = jnp.concatenate(
        [rotated_key_rows[:LONG_DEV], stream_value_rows[:LONG_DEV]], axis=1
    )
    kv_long = lax.all_gather(kv_long, "req", axis=0, tiled=True)
    att_long = long_attention(my_index, queries[:LONG_DEV], kv_long)
    att_short = short_attention(
        my_index,
        req_count,
        queries[LONG_DEV:],
        rotated_key_rows[LONG_DEV:],
        stream_value_rows[LONG_DEV:],
        short_pages,
        short_fill,
    )
    attended = jnp.concatenate([att_long, att_short])
    mixed_out = lax.psum_scatter(
        jnp.dot(attended, out_weight, preferred_element_type=jnp.float32).astype(jnp.bfloat16),
        "tp",
        scatter_dimension=0,
        tiled=True,
    )
    pages_per = tok_rows // PAGE_ROWS
    capacity = (pages_per + req_count - 1) // req_count
    slot_count = capacity * req_count
    width = rotated_key_rows.shape[1]
    own_off = my_index * SHORT_DEV + jnp.arange(SHORT_DEV, dtype=jnp.int32)
    short_live = short_layout(own_off, short_pages, short_fill)[2]
    own_live = jnp.concatenate([jnp.ones((LONG_DEV,), bool), short_live])
    kv_rows = jnp.stack([rotated_key_rows, stream_value_rows])
    kv_rows = jnp.where(own_live[None, :, None], kv_rows, jnp.zeros_like(kv_rows))
    kv_pages = kv_rows.reshape(2, pages_per, PAGE_ROWS * width)
    page_map = stream_page_table.reshape(req_count, pages_per)
    owners = page_map // slot_count
    earlier = (
        jnp.arange(pages_per, dtype=jnp.int32)[:, None]
        > jnp.arange(pages_per, dtype=jnp.int32)[None, :]
    )
    matching = owners[:, :, None] == owners[:, None, :]
    order_in = jnp.sum((matching & earlier[None]).astype(jnp.int32), axis=2)
    my_owner = owners[my_index]
    my_order = order_in[my_index]
    send_map = (
        (my_owner * capacity + my_order)[:, None]
        == jnp.arange(slot_count, dtype=jnp.int32)[None, :]
    ).astype(jnp.bfloat16)
    outgoing = jnp.einsum(
        "ks,xkr->xsr", send_map, kv_pages, preferred_element_type=jnp.float32
    ).astype(jnp.bfloat16)
    outgoing = outgoing.reshape(2, req_count, capacity, PAGE_ROWS * width)
    incoming = lax.all_to_all(outgoing, "req", split_axis=1, concat_axis=1, tiled=True)
    mine_mask = owners == my_index
    placing = mine_mask[:, :, None] & (
        order_in[:, :, None] == jnp.arange(capacity, dtype=jnp.int32)[None, None, :]
    )
    target = (page_map % slot_count)[:, :, None] == jnp.arange(slot_count, dtype=jnp.int32)[
        None, None, :
    ]
    routing = jnp.einsum(
        "skc,skt->sct",
        placing.astype(jnp.bfloat16),
        target.astype(jnp.bfloat16),
        preferred_element_type=jnp.float32,
    ).astype(jnp.bfloat16)
    written_cache = jnp.einsum(
        "sct,xscr->xtr", routing, incoming, preferred_element_type=jnp.float32
    ).astype(jnp.bfloat16)
    written_cache = written_cache.reshape(2, slot_count, PAGE_ROWS, width)
    return (mixed_out, written_cache)


def solution(mesh):
    in_specs = (P("req", "tp"), P("req", "tp"), P("req", "tp"), P("tp", None), P(), P(), P())
    out_specs = (P(("req", "tp"), None), P(None, "req", None, "tp"))
    return jax.shard_map(local, mesh=mesh, in_specs=in_specs, out_specs=out_specs, check_vma=False)
```

```python
import functools

import jax
import jax.numpy as jnp
from jax import lax
from jax.experimental import pallas as pl
from jax.experimental.pallas import tpu as pltpu
from jax.sharding import PartitionSpec as P

HEAD_SIZE = 128
LONG_DEV = 512
SHORT_DEV = 128
PAGE_ROWS = 16
BLOCK_TOKENS = 640
LONG_CHUNKS = 4


NEGATIVE_FILL = -1e30


def short_layout(offset, short_pages, short_fill):
    page_id = offset // PAGE_ROWS
    page_ends = jnp.cumsum(short_pages)
    page_starts = page_ends - short_pages
    limits = page_starts * PAGE_ROWS + (short_pages - 1) * PAGE_ROWS + short_fill
    owner_hit = page_ends[None, :] <= page_id[:, None]
    prompt = jnp.sum(owner_hit.astype(jnp.int32), axis=1)
    select = jnp.arange(short_pages.shape[0], dtype=jnp.int32)[None, :] == prompt[:, None]
    begin_at = jnp.sum(jnp.where(select, page_starts[None, :], 0), axis=1) * PAGE_ROWS
    limit_at = jnp.sum(jnp.where(select, limits[None, :], 0), axis=1)
    return (prompt, offset - begin_at, offset < limit_at)


def flash_kernel(b_ref, q_ref, k_ref, v_ref, *refs, group, tq, tk, chunk_rows, chunk, first, last):
    if first:
        m_out, l_out, acc_out = refs[-3:]
        m_in, l_in, acc_in = m_out, l_out, acc_out
    elif last:
        m_in, l_in, acc_in, o_ref = refs
        m_out, l_out, acc_out = m_in, l_in, acc_in
    else:
        m_in, l_in, acc_in, m_out, l_out, acc_out = refs
    i = pl.program_id(1)
    t = pl.program_id(2)
    b = b_ref[0]
    per_tile = tk // chunk_rows
    scale = HEAD_SIZE ** (-0.5)

    @pl.when(t == 0)
    def _init():
        if first:
            m_out[...] = jnp.full(m_out.shape, NEGATIVE_FILL, jnp.float32)
            l_out[...] = jnp.zeros(l_out.shape, jnp.float32)
            acc_out[...] = jnp.zeros(acc_out.shape, jnp.float32)
        elif not last:
            m_out[...] = m_in[...]
            l_out[...] = l_in[...]
            acc_out[...] = acc_in[...]

    def step(masked):
        k = k_ref[...]
        v = v_ref[...]
        if masked:
            rows = i * tq + lax.broadcasted_iota(jnp.int32, (tq, tk), 0)
            cols = lax.broadcasted_iota(jnp.int32, (tq, tk), 1)
            src = t * per_tile + cols // chunk_rows
            key_pos = chunk * chunk_rows + cols % chunk_rows
            allowed = (src < b) | ((src == b) & (key_pos <= rows))
        for g in range(group):
            qg = q_ref[:, g * HEAD_SIZE:(g + 1) * HEAD_SIZE]
            s = lax.dot_general(
                qg, k, (((1,), (1,)), ((), ())), preferred_element_type=jnp.float32
            ) * scale
            if masked:
                s = jnp.where(allowed, s, NEGATIVE_FILL)
            m_prev = m_out[g]
            m_new = jnp.maximum(m_prev, jnp.max(s, axis=1, keepdims=True))
            p = jnp.exp(s - m_new[:, :1])
            alpha = jnp.exp(m_prev - m_new)
            l_out[g] = alpha * l_out[g] + jnp.sum(p, axis=1, keepdims=True)
            acc_out[g] = acc_out[g] * alpha + lax.dot_general(
                p.astype(jnp.bfloat16), v, (((1,), (0,)), ((), ())),
                preferred_element_type=jnp.float32,
            )
            m_out[g] = m_new

    @pl.when(t * per_tile + per_tile - 1 < b)
    def _full():
        step(False)

    @pl.when((t * per_tile + per_tile - 1 >= b) & (t * per_tile <= b))
    def _diag():
        step(True)

    if last:
        @pl.when(t == pl.num_programs(2) - 1)
        def _fin():
            for g in range(group):
                o_ref[:, g * HEAD_SIZE:(g + 1) * HEAD_SIZE] = (
                    acc_out[g] / l_out[g]
                ).astype(o_ref.dtype)


def long_attention_chunk(b_arr, q_long, kv_chunk, state, chunk, first, last):
    rows, q_cols = q_long.shape
    kv_cols = kv_chunk.shape[1] // 2
    heads_kv = kv_cols // HEAD_SIZE
    group = q_cols // kv_cols
    chunk_rows = LONG_DEV // LONG_CHUNKS
    total = kv_chunk.shape[0]
    tk = min(512, total)
    per_tile = tk // chunk_rows
    tq = LONG_DEV
    kernel = functools.partial(
        flash_kernel, group=group, tq=tq, tk=tk, chunk_rows=chunk_rows, chunk=chunk,
        first=first, last=last,
    )
    state_shape = jax.ShapeDtypeStruct((heads_kv, group, rows, HEAD_SIZE), jnp.float32)
    state_spec = pl.BlockSpec((None, group, tq, HEAD_SIZE), lambda h, i, t, b: (h, 0, i, 0))
    kv_spec_k = pl.BlockSpec((tk, HEAD_SIZE), lambda h, i, t, b: (jnp.minimum(t, b[0] // per_tile), h))
    kv_spec_v = pl.BlockSpec(
        (tk, HEAD_SIZE), lambda h, i, t, b: (jnp.minimum(t, b[0] // per_tile), heads_kv + h)
    )
    q_spec = pl.BlockSpec((tq, group * HEAD_SIZE), lambda h, i, t, b: (i, h))
    in_specs = [q_spec, kv_spec_k, kv_spec_v]
    operands = [b_arr, q_long, kv_chunk, kv_chunk]
    aliases = {}
    if not first:
        in_specs += [state_spec] * 3
        operands += list(state)
    if last:
        out_specs = q_spec
        out_shape = jax.ShapeDtypeStruct((rows, q_cols), jnp.bfloat16)
    else:
        out_specs = [state_spec] * 3
        out_shape = [state_shape] * 3
        if not first:
            aliases = {4: 0, 5: 1, 6: 2}
    grid_spec = pltpu.PrefetchScalarGridSpec(
        num_scalar_prefetch=1,
        grid=(heads_kv, rows // tq, total // tk),
        in_specs=in_specs,
        out_specs=out_specs,
    )
    return pl.pallas_call(
        kernel,
        grid_spec=grid_spec,
        out_shape=out_shape,
        input_output_aliases=aliases,
        compiler_params=pltpu.CompilerParams(
            dimension_semantics=("arbitrary", "arbitrary", "arbitrary")
        ),
    )(*operands)


def long_attention(my_index, q_long, k_long, v_long):
    b_arr = jnp.reshape(my_index, (1,)).astype(jnp.int32)
    chunk_rows = LONG_DEV // LONG_CHUNKS
    state = None
    for c in range(LONG_CHUNKS):
        kv = jnp.concatenate(
            [k_long[c * chunk_rows:(c + 1) * chunk_rows], v_long[c * chunk_rows:(c + 1) * chunk_rows]],
            axis=1,
        )
        kv = lax.all_gather(kv, "req", axis=0, tiled=True)
        state = long_attention_chunk(
            b_arr, q_long, kv, state, c, c == 0, c == LONG_CHUNKS - 1
        )
    return state


def short_attention(my_index, req_count, q_short, k_short, v_short, short_pages, short_fill):
    heads_kv = k_short.shape[1] // HEAD_SIZE
    group = q_short.shape[1] // k_short.shape[1]
    perm = [(s, s + 1) for s in range(req_count - 1)]
    k_prev = lax.ppermute(k_short, "req", perm)
    v_prev = lax.ppermute(v_short, "req", perm)
    own_off = my_index * SHORT_DEV + jnp.arange(SHORT_DEV, dtype=jnp.int32)
    key_off = (my_index - 1) * SHORT_DEV + jnp.arange(2 * SHORT_DEV, dtype=jnp.int32)
    q_seg, q_pos, q_live = short_layout(own_off, short_pages, short_fill)
    k_seg, k_pos, k_live = short_layout(key_off, short_pages, short_fill)
    k_live = k_live & (key_off >= 0)
    allowed = (q_seg[:, None] == k_seg[None, :]) & (k_pos[None, :] <= q_pos[:, None]) & k_live[None, :]
    keys = jnp.concatenate([k_prev, k_short]).reshape(2 * SHORT_DEV, heads_kv, HEAD_SIZE)
    values = jnp.concatenate([v_prev, v_short]).reshape(2 * SHORT_DEV, heads_kv, HEAD_SIZE)
    qs = q_short.reshape(SHORT_DEV, heads_kv, group, HEAD_SIZE)
    scores = jnp.einsum(
        "qhgd,khd->hgqk", qs, keys, preferred_element_type=jnp.float32
    ) * HEAD_SIZE ** (-0.5)
    scores = jnp.where(allowed[None, None], scores, NEGATIVE_FILL)
    row_max = jnp.max(scores, axis=-1, keepdims=True)
    weights = jnp.exp(scores - row_max)
    denom = jnp.sum(weights, axis=-1)
    weighted = jnp.einsum(
        "hgqk,khd->qhgd", weights.astype(jnp.bfloat16), values, preferred_element_type=jnp.float32
    )
    attended = weighted / jnp.transpose(denom, (2, 0, 1))[..., None]
    attended = jnp.where(q_live[:, None, None, None], attended, 0.0)
    return attended.reshape(SHORT_DEV, -1).astype(jnp.bfloat16)


def local(
    queries,
    rotated_key_rows,
    stream_value_rows,
    out_weight,
    short_pages,
    short_fill,
    stream_page_table,
):
    req_count = lax.axis_size("req")
    my_index = lax.axis_index("req")
    tok_rows = queries.shape[0]
    pages_per = tok_rows // PAGE_ROWS
    capacity = (pages_per + req_count - 1) // req_count
    slot_count = capacity * req_count
    width = rotated_key_rows.shape[1]
    own_off = my_index * SHORT_DEV + jnp.arange(SHORT_DEV, dtype=jnp.int32)
    short_live = short_layout(own_off, short_pages, short_fill)[2]
    own_live = jnp.concatenate([jnp.ones((LONG_DEV,), bool), short_live])
    kv_rows = jnp.stack([rotated_key_rows, stream_value_rows])
    kv_rows = jnp.where(own_live[None, :, None], kv_rows, jnp.zeros_like(kv_rows))
    kv_pages = kv_rows.reshape(2, pages_per, PAGE_ROWS * width)
    page_map = stream_page_table.reshape(req_count, pages_per)
    owners = page_map // slot_count
    earlier = (
        jnp.arange(pages_per, dtype=jnp.int32)[:, None]
        > jnp.arange(pages_per, dtype=jnp.int32)[None, :]
    )
    matching = owners[:, :, None] == owners[:, None, :]
    order_in = jnp.sum((matching & earlier[None]).astype(jnp.int32), axis=2)
    my_owner = owners[my_index]
    my_order = order_in[my_index]
    send_map = (
        (my_owner * capacity + my_order)[:, None]
        == jnp.arange(slot_count, dtype=jnp.int32)[None, :]
    ).astype(jnp.bfloat16)
    outgoing = jnp.einsum(
        "ks,xkr->xsr", send_map, kv_pages, preferred_element_type=jnp.float32
    ).astype(jnp.bfloat16)
    outgoing = outgoing.reshape(2, req_count, capacity, PAGE_ROWS * width)
    incoming = lax.all_to_all(outgoing, "req", split_axis=1, concat_axis=1, tiled=True)
    mine_mask = owners == my_index
    placing = mine_mask[:, :, None] & (
        order_in[:, :, None] == jnp.arange(capacity, dtype=jnp.int32)[None, None, :]
    )
    target = (page_map % slot_count)[:, :, None] == jnp.arange(slot_count, dtype=jnp.int32)[
        None, None, :
    ]
    routing = jnp.einsum(
        "skc,skt->sct",
        placing.astype(jnp.bfloat16),
        target.astype(jnp.bfloat16),
        preferred_element_type=jnp.float32,
    ).astype(jnp.bfloat16)
    incoming, queries = lax.optimization_barrier((incoming, queries))
    att_long = long_attention(
        my_index, queries[:LONG_DEV], rotated_key_rows[:LONG_DEV], stream_value_rows[:LONG_DEV]
    )
    att_short = short_attention(
        my_index,
        req_count,
        queries[LONG_DEV:],
        rotated_key_rows[LONG_DEV:],
        stream_value_rows[LONG_DEV:],
        short_pages,
        short_fill,
    )
    attended = jnp.concatenate([att_long, att_short])
    mixed_out = lax.psum_scatter(
        jnp.dot(attended, out_weight, preferred_element_type=jnp.float32).astype(jnp.bfloat16),
        "tp",
        scatter_dimension=0,
        tiled=True,
    )
    written_cache = jnp.einsum(
        "sct,xscr->xtr", routing, incoming, preferred_element_type=jnp.float32
    ).astype(jnp.bfloat16)
    written_cache = written_cache.reshape(2, slot_count, PAGE_ROWS, width)
    return (mixed_out, written_cache)


def solution(mesh):
    in_specs = (P("req", "tp"), P("req", "tp"), P("req", "tp"), P("tp", None), P(), P(), P())
    out_specs = (P(("req", "tp"), None), P(None, "req", None, "tp"))
    return jax.shard_map(local, mesh=mesh, in_specs=in_specs, out_specs=out_specs, check_vma=False)
```

```python
import functools

import jax
import jax.numpy as jnp
from jax import lax
from jax.experimental import pallas as pl
from jax.experimental.pallas import tpu as pltpu
from jax.sharding import PartitionSpec as P

HEAD_SIZE = 128
LONG_DEV = 512
SHORT_DEV = 128
PAGE_ROWS = 16
BLOCK_TOKENS = 640
LONG_CHUNKS = 2


NEGATIVE_FILL = -1e30


def short_layout(offset, short_pages, short_fill):
    page_id = offset // PAGE_ROWS
    page_ends = jnp.cumsum(short_pages)
    page_starts = page_ends - short_pages
    limits = page_starts * PAGE_ROWS + (short_pages - 1) * PAGE_ROWS + short_fill
    owner_hit = page_ends[None, :] <= page_id[:, None]
    prompt = jnp.sum(owner_hit.astype(jnp.int32), axis=1)
    select = jnp.arange(short_pages.shape[0], dtype=jnp.int32)[None, :] == prompt[:, None]
    begin_at = jnp.sum(jnp.where(select, page_starts[None, :], 0), axis=1) * PAGE_ROWS
    limit_at = jnp.sum(jnp.where(select, limits[None, :], 0), axis=1)
    return (prompt, offset - begin_at, offset < limit_at)


def flash_kernel(b_ref, q_ref, k_ref, v_ref, *refs, group, tq, tk, chunk_rows, chunk, first, last):
    if first:
        m_out, l_out, acc_out = refs[-3:]
        m_in, l_in, acc_in = m_out, l_out, acc_out
    elif last:
        m_in, l_in, acc_in, o_ref = refs
        m_out, l_out, acc_out = m_in, l_in, acc_in
    else:
        m_in, l_in, acc_in, m_out, l_out, acc_out = refs
    i = pl.program_id(1)
    t = pl.program_id(2)
    b = b_ref[0]
    per_tile = tk // chunk_rows
    scale = HEAD_SIZE ** (-0.5)

    @pl.when(t == 0)
    def _init():
        if first:
            m_out[...] = jnp.full(m_out.shape, NEGATIVE_FILL, jnp.float32)
            l_out[...] = jnp.zeros(l_out.shape, jnp.float32)
            acc_out[...] = jnp.zeros(acc_out.shape, jnp.float32)
        elif not last:
            m_out[...] = m_in[...]
            l_out[...] = l_in[...]
            acc_out[...] = acc_in[...]

    def step(masked):
        k = k_ref[...]
        v = v_ref[...]
        if masked:
            rows = i * tq + lax.broadcasted_iota(jnp.int32, (tq, tk), 0)
            cols = lax.broadcasted_iota(jnp.int32, (tq, tk), 1)
            src = t * per_tile + cols // chunk_rows
            key_pos = chunk * chunk_rows + cols % chunk_rows
            allowed = (src < b) | ((src == b) & (key_pos <= rows))
        for g in range(group):
            qg = q_ref[:, g * HEAD_SIZE:(g + 1) * HEAD_SIZE]
            s = lax.dot_general(
                qg, k, (((1,), (1,)), ((), ())), preferred_element_type=jnp.float32
            ) * scale
            if masked:
                s = jnp.where(allowed, s, NEGATIVE_FILL)
            m_prev = m_out[g]
            m_new = jnp.maximum(m_prev, jnp.max(s, axis=1, keepdims=True))
            p = jnp.exp(s - m_new[:, :1])
            alpha = jnp.exp(m_prev - m_new)
            l_out[g] = alpha * l_out[g] + jnp.sum(p, axis=1, keepdims=True)
            acc_out[g] = acc_out[g] * alpha + lax.dot_general(
                p.astype(jnp.bfloat16), v, (((1,), (0,)), ((), ())),
                preferred_element_type=jnp.float32,
            )
            m_out[g] = m_new

    @pl.when(t * per_tile + per_tile - 1 < b)
    def _full():
        step(False)

    @pl.when((t * per_tile + per_tile - 1 >= b) & (t * per_tile <= b))
    def _diag():
        step(True)

    if last:
        @pl.when(t == pl.num_programs(2) - 1)
        def _fin():
            for g in range(group):
                o_ref[:, g * HEAD_SIZE:(g + 1) * HEAD_SIZE] = (
                    acc_out[g] / l_out[g]
                ).astype(o_ref.dtype)


def long_attention_chunk(b_arr, q_long, kv_chunk, state, chunk, first, last):
    rows, q_cols = q_long.shape
    kv_cols = kv_chunk.shape[1] // 2
    heads_kv = kv_cols // HEAD_SIZE
    group = q_cols // kv_cols
    chunk_rows = LONG_DEV // LONG_CHUNKS
    total = kv_chunk.shape[0]
    tk = min(512, total)
    per_tile = tk // chunk_rows
    tq = LONG_DEV
    kernel = functools.partial(
        flash_kernel, group=group, tq=tq, tk=tk, chunk_rows=chunk_rows, chunk=chunk,
        first=first, last=last,
    )
    state_shape = jax.ShapeDtypeStruct((heads_kv, group, rows, HEAD_SIZE), jnp.float32)
    state_spec = pl.BlockSpec((None, group, tq, HEAD_SIZE), lambda h, i, t, b: (h, 0, i, 0))
    kv_spec_k = pl.BlockSpec((tk, HEAD_SIZE), lambda h, i, t, b: (jnp.minimum(t, b[0] // per_tile), h))
    kv_spec_v = pl.BlockSpec(
        (tk, HEAD_SIZE), lambda h, i, t, b: (jnp.minimum(t, b[0] // per_tile), heads_kv + h)
    )
    q_spec = pl.BlockSpec((tq, group * HEAD_SIZE), lambda h, i, t, b: (i, h))
    in_specs = [q_spec, kv_spec_k, kv_spec_v]
    operands = [b_arr, q_long, kv_chunk, kv_chunk]
    aliases = {}
    if not first:
        in_specs += [state_spec] * 3
        operands += list(state)
    if last:
        out_specs = q_spec
        out_shape = jax.ShapeDtypeStruct((rows, q_cols), jnp.bfloat16)
    else:
        out_specs = [state_spec] * 3
        out_shape = [state_shape] * 3
        if not first:
            aliases = {4: 0, 5: 1, 6: 2}
    grid_spec = pltpu.PrefetchScalarGridSpec(
        num_scalar_prefetch=1,
        grid=(heads_kv, rows // tq, total // tk),
        in_specs=in_specs,
        out_specs=out_specs,
    )
    return pl.pallas_call(
        kernel,
        grid_spec=grid_spec,
        out_shape=out_shape,
        input_output_aliases=aliases,
        compiler_params=pltpu.CompilerParams(
            dimension_semantics=("arbitrary", "arbitrary", "arbitrary")
        ),
    )(*operands)


def long_attention(my_index, q_long, k_long, v_long):
    b_arr = jnp.reshape(my_index, (1,)).astype(jnp.int32)
    chunk_rows = LONG_DEV // LONG_CHUNKS
    state = None
    for c in range(LONG_CHUNKS):
        kv = jnp.concatenate(
            [k_long[c * chunk_rows:(c + 1) * chunk_rows], v_long[c * chunk_rows:(c + 1) * chunk_rows]],
            axis=1,
        )
        kv = lax.all_gather(kv, "req", axis=0, tiled=True)
        state = long_attention_chunk(
            b_arr, q_long, kv, state, c, c == 0, c == LONG_CHUNKS - 1
        )
    return state


def short_attention(my_index, req_count, q_short, k_short, v_short, short_pages, short_fill):
    heads_kv = k_short.shape[1] // HEAD_SIZE
    group = q_short.shape[1] // k_short.shape[1]
    perm = [(s, s + 1) for s in range(req_count - 1)]
    k_prev = lax.ppermute(k_short, "req", perm)
    v_prev = lax.ppermute(v_short, "req", perm)
    own_off = my_index * SHORT_DEV + jnp.arange(SHORT_DEV, dtype=jnp.int32)
    key_off = (my_index - 1) * SHORT_DEV + jnp.arange(2 * SHORT_DEV, dtype=jnp.int32)
    q_seg, q_pos, q_live = short_layout(own_off, short_pages, short_fill)
    k_seg, k_pos, k_live = short_layout(key_off, short_pages, short_fill)
    k_live = k_live & (key_off >= 0)
    allowed = (q_seg[:, None] == k_seg[None, :]) & (k_pos[None, :] <= q_pos[:, None]) & k_live[None, :]
    keys = jnp.concatenate([k_prev, k_short]).reshape(2 * SHORT_DEV, heads_kv, HEAD_SIZE)
    values = jnp.concatenate([v_prev, v_short]).reshape(2 * SHORT_DEV, heads_kv, HEAD_SIZE)
    qs = q_short.reshape(SHORT_DEV, heads_kv, group, HEAD_SIZE)
    scores = jnp.einsum(
        "qhgd,khd->hgqk", qs, keys, preferred_element_type=jnp.float32
    ) * HEAD_SIZE ** (-0.5)
    scores = jnp.where(allowed[None, None], scores, NEGATIVE_FILL)
    row_max = jnp.max(scores, axis=-1, keepdims=True)
    weights = jnp.exp(scores - row_max)
    denom = jnp.sum(weights, axis=-1)
    weighted = jnp.einsum(
        "hgqk,khd->qhgd", weights.astype(jnp.bfloat16), values, preferred_element_type=jnp.float32
    )
    attended = weighted / jnp.transpose(denom, (2, 0, 1))[..., None]
    attended = jnp.where(q_live[:, None, None, None], attended, 0.0)
    return attended.reshape(SHORT_DEV, -1).astype(jnp.bfloat16)


def local(
    queries,
    rotated_key_rows,
    stream_value_rows,
    out_weight,
    short_pages,
    short_fill,
    stream_page_table,
):
    req_count = lax.axis_size("req")
    my_index = lax.axis_index("req")
    tok_rows = queries.shape[0]
    pages_per = tok_rows // PAGE_ROWS
    capacity = (pages_per + req_count - 1) // req_count
    slot_count = capacity * req_count
    width = rotated_key_rows.shape[1]
    own_off = my_index * SHORT_DEV + jnp.arange(SHORT_DEV, dtype=jnp.int32)
    short_live = short_layout(own_off, short_pages, short_fill)[2]
    own_live = jnp.concatenate([jnp.ones((LONG_DEV,), bool), short_live])
    kv_rows = jnp.stack([rotated_key_rows, stream_value_rows])
    kv_rows = jnp.where(own_live[None, :, None], kv_rows, jnp.zeros_like(kv_rows))
    kv_pages = kv_rows.reshape(2, pages_per, PAGE_ROWS * width)
    page_map = stream_page_table.reshape(req_count, pages_per)
    owners = page_map // slot_count
    earlier = (
        jnp.arange(pages_per, dtype=jnp.int32)[:, None]
        > jnp.arange(pages_per, dtype=jnp.int32)[None, :]
    )
    matching = owners[:, :, None] == owners[:, None, :]
    order_in = jnp.sum((matching & earlier[None]).astype(jnp.int32), axis=2)
    my_owner = owners[my_index]
    my_order = order_in[my_index]
    send_map = (
        (my_owner * capacity + my_order)[:, None]
        == jnp.arange(slot_count, dtype=jnp.int32)[None, :]
    ).astype(jnp.bfloat16)
    outgoing = jnp.einsum(
        "ks,xkr->xsr", send_map, kv_pages, preferred_element_type=jnp.float32
    ).astype(jnp.bfloat16)
    outgoing = outgoing.reshape(2, req_count, capacity, PAGE_ROWS * width)
    incoming = lax.all_to_all(outgoing, "req", split_axis=1, concat_axis=1, tiled=True)
    mine_mask = owners == my_index
    placing = mine_mask[:, :, None] & (
        order_in[:, :, None] == jnp.arange(capacity, dtype=jnp.int32)[None, None, :]
    )
    target = (page_map % slot_count)[:, :, None] == jnp.arange(slot_count, dtype=jnp.int32)[
        None, None, :
    ]
    routing = jnp.einsum(
        "skc,skt->sct",
        placing.astype(jnp.bfloat16),
        target.astype(jnp.bfloat16),
        preferred_element_type=jnp.float32,
    ).astype(jnp.bfloat16)
    incoming, queries = lax.optimization_barrier((incoming, queries))
    att_long = long_attention(
        my_index, queries[:LONG_DEV], rotated_key_rows[:LONG_DEV], stream_value_rows[:LONG_DEV]
    )
    att_short = short_attention(
        my_index,
        req_count,
        queries[LONG_DEV:],
        rotated_key_rows[LONG_DEV:],
        stream_value_rows[LONG_DEV:],
        short_pages,
        short_fill,
    )
    attended = jnp.concatenate([att_long, att_short])
    mixed_out = lax.psum_scatter(
        jnp.dot(attended, out_weight, preferred_element_type=jnp.float32).astype(jnp.bfloat16),
        "tp",
        scatter_dimension=0,
        tiled=True,
    )
    written_cache = jnp.einsum(
        "sct,xscr->xtr", routing, incoming, preferred_element_type=jnp.float32
    ).astype(jnp.bfloat16)
    written_cache = written_cache.reshape(2, slot_count, PAGE_ROWS, width)
    return (mixed_out, written_cache)


def solution(mesh):
    in_specs = (P("req", "tp"), P("req", "tp"), P("req", "tp"), P("tp", None), P(), P(), P())
    out_specs = (P(("req", "tp"), None), P(None, "req", None, "tp"))
    return jax.shard_map(local, mesh=mesh, in_specs=in_specs, out_specs=out_specs, check_vma=False)
```

```python
import functools

import jax
import jax.numpy as jnp
from jax import lax
from jax.experimental import pallas as pl
from jax.experimental.pallas import tpu as pltpu
from jax.sharding import PartitionSpec as P

HEAD_SIZE = 128
LONG_DEV = 512
SHORT_DEV = 128
PAGE_ROWS = 16
BLOCK_TOKENS = 640
LONG_CHUNK_ROWS = (256, 128, 128)


NEGATIVE_FILL = -1e30


def short_layout(offset, short_pages, short_fill):
    page_id = offset // PAGE_ROWS
    page_ends = jnp.cumsum(short_pages)
    page_starts = page_ends - short_pages
    limits = page_starts * PAGE_ROWS + (short_pages - 1) * PAGE_ROWS + short_fill
    owner_hit = page_ends[None, :] <= page_id[:, None]
    prompt = jnp.sum(owner_hit.astype(jnp.int32), axis=1)
    select = jnp.arange(short_pages.shape[0], dtype=jnp.int32)[None, :] == prompt[:, None]
    begin_at = jnp.sum(jnp.where(select, page_starts[None, :], 0), axis=1) * PAGE_ROWS
    limit_at = jnp.sum(jnp.where(select, limits[None, :], 0), axis=1)
    return (prompt, offset - begin_at, offset < limit_at)


def flash_kernel(b_ref, q_ref, k_ref, v_ref, *refs, group, tq, tk, chunk_rows, chunk_start, first, last):
    if first:
        m_out, l_out, acc_out = refs[-3:]
        m_in, l_in, acc_in = m_out, l_out, acc_out
    elif last:
        m_in, l_in, acc_in, o_ref = refs
        m_out, l_out, acc_out = m_in, l_in, acc_in
    else:
        m_in, l_in, acc_in, m_out, l_out, acc_out = refs
    i = pl.program_id(1)
    t = pl.program_id(2)
    b = b_ref[0]
    per_tile = tk // chunk_rows
    scale = HEAD_SIZE ** (-0.5)

    @pl.when(t == 0)
    def _init():
        if first:
            m_out[...] = jnp.full(m_out.shape, NEGATIVE_FILL, jnp.float32)
            l_out[...] = jnp.zeros(l_out.shape, jnp.float32)
            acc_out[...] = jnp.zeros(acc_out.shape, jnp.float32)
        elif not last:
            m_out[...] = m_in[...]
            l_out[...] = l_in[...]
            acc_out[...] = acc_in[...]

    def step(masked):
        k = k_ref[...]
        v = v_ref[...]
        if masked:
            rows = i * tq + lax.broadcasted_iota(jnp.int32, (tq, tk), 0)
            cols = lax.broadcasted_iota(jnp.int32, (tq, tk), 1)
            src = t * per_tile + cols // chunk_rows
            key_pos = chunk_start + cols % chunk_rows
            allowed = (src < b) | ((src == b) & (key_pos <= rows))
        for g in range(group):
            qg = q_ref[:, g * HEAD_SIZE:(g + 1) * HEAD_SIZE]
            s = lax.dot_general(
                qg, k, (((1,), (1,)), ((), ())), preferred_element_type=jnp.float32
            ) * scale
            if masked:
                s = jnp.where(allowed, s, NEGATIVE_FILL)
            m_prev = m_out[g]
            m_new = jnp.maximum(m_prev, jnp.max(s, axis=1, keepdims=True))
            p = jnp.exp(s - m_new[:, :1])
            alpha = jnp.exp(m_prev - m_new)
            l_out[g] = alpha * l_out[g] + jnp.sum(p, axis=1, keepdims=True)
            acc_out[g] = acc_out[g] * alpha + lax.dot_general(
                p.astype(jnp.bfloat16), v, (((1,), (0,)), ((), ())),
                preferred_element_type=jnp.float32,
            )
            m_out[g] = m_new

    @pl.when(t * per_tile + per_tile - 1 < b)
    def _full():
        step(False)

    @pl.when((t * per_tile + per_tile - 1 >= b) & (t * per_tile <= b))
    def _diag():
        step(True)

    if last:
        @pl.when(t == pl.num_programs(2) - 1)
        def _fin():
            for g in range(group):
                o_ref[:, g * HEAD_SIZE:(g + 1) * HEAD_SIZE] = (
                    acc_out[g] / l_out[g]
                ).astype(o_ref.dtype)


def long_attention_chunk(b_arr, q_long, kv_chunk, state, chunk_rows, chunk_start, first, last):
    rows, q_cols = q_long.shape
    kv_cols = kv_chunk.shape[1] // 2
    heads_kv = kv_cols // HEAD_SIZE
    group = q_cols // kv_cols
    total = kv_chunk.shape[0]
    tk = min(512, total)
    per_tile = tk // chunk_rows
    tq = LONG_DEV
    kernel = functools.partial(
        flash_kernel, group=group, tq=tq, tk=tk, chunk_rows=chunk_rows, chunk_start=chunk_start,
        first=first, last=last,
    )
    state_shape = jax.ShapeDtypeStruct((heads_kv, group, rows, HEAD_SIZE), jnp.float32)
    state_spec = pl.BlockSpec((None, group, tq, HEAD_SIZE), lambda h, i, t, b: (h, 0, i, 0))
    kv_spec_k = pl.BlockSpec((tk, HEAD_SIZE), lambda h, i, t, b: (jnp.minimum(t, b[0] // per_tile), h))
    kv_spec_v = pl.BlockSpec(
        (tk, HEAD_SIZE), lambda h, i, t, b: (jnp.minimum(t, b[0] // per_tile), heads_kv + h)
    )
    q_spec = pl.BlockSpec((tq, group * HEAD_SIZE), lambda h, i, t, b: (i, h))
    in_specs = [q_spec, kv_spec_k, kv_spec_v]
    operands = [b_arr, q_long, kv_chunk, kv_chunk]
    aliases = {}
    if not first:
        in_specs += [state_spec] * 3
        operands += list(state)
    if last:
        out_specs = q_spec
        out_shape = jax.ShapeDtypeStruct((rows, q_cols), jnp.bfloat16)
    else:
        out_specs = [state_spec] * 3
        out_shape = [state_shape] * 3
        if not first:
            aliases = {4: 0, 5: 1, 6: 2}
    grid_spec = pltpu.PrefetchScalarGridSpec(
        num_scalar_prefetch=1,
        grid=(heads_kv, rows // tq, total // tk),
        in_specs=in_specs,
        out_specs=out_specs,
    )
    return pl.pallas_call(
        kernel,
        grid_spec=grid_spec,
        out_shape=out_shape,
        input_output_aliases=aliases,
        compiler_params=pltpu.CompilerParams(
            dimension_semantics=("arbitrary", "arbitrary", "arbitrary")
        ),
    )(*operands)


def long_attention(my_index, q_long, k_long, v_long):
    b_arr = jnp.reshape(my_index, (1,)).astype(jnp.int32)
    state = None
    start = 0
    for c, rows in enumerate(LONG_CHUNK_ROWS):
        kv = jnp.concatenate(
            [k_long[start:start + rows], v_long[start:start + rows]], axis=1
        )
        kv = lax.all_gather(kv, "req", axis=0, tiled=True)
        state = long_attention_chunk(
            b_arr, q_long, kv, state, rows, start, c == 0, c == len(LONG_CHUNK_ROWS) - 1
        )
        start += rows
    return state


def short_attention(my_index, req_count, q_short, k_short, v_short, short_pages, short_fill):
    heads_kv = k_short.shape[1] // HEAD_SIZE
    group = q_short.shape[1] // k_short.shape[1]
    perm = [(s, s + 1) for s in range(req_count - 1)]
    k_prev = lax.ppermute(k_short, "req", perm)
    v_prev = lax.ppermute(v_short, "req", perm)
    own_off = my_index * SHORT_DEV + jnp.arange(SHORT_DEV, dtype=jnp.int32)
    key_off = (my_index - 1) * SHORT_DEV + jnp.arange(2 * SHORT_DEV, dtype=jnp.int32)
    q_seg, q_pos, q_live = short_layout(own_off, short_pages, short_fill)
    k_seg, k_pos, k_live = short_layout(key_off, short_pages, short_fill)
    k_live = k_live & (key_off >= 0)
    allowed = (q_seg[:, None] == k_seg[None, :]) & (k_pos[None, :] <= q_pos[:, None]) & k_live[None, :]
    keys = jnp.concatenate([k_prev, k_short]).reshape(2 * SHORT_DEV, heads_kv, HEAD_SIZE)
    values = jnp.concatenate([v_prev, v_short]).reshape(2 * SHORT_DEV, heads_kv, HEAD_SIZE)
    qs = q_short.reshape(SHORT_DEV, heads_kv, group, HEAD_SIZE)
    scores = jnp.einsum(
        "qhgd,khd->hgqk", qs, keys, preferred_element_type=jnp.float32
    ) * HEAD_SIZE ** (-0.5)
    scores = jnp.where(allowed[None, None], scores, NEGATIVE_FILL)
    row_max = jnp.max(scores, axis=-1, keepdims=True)
    weights = jnp.exp(scores - row_max)
    denom = jnp.sum(weights, axis=-1)
    weighted = jnp.einsum(
        "hgqk,khd->qhgd", weights.astype(jnp.bfloat16), values, preferred_element_type=jnp.float32
    )
    attended = weighted / jnp.transpose(denom, (2, 0, 1))[..., None]
    attended = jnp.where(q_live[:, None, None, None], attended, 0.0)
    return attended.reshape(SHORT_DEV, -1).astype(jnp.bfloat16)


def local(
    queries,
    rotated_key_rows,
    stream_value_rows,
    out_weight,
    short_pages,
    short_fill,
    stream_page_table,
):
    req_count = lax.axis_size("req")
    my_index = lax.axis_index("req")
    tok_rows = queries.shape[0]
    pages_per = tok_rows // PAGE_ROWS
    capacity = (pages_per + req_count - 1) // req_count
    slot_count = capacity * req_count
    width = rotated_key_rows.shape[1]
    own_off = my_index * SHORT_DEV + jnp.arange(SHORT_DEV, dtype=jnp.int32)
    short_live = short_layout(own_off, short_pages, short_fill)[2]
    own_live = jnp.concatenate([jnp.ones((LONG_DEV,), bool), short_live])
    kv_rows = jnp.stack([rotated_key_rows, stream_value_rows])
    kv_rows = jnp.where(own_live[None, :, None], kv_rows, jnp.zeros_like(kv_rows))
    kv_pages = kv_rows.reshape(2, pages_per, PAGE_ROWS * width)
    page_map = stream_page_table.reshape(req_count, pages_per)
    owners = page_map // slot_count
    earlier = (
        jnp.arange(pages_per, dtype=jnp.int32)[:, None]
        > jnp.arange(pages_per, dtype=jnp.int32)[None, :]
    )
    matching = owners[:, :, None] == owners[:, None, :]
    order_in = jnp.sum((matching & earlier[None]).astype(jnp.int32), axis=2)
    my_owner = owners[my_index]
    my_order = order_in[my_index]
    send_map = (
        (my_owner * capacity + my_order)[:, None]
        == jnp.arange(slot_count, dtype=jnp.int32)[None, :]
    ).astype(jnp.bfloat16)
    outgoing = jnp.einsum(
        "ks,xkr->xsr", send_map, kv_pages, preferred_element_type=jnp.float32
    ).astype(jnp.bfloat16)
    outgoing = outgoing.reshape(2, req_count, capacity, PAGE_ROWS * width)
    incoming = lax.all_to_all(outgoing, "req", split_axis=1, concat_axis=1, tiled=True)
    mine_mask = owners == my_index
    placing = mine_mask[:, :, None] & (
        order_in[:, :, None] == jnp.arange(capacity, dtype=jnp.int32)[None, None, :]
    )
    target = (page_map % slot_count)[:, :, None] == jnp.arange(slot_count, dtype=jnp.int32)[
        None, None, :
    ]
    routing = jnp.einsum(
        "skc,skt->sct",
        placing.astype(jnp.bfloat16),
        target.astype(jnp.bfloat16),
        preferred_element_type=jnp.float32,
    ).astype(jnp.bfloat16)
    incoming, queries = lax.optimization_barrier((incoming, queries))
    att_long = long_attention(
        my_index, queries[:LONG_DEV], rotated_key_rows[:LONG_DEV], stream_value_rows[:LONG_DEV]
    )
    att_short = short_attention(
        my_index,
        req_count,
        queries[LONG_DEV:],
        rotated_key_rows[LONG_DEV:],
        stream_value_rows[LONG_DEV:],
        short_pages,
        short_fill,
    )
    attended = jnp.concatenate([att_long, att_short])
    half = out_weight.shape[1] // 2
    mixed_parts = [
        lax.psum_scatter(
            jnp.dot(
                attended, out_weight[:, p * half:(p + 1) * half], preferred_element_type=jnp.float32
            ).astype(jnp.bfloat16),
            "tp",
            scatter_dimension=0,
            tiled=True,
        )
        for p in range(2)
    ]
    mixed_out = jnp.concatenate(mixed_parts, axis=1)
    written_cache = jnp.einsum(
        "sct,xscr->xtr", routing, incoming, preferred_element_type=jnp.float32
    ).astype(jnp.bfloat16)
    written_cache = written_cache.reshape(2, slot_count, PAGE_ROWS, width)
    return (mixed_out, written_cache)


def solution(mesh):
    in_specs = (P("req", "tp"), P("req", "tp"), P("req", "tp"), P("tp", None), P(), P(), P())
    out_specs = (P(("req", "tp"), None), P(None, "req", None, "tp"))
    return jax.shard_map(local, mesh=mesh, in_specs=in_specs, out_specs=out_specs, check_vma=False)
```

```python
import functools

import jax
import jax.numpy as jnp
from jax import lax
from jax.experimental import pallas as pl
from jax.experimental.pallas import tpu as pltpu
from jax.sharding import PartitionSpec as P

HEAD_SIZE = 128
LONG_DEV = 512
SHORT_DEV = 128
PAGE_ROWS = 16
BLOCK_TOKENS = 640
LONG_CHUNK_ROWS = (128, 256, 128)


NEGATIVE_FILL = -1e30


def short_layout(offset, short_pages, short_fill):
    page_id = offset // PAGE_ROWS
    page_ends = jnp.cumsum(short_pages)
    page_starts = page_ends - short_pages
    limits = page_starts * PAGE_ROWS + (short_pages - 1) * PAGE_ROWS + short_fill
    owner_hit = page_ends[None, :] <= page_id[:, None]
    prompt = jnp.sum(owner_hit.astype(jnp.int32), axis=1)
    select = jnp.arange(short_pages.shape[0], dtype=jnp.int32)[None, :] == prompt[:, None]
    begin_at = jnp.sum(jnp.where(select, page_starts[None, :], 0), axis=1) * PAGE_ROWS
    limit_at = jnp.sum(jnp.where(select, limits[None, :], 0), axis=1)
    return (prompt, offset - begin_at, offset < limit_at)


def flash_kernel(b_ref, q_ref, k_ref, v_ref, *refs, group, tq, tk, chunk_rows, chunk_start, first, last):
    if first:
        m_out, l_out, acc_out = refs[-3:]
        m_in, l_in, acc_in = m_out, l_out, acc_out
    elif last:
        m_in, l_in, acc_in, o_ref = refs
        m_out, l_out, acc_out = m_in, l_in, acc_in
    else:
        m_in, l_in, acc_in, m_out, l_out, acc_out = refs
    i = pl.program_id(1)
    t = pl.program_id(2)
    b = b_ref[0]
    per_tile = tk // chunk_rows
    scale = HEAD_SIZE ** (-0.5)

    @pl.when(t == 0)
    def _init():
        if first:
            m_out[...] = jnp.full(m_out.shape, NEGATIVE_FILL, jnp.float32)
            l_out[...] = jnp.zeros(l_out.shape, jnp.float32)
            acc_out[...] = jnp.zeros(acc_out.shape, jnp.float32)
        elif not last:
            m_out[...] = m_in[...]
            l_out[...] = l_in[...]
            acc_out[...] = acc_in[...]

    def step(masked):
        k = k_ref[...]
        v = v_ref[...]
        if masked:
            rows = i * tq + lax.broadcasted_iota(jnp.int32, (tq, tk), 0)
            cols = lax.broadcasted_iota(jnp.int32, (tq, tk), 1)
            src = t * per_tile + cols // chunk_rows
            key_pos = chunk_start + cols % chunk_rows
            allowed = (src < b) | ((src == b) & (key_pos <= rows))
        for g in range(group):
            qg = q_ref[:, g * HEAD_SIZE:(g + 1) * HEAD_SIZE]
            s = lax.dot_general(
                qg, k, (((1,), (1,)), ((), ())), preferred_element_type=jnp.float32
            ) * scale
            if masked:
                s = jnp.where(allowed, s, NEGATIVE_FILL)
            m_prev = m_out[g]
            m_new = jnp.maximum(m_prev, jnp.max(s, axis=1, keepdims=True))
            p = jnp.exp(s - m_new[:, :1])
            alpha = jnp.exp(m_prev - m_new)
            l_out[g] = alpha * l_out[g] + jnp.sum(p, axis=1, keepdims=True)
            acc_out[g] = acc_out[g] * alpha + lax.dot_general(
                p.astype(jnp.bfloat16), v, (((1,), (0,)), ((), ())),
                preferred_element_type=jnp.float32,
            )
            m_out[g] = m_new

    @pl.when(t * per_tile + per_tile - 1 < b)
    def _full():
        step(False)

    @pl.when((t * per_tile + per_tile - 1 >= b) & (t * per_tile <= b))
    def _diag():
        step(True)

    if last:
        @pl.when(t == pl.num_programs(2) - 1)
        def _fin():
            for g in range(group):
                o_ref[:, g * HEAD_SIZE:(g + 1) * HEAD_SIZE] = (
                    acc_out[g] / l_out[g]
                ).astype(o_ref.dtype)


def long_attention_chunk(b_arr, q_long, kv_chunk, state, chunk_rows, chunk_start, first, last):
    rows, q_cols = q_long.shape
    kv_cols = kv_chunk.shape[1] // 2
    heads_kv = kv_cols // HEAD_SIZE
    group = q_cols // kv_cols
    total = kv_chunk.shape[0]
    tk = min(512, total)
    per_tile = tk // chunk_rows
    tq = LONG_DEV
    kernel = functools.partial(
        flash_kernel, group=group, tq=tq, tk=tk, chunk_rows=chunk_rows, chunk_start=chunk_start,
        first=first, last=last,
    )
    state_shape = jax.ShapeDtypeStruct((heads_kv, group, rows, HEAD_SIZE), jnp.float32)
    state_spec = pl.BlockSpec((None, group, tq, HEAD_SIZE), lambda h, i, t, b: (h, 0, i, 0))
    kv_spec_k = pl.BlockSpec((tk, HEAD_SIZE), lambda h, i, t, b: (jnp.minimum(t, b[0] // per_tile), h))
    kv_spec_v = pl.BlockSpec(
        (tk, HEAD_SIZE), lambda h, i, t, b: (jnp.minimum(t, b[0] // per_tile), heads_kv + h)
    )
    q_spec = pl.BlockSpec((tq, group * HEAD_SIZE), lambda h, i, t, b: (i, h))
    in_specs = [q_spec, kv_spec_k, kv_spec_v]
    operands = [b_arr, q_long, kv_chunk, kv_chunk]
    aliases = {}
    if not first:
        in_specs += [state_spec] * 3
        operands += list(state)
    if last:
        out_specs = q_spec
        out_shape = jax.ShapeDtypeStruct((rows, q_cols), jnp.bfloat16)
    else:
        out_specs = [state_spec] * 3
        out_shape = [state_shape] * 3
        if not first:
            aliases = {4: 0, 5: 1, 6: 2}
    grid_spec = pltpu.PrefetchScalarGridSpec(
        num_scalar_prefetch=1,
        grid=(heads_kv, rows // tq, total // tk),
        in_specs=in_specs,
        out_specs=out_specs,
    )
    return pl.pallas_call(
        kernel,
        grid_spec=grid_spec,
        out_shape=out_shape,
        input_output_aliases=aliases,
        compiler_params=pltpu.CompilerParams(
            dimension_semantics=("arbitrary", "arbitrary", "arbitrary")
        ),
    )(*operands)


def long_attention(my_index, q_long, k_long, v_long):
    b_arr = jnp.reshape(my_index, (1,)).astype(jnp.int32)
    state = None
    start = 0
    for c, rows in enumerate(LONG_CHUNK_ROWS):
        kv = jnp.concatenate(
            [k_long[start:start + rows], v_long[start:start + rows]], axis=1
        )
        kv = lax.all_gather(kv, "req", axis=0, tiled=True)
        state = long_attention_chunk(
            b_arr, q_long, kv, state, rows, start, c == 0, c == len(LONG_CHUNK_ROWS) - 1
        )
        start += rows
    return state


def short_attention(my_index, req_count, q_short, k_short, v_short, short_pages, short_fill):
    heads_kv = k_short.shape[1] // HEAD_SIZE
    group = q_short.shape[1] // k_short.shape[1]
    perm = [(s, s + 1) for s in range(req_count - 1)]
    k_prev = lax.ppermute(k_short, "req", perm)
    v_prev = lax.ppermute(v_short, "req", perm)
    own_off = my_index * SHORT_DEV + jnp.arange(SHORT_DEV, dtype=jnp.int32)
    key_off = (my_index - 1) * SHORT_DEV + jnp.arange(2 * SHORT_DEV, dtype=jnp.int32)
    q_seg, q_pos, q_live = short_layout(own_off, short_pages, short_fill)
    k_seg, k_pos, k_live = short_layout(key_off, short_pages, short_fill)
    k_live = k_live & (key_off >= 0)
    allowed = (q_seg[:, None] == k_seg[None, :]) & (k_pos[None, :] <= q_pos[:, None]) & k_live[None, :]
    keys = jnp.concatenate([k_prev, k_short]).reshape(2 * SHORT_DEV, heads_kv, HEAD_SIZE)
    values = jnp.concatenate([v_prev, v_short]).reshape(2 * SHORT_DEV, heads_kv, HEAD_SIZE)
    qs = q_short.reshape(SHORT_DEV, heads_kv, group, HEAD_SIZE)
    scores = jnp.einsum(
        "qhgd,khd->hgqk", qs, keys, preferred_element_type=jnp.float32
    ) * HEAD_SIZE ** (-0.5)
    scores = jnp.where(allowed[None, None], scores, NEGATIVE_FILL)
    row_max = jnp.max(scores, axis=-1, keepdims=True)
    weights = jnp.exp(scores - row_max)
    denom = jnp.sum(weights, axis=-1)
    weighted = jnp.einsum(
        "hgqk,khd->qhgd", weights.astype(jnp.bfloat16), values, preferred_element_type=jnp.float32
    )
    attended = weighted / jnp.transpose(denom, (2, 0, 1))[..., None]
    attended = jnp.where(q_live[:, None, None, None], attended, 0.0)
    return attended.reshape(SHORT_DEV, -1).astype(jnp.bfloat16)


def local(
    queries,
    rotated_key_rows,
    stream_value_rows,
    out_weight,
    short_pages,
    short_fill,
    stream_page_table,
):
    req_count = lax.axis_size("req")
    my_index = lax.axis_index("req")
    tok_rows = queries.shape[0]
    pages_per = tok_rows // PAGE_ROWS
    capacity = (pages_per + req_count - 1) // req_count
    slot_count = capacity * req_count
    width = rotated_key_rows.shape[1]
    own_off = my_index * SHORT_DEV + jnp.arange(SHORT_DEV, dtype=jnp.int32)
    short_live = short_layout(own_off, short_pages, short_fill)[2]
    own_live = jnp.concatenate([jnp.ones((LONG_DEV,), bool), short_live])
    kv_rows = jnp.stack([rotated_key_rows, stream_value_rows])
    kv_rows = jnp.where(own_live[None, :, None], kv_rows, jnp.zeros_like(kv_rows))
    kv_pages = kv_rows.reshape(2, pages_per, PAGE_ROWS * width)
    page_map = stream_page_table.reshape(req_count, pages_per)
    owners = page_map // slot_count
    earlier = (
        jnp.arange(pages_per, dtype=jnp.int32)[:, None]
        > jnp.arange(pages_per, dtype=jnp.int32)[None, :]
    )
    matching = owners[:, :, None] == owners[:, None, :]
    order_in = jnp.sum((matching & earlier[None]).astype(jnp.int32), axis=2)
    my_owner = owners[my_index]
    my_order = order_in[my_index]
    send_map = (
        (my_owner * capacity + my_order)[:, None]
        == jnp.arange(slot_count, dtype=jnp.int32)[None, :]
    ).astype(jnp.bfloat16)
    outgoing = jnp.einsum(
        "ks,xkr->xsr", send_map, kv_pages, preferred_element_type=jnp.float32
    ).astype(jnp.bfloat16)
    outgoing = outgoing.reshape(2, req_count, capacity, PAGE_ROWS * width)
    incoming = lax.all_to_all(outgoing, "req", split_axis=1, concat_axis=1, tiled=True)
    mine_mask = owners == my_index
    placing = mine_mask[:, :, None] & (
        order_in[:, :, None] == jnp.arange(capacity, dtype=jnp.int32)[None, None, :]
    )
    target = (page_map % slot_count)[:, :, None] == jnp.arange(slot_count, dtype=jnp.int32)[
        None, None, :
    ]
    routing = jnp.einsum(
        "skc,skt->sct",
        placing.astype(jnp.bfloat16),
        target.astype(jnp.bfloat16),
        preferred_element_type=jnp.float32,
    ).astype(jnp.bfloat16)
    incoming, queries = lax.optimization_barrier((incoming, queries))
    att_long = long_attention(
        my_index, queries[:LONG_DEV], rotated_key_rows[:LONG_DEV], stream_value_rows[:LONG_DEV]
    )
    att_short = short_attention(
        my_index,
        req_count,
        queries[LONG_DEV:],
        rotated_key_rows[LONG_DEV:],
        stream_value_rows[LONG_DEV:],
        short_pages,
        short_fill,
    )
    attended = jnp.concatenate([att_long, att_short])
    mixed_out = lax.psum_scatter(
        jnp.dot(attended, out_weight, preferred_element_type=jnp.float32).astype(jnp.bfloat16),
        "tp",
        scatter_dimension=0,
        tiled=True,
    )
    written_cache = jnp.einsum(
        "sct,xscr->xtr", routing, incoming, preferred_element_type=jnp.float32
    ).astype(jnp.bfloat16)
    written_cache = written_cache.reshape(2, slot_count, PAGE_ROWS, width)
    return (mixed_out, written_cache)


def solution(mesh):
    in_specs = (P("req", "tp"), P("req", "tp"), P("req", "tp"), P("tp", None), P(), P(), P())
    out_specs = (P(("req", "tp"), None), P(None, "req", None, "tp"))
    return jax.shard_map(local, mesh=mesh, in_specs=in_specs, out_specs=out_specs, check_vma=False)
```

```python
import functools

import jax
import jax.numpy as jnp
from jax import lax
from jax.experimental import pallas as pl
from jax.experimental.pallas import tpu as pltpu
from jax.sharding import PartitionSpec as P

HEAD_SIZE = 128
LONG_DEV = 512
SHORT_DEV = 128
PAGE_ROWS = 16
BLOCK_TOKENS = 640
LONG_CHUNKS = 2


NEGATIVE_FILL = -1e30


def short_layout(offset, short_pages, short_fill):
    page_id = offset // PAGE_ROWS
    page_ends = jnp.cumsum(short_pages)
    page_starts = page_ends - short_pages
    limits = page_starts * PAGE_ROWS + (short_pages - 1) * PAGE_ROWS + short_fill
    owner_hit = page_ends[None, :] <= page_id[:, None]
    prompt = jnp.sum(owner_hit.astype(jnp.int32), axis=1)
    select = jnp.arange(short_pages.shape[0], dtype=jnp.int32)[None, :] == prompt[:, None]
    begin_at = jnp.sum(jnp.where(select, page_starts[None, :], 0), axis=1) * PAGE_ROWS
    limit_at = jnp.sum(jnp.where(select, limits[None, :], 0), axis=1)
    return (prompt, offset - begin_at, offset < limit_at)


def flash_kernel(b_ref, q_ref, k_ref, v_ref, *refs, group, tq, tk, chunk_rows, chunk, first, last):
    if first:
        m_out, l_out, acc_out = refs[-3:]
        m_in, l_in, acc_in = m_out, l_out, acc_out
    elif last:
        m_in, l_in, acc_in, o_ref = refs
        m_out, l_out, acc_out = m_in, l_in, acc_in
    else:
        m_in, l_in, acc_in, m_out, l_out, acc_out = refs
    i = pl.program_id(1)
    t = pl.program_id(2)
    lo = b_ref[0]
    hi = b_ref[1]
    diag = b_ref[2]
    per_tile = tk // chunk_rows
    tile_lo = t * per_tile
    tile_hi = tile_lo + per_tile - 1
    scale = HEAD_SIZE ** (-0.5)

    @pl.when(t == 0)
    def _init():
        if first:
            m_out[...] = jnp.full(m_out.shape, NEGATIVE_FILL, jnp.float32)
            l_out[...] = jnp.zeros(l_out.shape, jnp.float32)
            acc_out[...] = jnp.zeros(acc_out.shape, jnp.float32)
        elif not last:
            m_out[...] = m_in[...]
            l_out[...] = l_in[...]
            acc_out[...] = acc_in[...]

    def step(masked):
        k = k_ref[...]
        v = v_ref[...]
        if masked:
            rows = i * tq + lax.broadcasted_iota(jnp.int32, (tq, tk), 0)
            cols = lax.broadcasted_iota(jnp.int32, (tq, tk), 1)
            src = t * per_tile + cols // chunk_rows
            key_pos = chunk * chunk_rows + cols % chunk_rows
            allowed = (src >= lo) & (src <= hi) & (
                (src < diag) | ((src == diag) & (key_pos <= rows))
            )
        for g in range(group):
            qg = q_ref[:, g * HEAD_SIZE:(g + 1) * HEAD_SIZE]
            s = lax.dot_general(
                qg, k, (((1,), (1,)), ((), ())), preferred_element_type=jnp.float32
            ) * scale
            if masked:
                s = jnp.where(allowed, s, NEGATIVE_FILL)
            m_prev = m_out[g]
            m_new = jnp.maximum(m_prev, jnp.max(s, axis=1, keepdims=True))
            p = jnp.exp(s - m_new[:, :1])
            alpha = jnp.exp(m_prev - m_new)
            l_out[g] = alpha * l_out[g] + jnp.sum(p, axis=1, keepdims=True)
            acc_out[g] = acc_out[g] * alpha + lax.dot_general(
                p.astype(jnp.bfloat16), v, (((1,), (0,)), ((), ())),
                preferred_element_type=jnp.float32,
            )
            m_out[g] = m_new

    full = (tile_lo >= lo) & (tile_hi <= hi) & (tile_hi < diag)
    touched = (tile_hi >= lo) & (tile_lo <= hi)

    @pl.when(full)
    def _full():
        step(False)

    @pl.when(touched & jnp.logical_not(full))
    def _diag():
        step(True)

    if last:
        @pl.when(t == pl.num_programs(2) - 1)
        def _fin():
            for g in range(group):
                o_ref[:, g * HEAD_SIZE:(g + 1) * HEAD_SIZE] = (
                    acc_out[g] / l_out[g]
                ).astype(o_ref.dtype)


def long_attention_chunk(b_arr, q_long, kv_chunk, state, chunk, first, last):
    rows, q_cols = q_long.shape
    kv_cols = kv_chunk.shape[1] // 2
    heads_kv = kv_cols // HEAD_SIZE
    group = q_cols // kv_cols
    chunk_rows = LONG_DEV // LONG_CHUNKS
    total = kv_chunk.shape[0]
    tk = min(512, total)
    per_tile = tk // chunk_rows
    tq = LONG_DEV
    kernel = functools.partial(
        flash_kernel, group=group, tq=tq, tk=tk, chunk_rows=chunk_rows, chunk=chunk,
        first=first, last=last,
    )
    state_shape = jax.ShapeDtypeStruct((heads_kv, group, rows, HEAD_SIZE), jnp.float32)
    state_spec = pl.BlockSpec((None, group, tq, HEAD_SIZE), lambda h, i, t, b: (h, 0, i, 0))
    def tile_of(t, b):
        return jnp.minimum(
            jnp.maximum(t, b[0] // per_tile), jnp.maximum(b[0], b[1]) // per_tile
        )

    kv_spec_k = pl.BlockSpec((tk, HEAD_SIZE), lambda h, i, t, b: (tile_of(t, b), h))
    kv_spec_v = pl.BlockSpec((tk, HEAD_SIZE), lambda h, i, t, b: (tile_of(t, b), heads_kv + h))
    q_spec = pl.BlockSpec((tq, group * HEAD_SIZE), lambda h, i, t, b: (i, h))
    in_specs = [q_spec, kv_spec_k, kv_spec_v]
    operands = [b_arr, q_long, kv_chunk, kv_chunk]
    aliases = {}
    if not first:
        in_specs += [state_spec] * 3
        operands += list(state)
    if last:
        out_specs = q_spec
        out_shape = jax.ShapeDtypeStruct((rows, q_cols), jnp.bfloat16)
    else:
        out_specs = [state_spec] * 3
        out_shape = [state_shape] * 3
        if not first:
            aliases = {4: 0, 5: 1, 6: 2}
    grid_spec = pltpu.PrefetchScalarGridSpec(
        num_scalar_prefetch=1,
        grid=(heads_kv, rows // tq, total // tk),
        in_specs=in_specs,
        out_specs=out_specs,
    )
    return pl.pallas_call(
        kernel,
        grid_spec=grid_spec,
        out_shape=out_shape,
        input_output_aliases=aliases,
        compiler_params=pltpu.CompilerParams(
            dimension_semantics=("arbitrary", "arbitrary", "arbitrary")
        ),
    )(*operands)


def long_attention(my_index, req_count, q_long, k_long, v_long):
    half = req_count // 2
    chunk_rows = LONG_DEV // 2
    rows, q_cols = q_long.shape
    heavy = my_index >= half
    partner = jnp.where(heavy, my_index - half, my_index + half)
    gathered = []
    for c in range(2):
        kv = jnp.concatenate(
            [k_long[c * chunk_rows:(c + 1) * chunk_rows], v_long[c * chunk_rows:(c + 1) * chunk_rows]],
            axis=1,
        )
        gathered.append(lax.all_gather(kv, "req", axis=0, tiled=True))
    partner_q = lax.ppermute(q_long, "req", [(s + half, s) for s in range(half)])

    def params(lo, hi, diag):
        return jnp.stack([lo, hi, diag]).astype(jnp.int32)

    own_lo = jnp.where(heavy, half, 0)
    state = long_attention_chunk(
        params(own_lo, my_index, my_index), q_long, gathered[0], None, 0, True, False
    )
    help_hi = jnp.where(heavy, -1, half - 1)
    helped = long_attention_chunk(
        params(jnp.int32(0), help_hi, partner), partner_q, gathered[0], None, 0, True, False
    )
    state, helped = lax.optimization_barrier((state, helped))
    h_max, h_sum, h_acc = helped
    h_out = (h_acc / jnp.where(h_sum > 0, h_sum, 1.0)).astype(jnp.bfloat16)
    back = [(s, s + half) for s in range(half)]
    h_out = lax.ppermute(h_out, "req", back)
    h_max = lax.ppermute(h_max[..., :1], "req", back)
    h_sum = lax.ppermute(h_sum[..., :1], "req", back)
    own_max, own_sum, own_acc = long_attention_chunk(
        params(jnp.int32(0), my_index, my_index), q_long, gathered[1], state, 1, False, False,
    )
    top = jnp.maximum(own_max, jnp.where(heavy, h_max, NEGATIVE_FILL))
    own_w = jnp.exp(own_max - top)
    help_w = jnp.where(heavy, jnp.exp(h_max - top) * h_sum, 0.0)
    total = own_sum * own_w + help_w
    out = (own_acc * own_w + h_out.astype(jnp.float32) * help_w) / total
    heads_kv, group = out.shape[0], out.shape[1]
    return out.transpose(2, 0, 1, 3).reshape(rows, heads_kv * group * HEAD_SIZE).astype(jnp.bfloat16)


def short_attention(my_index, req_count, q_short, k_short, v_short, short_pages, short_fill):
    heads_kv = k_short.shape[1] // HEAD_SIZE
    group = q_short.shape[1] // k_short.shape[1]
    perm = [(s, s + 1) for s in range(req_count - 1)]
    k_prev = lax.ppermute(k_short, "req", perm)
    v_prev = lax.ppermute(v_short, "req", perm)
    own_off = my_index * SHORT_DEV + jnp.arange(SHORT_DEV, dtype=jnp.int32)
    key_off = (my_index - 1) * SHORT_DEV + jnp.arange(2 * SHORT_DEV, dtype=jnp.int32)
    q_seg, q_pos, q_live = short_layout(own_off, short_pages, short_fill)
    k_seg, k_pos, k_live = short_layout(key_off, short_pages, short_fill)
    k_live = k_live & (key_off >= 0)
    allowed = (q_seg[:, None] == k_seg[None, :]) & (k_pos[None, :] <= q_pos[:, None]) & k_live[None, :]
    keys = jnp.concatenate([k_prev, k_short]).reshape(2 * SHORT_DEV, heads_kv, HEAD_SIZE)
    values = jnp.concatenate([v_prev, v_short]).reshape(2 * SHORT_DEV, heads_kv, HEAD_SIZE)
    qs = q_short.reshape(SHORT_DEV, heads_kv, group, HEAD_SIZE)
    scores = jnp.einsum(
        "qhgd,khd->hgqk", qs, keys, preferred_element_type=jnp.float32
    ) * HEAD_SIZE ** (-0.5)
    scores = jnp.where(allowed[None, None], scores, NEGATIVE_FILL)
    row_max = jnp.max(scores, axis=-1, keepdims=True)
    weights = jnp.exp(scores - row_max)
    denom = jnp.sum(weights, axis=-1)
    weighted = jnp.einsum(
        "hgqk,khd->qhgd", weights.astype(jnp.bfloat16), values, preferred_element_type=jnp.float32
    )
    attended = weighted / jnp.transpose(denom, (2, 0, 1))[..., None]
    attended = jnp.where(q_live[:, None, None, None], attended, 0.0)
    return attended.reshape(SHORT_DEV, -1).astype(jnp.bfloat16)


def local(
    queries,
    rotated_key_rows,
    stream_value_rows,
    out_weight,
    short_pages,
    short_fill,
    stream_page_table,
):
    req_count = lax.axis_size("req")
    my_index = lax.axis_index("req")
    tok_rows = queries.shape[0]
    pages_per = tok_rows // PAGE_ROWS
    capacity = (pages_per + req_count - 1) // req_count
    slot_count = capacity * req_count
    width = rotated_key_rows.shape[1]
    own_off = my_index * SHORT_DEV + jnp.arange(SHORT_DEV, dtype=jnp.int32)
    short_live = short_layout(own_off, short_pages, short_fill)[2]
    own_live = jnp.concatenate([jnp.ones((LONG_DEV,), bool), short_live])
    kv_rows = jnp.stack([rotated_key_rows, stream_value_rows])
    kv_rows = jnp.where(own_live[None, :, None], kv_rows, jnp.zeros_like(kv_rows))
    kv_pages = kv_rows.reshape(2, pages_per, PAGE_ROWS * width)
    page_map = stream_page_table.reshape(req_count, pages_per)
    owners = page_map // slot_count
    earlier = (
        jnp.arange(pages_per, dtype=jnp.int32)[:, None]
        > jnp.arange(pages_per, dtype=jnp.int32)[None, :]
    )
    matching = owners[:, :, None] == owners[:, None, :]
    order_in = jnp.sum((matching & earlier[None]).astype(jnp.int32), axis=2)
    my_owner = owners[my_index]
    my_order = order_in[my_index]
    send_map = (
        (my_owner * capacity + my_order)[:, None]
        == jnp.arange(slot_count, dtype=jnp.int32)[None, :]
    ).astype(jnp.bfloat16)
    outgoing = jnp.einsum(
        "ks,xkr->xsr", send_map, kv_pages, preferred_element_type=jnp.float32
    ).astype(jnp.bfloat16)
    outgoing = outgoing.reshape(2, req_count, capacity, PAGE_ROWS * width)
    incoming = lax.all_to_all(outgoing, "req", split_axis=1, concat_axis=1, tiled=True)
    mine_mask = owners == my_index
    placing = mine_mask[:, :, None] & (
        order_in[:, :, None] == jnp.arange(capacity, dtype=jnp.int32)[None, None, :]
    )
    target = (page_map % slot_count)[:, :, None] == jnp.arange(slot_count, dtype=jnp.int32)[
        None, None, :
    ]
    routing = jnp.einsum(
        "skc,skt->sct",
        placing.astype(jnp.bfloat16),
        target.astype(jnp.bfloat16),
        preferred_element_type=jnp.float32,
    ).astype(jnp.bfloat16)
    incoming, queries = lax.optimization_barrier((incoming, queries))
    att_long = long_attention(
        my_index, req_count, queries[:LONG_DEV], rotated_key_rows[:LONG_DEV], stream_value_rows[:LONG_DEV]
    )
    att_short = short_attention(
        my_index,
        req_count,
        queries[LONG_DEV:],
        rotated_key_rows[LONG_DEV:],
        stream_value_rows[LONG_DEV:],
        short_pages,
        short_fill,
    )
    attended = jnp.concatenate([att_long, att_short])
    mixed_out = lax.psum_scatter(
        jnp.dot(attended, out_weight, preferred_element_type=jnp.float32).astype(jnp.bfloat16),
        "tp",
        scatter_dimension=0,
        tiled=True,
    )
    written_cache = jnp.einsum(
        "sct,xscr->xtr", routing, incoming, preferred_element_type=jnp.float32
    ).astype(jnp.bfloat16)
    written_cache = written_cache.reshape(2, slot_count, PAGE_ROWS, width)
    return (mixed_out, written_cache)


def solution(mesh):
    in_specs = (P("req", "tp"), P("req", "tp"), P("req", "tp"), P("tp", None), P(), P(), P())
    out_specs = (P(("req", "tp"), None), P(None, "req", None, "tp"))
    return jax.shard_map(local, mesh=mesh, in_specs=in_specs, out_specs=out_specs, check_vma=False)
```

```python
import functools

import jax
import jax.numpy as jnp
from jax import lax
from jax.experimental import pallas as pl
from jax.experimental.pallas import tpu as pltpu
from jax.sharding import PartitionSpec as P

HEAD_SIZE = 128
LONG_DEV = 512
SHORT_DEV = 128
PAGE_ROWS = 16
BLOCK_TOKENS = 640
LONG_CHUNKS = 2


NEGATIVE_FILL = -1e30


def short_layout(offset, short_pages, short_fill):
    page_id = offset // PAGE_ROWS
    page_ends = jnp.cumsum(short_pages)
    page_starts = page_ends - short_pages
    limits = page_starts * PAGE_ROWS + (short_pages - 1) * PAGE_ROWS + short_fill
    owner_hit = page_ends[None, :] <= page_id[:, None]
    prompt = jnp.sum(owner_hit.astype(jnp.int32), axis=1)
    select = jnp.arange(short_pages.shape[0], dtype=jnp.int32)[None, :] == prompt[:, None]
    begin_at = jnp.sum(jnp.where(select, page_starts[None, :], 0), axis=1) * PAGE_ROWS
    limit_at = jnp.sum(jnp.where(select, limits[None, :], 0), axis=1)
    return (prompt, offset - begin_at, offset < limit_at)


def flash_kernel(b_ref, q_ref, k_ref, v_ref, *refs, group, tq, tk, chunk_rows, chunk, first, last):
    if first:
        m_out, l_out, acc_out = refs[-3:]
        m_in, l_in, acc_in = m_out, l_out, acc_out
    elif last:
        m_in, l_in, acc_in, o_ref = refs
        m_out, l_out, acc_out = m_in, l_in, acc_in
    else:
        m_in, l_in, acc_in, m_out, l_out, acc_out = refs
    i = pl.program_id(1)
    t = pl.program_id(2)
    b = b_ref[0]
    per_tile = tk // chunk_rows
    scale = HEAD_SIZE ** (-0.5)

    @pl.when(t == 0)
    def _init():
        if first:
            m_out[...] = jnp.full(m_out.shape, NEGATIVE_FILL, jnp.float32)
            l_out[...] = jnp.zeros(l_out.shape, jnp.float32)
            acc_out[...] = jnp.zeros(acc_out.shape, jnp.float32)
        elif not last:
            m_out[...] = m_in[...]
            l_out[...] = l_in[...]
            acc_out[...] = acc_in[...]

    def step(masked):
        k = k_ref[...]
        v = v_ref[...]
        v_ext = jnp.concatenate([v, jnp.ones(v.shape, v.dtype)], axis=1)
        if masked:
            rows = i * tq + lax.broadcasted_iota(jnp.int32, (tq, tk), 0)
            cols = lax.broadcasted_iota(jnp.int32, (tq, tk), 1)
            src = t * per_tile + cols // chunk_rows
            key_pos = chunk * chunk_rows + cols % chunk_rows
            allowed = (src < b) | ((src == b) & (key_pos <= rows))
        for g in range(group):
            qg = q_ref[:, g * HEAD_SIZE:(g + 1) * HEAD_SIZE]
            s = lax.dot_general(
                qg, k, (((1,), (1,)), ((), ())), preferred_element_type=jnp.float32
            ) * scale
            if masked:
                s = jnp.where(allowed, s, NEGATIVE_FILL)
            m_prev = m_out[g]
            m_new = jnp.maximum(m_prev, jnp.max(s, axis=1, keepdims=True))
            p = jnp.exp(s - m_new[:, :1])
            alpha = jnp.exp(m_prev - m_new)
            pv = lax.dot_general(
                p.astype(jnp.bfloat16), v_ext, (((1,), (0,)), ((), ())),
                preferred_element_type=jnp.float32,
            )
            l_out[g] = alpha * l_out[g] + pv[:, HEAD_SIZE:]
            acc_out[g] = acc_out[g] * alpha + pv[:, :HEAD_SIZE]
            m_out[g] = m_new

    @pl.when(t * per_tile + per_tile - 1 < b)
    def _full():
        step(False)

    @pl.when((t * per_tile + per_tile - 1 >= b) & (t * per_tile <= b))
    def _diag():
        step(True)

    if last:
        @pl.when(t == pl.num_programs(2) - 1)
        def _fin():
            for g in range(group):
                o_ref[:, g * HEAD_SIZE:(g + 1) * HEAD_SIZE] = (
                    acc_out[g] / l_out[g]
                ).astype(o_ref.dtype)


def long_attention_chunk(b_arr, q_long, kv_chunk, state, chunk, first, last):
    rows, q_cols = q_long.shape
    kv_cols = kv_chunk.shape[1] // 2
    heads_kv = kv_cols // HEAD_SIZE
    group = q_cols // kv_cols
    chunk_rows = LONG_DEV // LONG_CHUNKS
    total = kv_chunk.shape[0]
    tk = min(512, total)
    per_tile = tk // chunk_rows
    tq = LONG_DEV
    kernel = functools.partial(
        flash_kernel, group=group, tq=tq, tk=tk, chunk_rows=chunk_rows, chunk=chunk,
        first=first, last=last,
    )
    state_shape = jax.ShapeDtypeStruct((heads_kv, group, rows, HEAD_SIZE), jnp.float32)
    state_spec = pl.BlockSpec((None, group, tq, HEAD_SIZE), lambda h, i, t, b: (h, 0, i, 0))
    kv_spec_k = pl.BlockSpec((tk, HEAD_SIZE), lambda h, i, t, b: (jnp.minimum(t, b[0] // per_tile), h))
    kv_spec_v = pl.BlockSpec(
        (tk, HEAD_SIZE), lambda h, i, t, b: (jnp.minimum(t, b[0] // per_tile), heads_kv + h)
    )
    q_spec = pl.BlockSpec((tq, group * HEAD_SIZE), lambda h, i, t, b: (i, h))
    in_specs = [q_spec, kv_spec_k, kv_spec_v]
    operands = [b_arr, q_long, kv_chunk, kv_chunk]
    aliases = {}
    if not first:
        in_specs += [state_spec] * 3
        operands += list(state)
    if last:
        out_specs = q_spec
        out_shape = jax.ShapeDtypeStruct((rows, q_cols), jnp.bfloat16)
    else:
        out_specs = [state_spec] * 3
        out_shape = [state_shape] * 3
        if not first:
            aliases = {4: 0, 5: 1, 6: 2}
    grid_spec = pltpu.PrefetchScalarGridSpec(
        num_scalar_prefetch=1,
        grid=(heads_kv, rows // tq, total // tk),
        in_specs=in_specs,
        out_specs=out_specs,
    )
    return pl.pallas_call(
        kernel,
        grid_spec=grid_spec,
        out_shape=out_shape,
        input_output_aliases=aliases,
        compiler_params=pltpu.CompilerParams(
            dimension_semantics=("arbitrary", "arbitrary", "arbitrary")
        ),
    )(*operands)


def long_attention(my_index, q_long, k_long, v_long):
    b_arr = jnp.reshape(my_index, (1,)).astype(jnp.int32)
    chunk_rows = LONG_DEV // LONG_CHUNKS
    state = None
    for c in range(LONG_CHUNKS):
        kv = jnp.concatenate(
            [k_long[c * chunk_rows:(c + 1) * chunk_rows], v_long[c * chunk_rows:(c + 1) * chunk_rows]],
            axis=1,
        )
        kv = lax.all_gather(kv, "req", axis=0, tiled=True)
        state = long_attention_chunk(
            b_arr, q_long, kv, state, c, c == 0, c == LONG_CHUNKS - 1
        )
    return state


def short_attention(my_index, req_count, q_short, k_short, v_short, short_pages, short_fill):
    heads_kv = k_short.shape[1] // HEAD_SIZE
    group = q_short.shape[1] // k_short.shape[1]
    perm = [(s, s + 1) for s in range(req_count - 1)]
    k_prev = lax.ppermute(k_short, "req", perm)
    v_prev = lax.ppermute(v_short, "req", perm)
    own_off = my_index * SHORT_DEV + jnp.arange(SHORT_DEV, dtype=jnp.int32)
    key_off = (my_index - 1) * SHORT_DEV + jnp.arange(2 * SHORT_DEV, dtype=jnp.int32)
    q_seg, q_pos, q_live = short_layout(own_off, short_pages, short_fill)
    k_seg, k_pos, k_live = short_layout(key_off, short_pages, short_fill)
    k_live = k_live & (key_off >= 0)
    allowed = (q_seg[:, None] == k_seg[None, :]) & (k_pos[None, :] <= q_pos[:, None]) & k_live[None, :]
    keys = jnp.concatenate([k_prev, k_short]).reshape(2 * SHORT_DEV, heads_kv, HEAD_SIZE)
    values = jnp.concatenate([v_prev, v_short]).reshape(2 * SHORT_DEV, heads_kv, HEAD_SIZE)
    qs = q_short.reshape(SHORT_DEV, heads_kv, group, HEAD_SIZE)
    scores = jnp.einsum(
        "qhgd,khd->hgqk", qs, keys, preferred_element_type=jnp.float32
    ) * HEAD_SIZE ** (-0.5)
    scores = jnp.where(allowed[None, None], scores, NEGATIVE_FILL)
    row_max = jnp.max(scores, axis=-1, keepdims=True)
    weights = jnp.exp(scores - row_max)
    denom = jnp.sum(weights, axis=-1)
    weighted = jnp.einsum(
        "hgqk,khd->qhgd", weights.astype(jnp.bfloat16), values, preferred_element_type=jnp.float32
    )
    attended = weighted / jnp.transpose(denom, (2, 0, 1))[..., None]
    attended = jnp.where(q_live[:, None, None, None], attended, 0.0)
    return attended.reshape(SHORT_DEV, -1).astype(jnp.bfloat16)


def local(
    queries,
    rotated_key_rows,
    stream_value_rows,
    out_weight,
    short_pages,
    short_fill,
    stream_page_table,
):
    req_count = lax.axis_size("req")
    my_index = lax.axis_index("req")
    tok_rows = queries.shape[0]
    pages_per = tok_rows // PAGE_ROWS
    capacity = (pages_per + req_count - 1) // req_count
    slot_count = capacity * req_count
    width = rotated_key_rows.shape[1]
    own_off = my_index * SHORT_DEV + jnp.arange(SHORT_DEV, dtype=jnp.int32)
    short_live = short_layout(own_off, short_pages, short_fill)[2]
    own_live = jnp.concatenate([jnp.ones((LONG_DEV,), bool), short_live])
    kv_rows = jnp.stack([rotated_key_rows, stream_value_rows])
    kv_rows = jnp.where(own_live[None, :, None], kv_rows, jnp.zeros_like(kv_rows))
    kv_pages = kv_rows.reshape(2, pages_per, PAGE_ROWS * width)
    page_map = stream_page_table.reshape(req_count, pages_per)
    owners = page_map // slot_count
    earlier = (
        jnp.arange(pages_per, dtype=jnp.int32)[:, None]
        > jnp.arange(pages_per, dtype=jnp.int32)[None, :]
    )
    matching = owners[:, :, None] == owners[:, None, :]
    order_in = jnp.sum((matching & earlier[None]).astype(jnp.int32), axis=2)
    my_owner = owners[my_index]
    my_order = order_in[my_index]
    send_map = (
        (my_owner * capacity + my_order)[:, None]
        == jnp.arange(slot_count, dtype=jnp.int32)[None, :]
    ).astype(jnp.bfloat16)
    outgoing = jnp.einsum(
        "ks,xkr->xsr", send_map, kv_pages, preferred_element_type=jnp.float32
    ).astype(jnp.bfloat16)
    outgoing = outgoing.reshape(2, req_count, capacity, PAGE_ROWS * width)
    incoming = lax.all_to_all(outgoing, "req", split_axis=1, concat_axis=1, tiled=True)
    mine_mask = owners == my_index
    placing = mine_mask[:, :, None] & (
        order_in[:, :, None] == jnp.arange(capacity, dtype=jnp.int32)[None, None, :]
    )
    target = (page_map % slot_count)[:, :, None] == jnp.arange(slot_count, dtype=jnp.int32)[
        None, None, :
    ]
    routing = jnp.einsum(
        "skc,skt->sct",
        placing.astype(jnp.bfloat16),
        target.astype(jnp.bfloat16),
        preferred_element_type=jnp.float32,
    ).astype(jnp.bfloat16)
    incoming, queries = lax.optimization_barrier((incoming, queries))
    att_long = long_attention(
        my_index, queries[:LONG_DEV], rotated_key_rows[:LONG_DEV], stream_value_rows[:LONG_DEV]
    )
    att_short = short_attention(
        my_index,
        req_count,
        queries[LONG_DEV:],
        rotated_key_rows[LONG_DEV:],
        stream_value_rows[LONG_DEV:],
        short_pages,
        short_fill,
    )
    attended = jnp.concatenate([att_long, att_short])
    mixed_out = lax.psum_scatter(
        jnp.dot(attended, out_weight, preferred_element_type=jnp.float32).astype(jnp.bfloat16),
        "tp",
        scatter_dimension=0,
        tiled=True,
    )
    written_cache = jnp.einsum(
        "sct,xscr->xtr", routing, incoming, preferred_element_type=jnp.float32
    ).astype(jnp.bfloat16)
    written_cache = written_cache.reshape(2, slot_count, PAGE_ROWS, width)
    return (mixed_out, written_cache)


def solution(mesh):
    in_specs = (P("req", "tp"), P("req", "tp"), P("req", "tp"), P("tp", None), P(), P(), P())
    out_specs = (P(("req", "tp"), None), P(None, "req", None, "tp"))
    return jax.shard_map(local, mesh=mesh, in_specs=in_specs, out_specs=out_specs, check_vma=False)
```

```python
import functools

import jax
import jax.numpy as jnp
from jax import lax
from jax.experimental import pallas as pl
from jax.experimental.pallas import tpu as pltpu
from jax.sharding import PartitionSpec as P

HEAD_SIZE = 128
LONG_DEV = 512
SHORT_DEV = 128
PAGE_ROWS = 16
BLOCK_TOKENS = 640
LONG_CHUNKS = 2


NEGATIVE_FILL = -1e30
LOG2_E = 1.4426950408889634


def short_layout(offset, short_pages, short_fill):
    page_id = offset // PAGE_ROWS
    page_ends = jnp.cumsum(short_pages)
    page_starts = page_ends - short_pages
    limits = page_starts * PAGE_ROWS + (short_pages - 1) * PAGE_ROWS + short_fill
    owner_hit = page_ends[None, :] <= page_id[:, None]
    prompt = jnp.sum(owner_hit.astype(jnp.int32), axis=1)
    select = jnp.arange(short_pages.shape[0], dtype=jnp.int32)[None, :] == prompt[:, None]
    begin_at = jnp.sum(jnp.where(select, page_starts[None, :], 0), axis=1) * PAGE_ROWS
    limit_at = jnp.sum(jnp.where(select, limits[None, :], 0), axis=1)
    return (prompt, offset - begin_at, offset < limit_at)


def flash_kernel(b_ref, q_ref, k_ref, v_ref, *refs, group, tq, tk, chunk_rows, chunk, first, last):
    if first:
        m_out, l_out, acc_out = refs[-3:]
        m_in, l_in, acc_in = m_out, l_out, acc_out
    elif last:
        m_in, l_in, acc_in, o_ref = refs
        m_out, l_out, acc_out = m_in, l_in, acc_in
    else:
        m_in, l_in, acc_in, m_out, l_out, acc_out = refs
    i = pl.program_id(1)
    t = pl.program_id(2)
    b = b_ref[0]
    per_tile = tk // chunk_rows
    scale = HEAD_SIZE ** (-0.5)
    log2_scale = scale * LOG2_E

    @pl.when(t == 0)
    def _init():
        if first:
            m_out[...] = jnp.full(m_out.shape, NEGATIVE_FILL, jnp.float32)
            l_out[...] = jnp.zeros(l_out.shape, jnp.float32)
            acc_out[...] = jnp.zeros(acc_out.shape, jnp.float32)
        elif not last:
            m_out[...] = m_in[...]
            l_out[...] = l_in[...]
            acc_out[...] = acc_in[...]

    def step(masked):
        k = k_ref[...]
        v = v_ref[...]
        v_ext = jnp.concatenate([v, jnp.ones(v.shape, v.dtype)], axis=1)
        if masked:
            rows = i * tq + lax.broadcasted_iota(jnp.int32, (tq, tk), 0)
            cols = lax.broadcasted_iota(jnp.int32, (tq, tk), 1)
            src = t * per_tile + cols // chunk_rows
            key_pos = chunk * chunk_rows + cols % chunk_rows
            allowed = (src < b) | ((src == b) & (key_pos <= rows))
        for g in range(group):
            qg = q_ref[:, g * HEAD_SIZE:(g + 1) * HEAD_SIZE]
            s = lax.dot_general(
                qg, k, (((1,), (1,)), ((), ())), preferred_element_type=jnp.float32
            )
            if masked:
                s = jnp.where(allowed, s, NEGATIVE_FILL)
            m_prev = m_out[g]
            m_new = jnp.maximum(m_prev, jnp.max(s, axis=1, keepdims=True) * scale)
            p = jnp.exp2(s * log2_scale - m_new[:, :1] * LOG2_E)
            alpha = jnp.exp2((m_prev - m_new) * LOG2_E)
            pv = lax.dot_general(
                p.astype(jnp.bfloat16), v_ext, (((1,), (0,)), ((), ())),
                preferred_element_type=jnp.float32,
            )
            l_out[g] = alpha * l_out[g] + pv[:, HEAD_SIZE:]
            acc_out[g] = acc_out[g] * alpha + pv[:, :HEAD_SIZE]
            m_out[g] = m_new

    @pl.when(t * per_tile + per_tile - 1 < b)
    def _full():
        step(False)

    @pl.when((t * per_tile + per_tile - 1 >= b) & (t * per_tile <= b))
    def _diag():
        step(True)

    if last:
        @pl.when(t == pl.num_programs(2) - 1)
        def _fin():
            for g in range(group):
                o_ref[:, g * HEAD_SIZE:(g + 1) * HEAD_SIZE] = (
                    acc_out[g] / l_out[g]
                ).astype(o_ref.dtype)


def long_attention_chunk(b_arr, q_long, kv_chunk, state, chunk, first, last):
    rows, q_cols = q_long.shape
    kv_cols = kv_chunk.shape[1] // 2
    heads_kv = kv_cols // HEAD_SIZE
    group = q_cols // kv_cols
    chunk_rows = LONG_DEV // LONG_CHUNKS
    total = kv_chunk.shape[0]
    tk = min(512, total)
    per_tile = tk // chunk_rows
    tq = LONG_DEV
    kernel = functools.partial(
        flash_kernel, group=group, tq=tq, tk=tk, chunk_rows=chunk_rows, chunk=chunk,
        first=first, last=last,
    )
    state_shape = jax.ShapeDtypeStruct((heads_kv, group, rows, HEAD_SIZE), jnp.float32)
    state_spec = pl.BlockSpec((None, group, tq, HEAD_SIZE), lambda h, i, t, b: (h, 0, i, 0))
    kv_spec_k = pl.BlockSpec((tk, HEAD_SIZE), lambda h, i, t, b: (jnp.minimum(t, b[0] // per_tile), h))
    kv_spec_v = pl.BlockSpec(
        (tk, HEAD_SIZE), lambda h, i, t, b: (jnp.minimum(t, b[0] // per_tile), heads_kv + h)
    )
    q_spec = pl.BlockSpec((tq, group * HEAD_SIZE), lambda h, i, t, b: (i, h))
    in_specs = [q_spec, kv_spec_k, kv_spec_v]
    operands = [b_arr, q_long, kv_chunk, kv_chunk]
    aliases = {}
    if not first:
        in_specs += [state_spec] * 3
        operands += list(state)
    if last:
        out_specs = q_spec
        out_shape = jax.ShapeDtypeStruct((rows, q_cols), jnp.bfloat16)
    else:
        out_specs = [state_spec] * 3
        out_shape = [state_shape] * 3
        if not first:
            aliases = {4: 0, 5: 1, 6: 2}
    grid_spec = pltpu.PrefetchScalarGridSpec(
        num_scalar_prefetch=1,
        grid=(heads_kv, rows // tq, total // tk),
        in_specs=in_specs,
        out_specs=out_specs,
    )
    return pl.pallas_call(
        kernel,
        grid_spec=grid_spec,
        out_shape=out_shape,
        input_output_aliases=aliases,
        compiler_params=pltpu.CompilerParams(
            dimension_semantics=("arbitrary", "arbitrary", "arbitrary")
        ),
    )(*operands)


def long_attention(my_index, q_long, k_long, v_long):
    b_arr = jnp.reshape(my_index, (1,)).astype(jnp.int32)
    chunk_rows = LONG_DEV // LONG_CHUNKS
    state = None
    for c in range(LONG_CHUNKS):
        kv = jnp.concatenate(
            [k_long[c * chunk_rows:(c + 1) * chunk_rows], v_long[c * chunk_rows:(c + 1) * chunk_rows]],
            axis=1,
        )
        kv = lax.all_gather(kv, "req", axis=0, tiled=True)
        state = long_attention_chunk(
            b_arr, q_long, kv, state, c, c == 0, c == LONG_CHUNKS - 1
        )
    return state


def short_attention(my_index, req_count, q_short, k_short, v_short, short_pages, short_fill):
    heads_kv = k_short.shape[1] // HEAD_SIZE
    group = q_short.shape[1] // k_short.shape[1]
    perm = [(s, s + 1) for s in range(req_count - 1)]
    k_prev = lax.ppermute(k_short, "req", perm)
    v_prev = lax.ppermute(v_short, "req", perm)
    own_off = my_index * SHORT_DEV + jnp.arange(SHORT_DEV, dtype=jnp.int32)
    key_off = (my_index - 1) * SHORT_DEV + jnp.arange(2 * SHORT_DEV, dtype=jnp.int32)
    q_seg, q_pos, q_live = short_layout(own_off, short_pages, short_fill)
    k_seg, k_pos, k_live = short_layout(key_off, short_pages, short_fill)
    k_live = k_live & (key_off >= 0)
    allowed = (q_seg[:, None] == k_seg[None, :]) & (k_pos[None, :] <= q_pos[:, None]) & k_live[None, :]
    keys = jnp.concatenate([k_prev, k_short]).reshape(2 * SHORT_DEV, heads_kv, HEAD_SIZE)
    values = jnp.concatenate([v_prev, v_short]).reshape(2 * SHORT_DEV, heads_kv, HEAD_SIZE)
    qs = q_short.reshape(SHORT_DEV, heads_kv, group, HEAD_SIZE)
    scores = jnp.einsum(
        "qhgd,khd->hgqk", qs, keys, preferred_element_type=jnp.float32
    ) * HEAD_SIZE ** (-0.5)
    scores = jnp.where(allowed[None, None], scores, NEGATIVE_FILL)
    row_max = jnp.max(scores, axis=-1, keepdims=True)
    weights = jnp.exp(scores - row_max)
    denom = jnp.sum(weights, axis=-1)
    weighted = jnp.einsum(
        "hgqk,khd->qhgd", weights.astype(jnp.bfloat16), values, preferred_element_type=jnp.float32
    )
    attended = weighted / jnp.transpose(denom, (2, 0, 1))[..., None]
    attended = jnp.where(q_live[:, None, None, None], attended, 0.0)
    return attended.reshape(SHORT_DEV, -1).astype(jnp.bfloat16)


def local(
    queries,
    rotated_key_rows,
    stream_value_rows,
    out_weight,
    short_pages,
    short_fill,
    stream_page_table,
):
    req_count = lax.axis_size("req")
    my_index = lax.axis_index("req")
    tok_rows = queries.shape[0]
    pages_per = tok_rows // PAGE_ROWS
    capacity = (pages_per + req_count - 1) // req_count
    slot_count = capacity * req_count
    width = rotated_key_rows.shape[1]
    own_off = my_index * SHORT_DEV + jnp.arange(SHORT_DEV, dtype=jnp.int32)
    short_live = short_layout(own_off, short_pages, short_fill)[2]
    own_live = jnp.concatenate([jnp.ones((LONG_DEV,), bool), short_live])
    kv_rows = jnp.stack([rotated_key_rows, stream_value_rows])
    kv_rows = jnp.where(own_live[None, :, None], kv_rows, jnp.zeros_like(kv_rows))
    kv_pages = kv_rows.reshape(2, pages_per, PAGE_ROWS * width)
    page_map = stream_page_table.reshape(req_count, pages_per)
    owners = page_map // slot_count
    earlier = (
        jnp.arange(pages_per, dtype=jnp.int32)[:, None]
        > jnp.arange(pages_per, dtype=jnp.int32)[None, :]
    )
    matching = owners[:, :, None] == owners[:, None, :]
    order_in = jnp.sum((matching & earlier[None]).astype(jnp.int32), axis=2)
    my_owner = owners[my_index]
    my_order = order_in[my_index]
    send_map = (
        (my_owner * capacity + my_order)[:, None]
        == jnp.arange(slot_count, dtype=jnp.int32)[None, :]
    ).astype(jnp.bfloat16)
    outgoing = jnp.einsum(
        "ks,xkr->xsr", send_map, kv_pages, preferred_element_type=jnp.float32
    ).astype(jnp.bfloat16)
    outgoing = outgoing.reshape(2, req_count, capacity, PAGE_ROWS * width)
    incoming = lax.all_to_all(outgoing, "req", split_axis=1, concat_axis=1, tiled=True)
    mine_mask = owners == my_index
    placing = mine_mask[:, :, None] & (
        order_in[:, :, None] == jnp.arange(capacity, dtype=jnp.int32)[None, None, :]
    )
    target = (page_map % slot_count)[:, :, None] == jnp.arange(slot_count, dtype=jnp.int32)[
        None, None, :
    ]
    routing = jnp.einsum(
        "skc,skt->sct",
        placing.astype(jnp.bfloat16),
        target.astype(jnp.bfloat16),
        preferred_element_type=jnp.float32,
    ).astype(jnp.bfloat16)
    incoming, queries = lax.optimization_barrier((incoming, queries))
    att_long = long_attention(
        my_index, queries[:LONG_DEV], rotated_key_rows[:LONG_DEV], stream_value_rows[:LONG_DEV]
    )
    att_short = short_attention(
        my_index,
        req_count,
        queries[LONG_DEV:],
        rotated_key_rows[LONG_DEV:],
        stream_value_rows[LONG_DEV:],
        short_pages,
        short_fill,
    )
    attended = jnp.concatenate([att_long, att_short])
    tp_count = lax.axis_size("tp")
    if tp_count == 2:
        tp_index = lax.axis_index("tp")
        half_rows = tok_rows // 2
        theirs = lax.dynamic_slice_in_dim(attended, (1 - tp_index) * half_rows, half_rows, 0)
        sent = jnp.dot(theirs, out_weight, preferred_element_type=jnp.float32).astype(jnp.bfloat16)
        received = lax.ppermute(sent, "tp", [(0, 1), (1, 0)])
        mine = lax.dynamic_slice_in_dim(attended, tp_index * half_rows, half_rows, 0)
        own = jnp.dot(mine, out_weight, preferred_element_type=jnp.float32).astype(jnp.bfloat16)
        first_group = jnp.where(tp_index == 0, own, received).astype(jnp.float32)
        second_group = jnp.where(tp_index == 0, received, own).astype(jnp.float32)
        mixed_out = (first_group + second_group).astype(jnp.bfloat16)
    else:
        mixed_out = lax.psum_scatter(
            jnp.dot(attended, out_weight, preferred_element_type=jnp.float32).astype(jnp.bfloat16),
            "tp",
            scatter_dimension=0,
            tiled=True,
        )
    written_cache = jnp.einsum(
        "sct,xscr->xtr", routing, incoming, preferred_element_type=jnp.float32
    ).astype(jnp.bfloat16)
    written_cache = written_cache.reshape(2, slot_count, PAGE_ROWS, width)
    return (mixed_out, written_cache)


def solution(mesh):
    in_specs = (P("req", "tp"), P("req", "tp"), P("req", "tp"), P("tp", None), P(), P(), P())
    out_specs = (P(("req", "tp"), None), P(None, "req", None, "tp"))
    return jax.shard_map(local, mesh=mesh, in_specs=in_specs, out_specs=out_specs, check_vma=False)
```

```python
import functools

import jax
import jax.numpy as jnp
from jax import lax
from jax.experimental import pallas as pl
from jax.experimental.pallas import tpu as pltpu
from jax.sharding import PartitionSpec as P

HEAD_SIZE = 128
LONG_DEV = 512
SHORT_DEV = 128
PAGE_ROWS = 16
BLOCK_TOKENS = 640
LONG_CHUNK_ROWS = (320, 192)


NEGATIVE_FILL = -1e30
LOG2_E = 1.4426950408889634


def short_layout(offset, short_pages, short_fill):
    page_id = offset // PAGE_ROWS
    page_ends = jnp.cumsum(short_pages)
    page_starts = page_ends - short_pages
    limits = page_starts * PAGE_ROWS + (short_pages - 1) * PAGE_ROWS + short_fill
    owner_hit = page_ends[None, :] <= page_id[:, None]
    prompt = jnp.sum(owner_hit.astype(jnp.int32), axis=1)
    select = jnp.arange(short_pages.shape[0], dtype=jnp.int32)[None, :] == prompt[:, None]
    begin_at = jnp.sum(jnp.where(select, page_starts[None, :], 0), axis=1) * PAGE_ROWS
    limit_at = jnp.sum(jnp.where(select, limits[None, :], 0), axis=1)
    return (prompt, offset - begin_at, offset < limit_at)


def flash_kernel(b_ref, q_ref, k_ref, v_ref, *refs, group, tq, tk, chunk_rows, chunk_start, first, last):
    if first:
        m_out, l_out, acc_out = refs[-3:]
        m_in, l_in, acc_in = m_out, l_out, acc_out
    elif last:
        m_in, l_in, acc_in, o_ref = refs
        m_out, l_out, acc_out = m_in, l_in, acc_in
    else:
        m_in, l_in, acc_in, m_out, l_out, acc_out = refs
    i = pl.program_id(1)
    t = pl.program_id(2)
    b = b_ref[0]
    per_tile = tk // chunk_rows
    scale = HEAD_SIZE ** (-0.5)
    log2_scale = scale * LOG2_E

    @pl.when(t == 0)
    def _init():
        if first:
            m_out[...] = jnp.full(m_out.shape, NEGATIVE_FILL, jnp.float32)
            l_out[...] = jnp.zeros(l_out.shape, jnp.float32)
            acc_out[...] = jnp.zeros(acc_out.shape, jnp.float32)
        elif not last:
            m_out[...] = m_in[...]
            l_out[...] = l_in[...]
            acc_out[...] = acc_in[...]

    def step(masked):
        k = k_ref[...]
        v = v_ref[...]
        v_ext = jnp.concatenate([v, jnp.ones(v.shape, v.dtype)], axis=1)
        if masked:
            rows = i * tq + lax.broadcasted_iota(jnp.int32, (tq, tk), 0)
            cols = lax.broadcasted_iota(jnp.int32, (tq, tk), 1)
            src = t * per_tile + cols // chunk_rows
            key_pos = chunk_start + cols % chunk_rows
            allowed = (src < b) | ((src == b) & (key_pos <= rows))
        for g in range(group):
            qg = q_ref[:, g * HEAD_SIZE:(g + 1) * HEAD_SIZE]
            s = lax.dot_general(
                qg, k, (((1,), (1,)), ((), ())), preferred_element_type=jnp.float32
            )
            if masked:
                s = jnp.where(allowed, s, NEGATIVE_FILL)
            m_prev = m_out[g]
            m_new = jnp.maximum(m_prev, jnp.max(s, axis=1, keepdims=True) * scale)
            p = jnp.exp2(s * log2_scale - m_new[:, :1] * LOG2_E)
            alpha = jnp.exp2((m_prev - m_new) * LOG2_E)
            pv = lax.dot_general(
                p.astype(jnp.bfloat16), v_ext, (((1,), (0,)), ((), ())),
                preferred_element_type=jnp.float32,
            )
            l_out[g] = alpha * l_out[g] + pv[:, HEAD_SIZE:]
            acc_out[g] = acc_out[g] * alpha + pv[:, :HEAD_SIZE]
            m_out[g] = m_new

    @pl.when(t * per_tile + per_tile - 1 < b)
    def _full():
        step(False)

    @pl.when((t * per_tile + per_tile - 1 >= b) & (t * per_tile <= b))
    def _diag():
        step(True)

    if last:
        @pl.when(t == pl.num_programs(2) - 1)
        def _fin():
            for g in range(group):
                o_ref[:, g * HEAD_SIZE:(g + 1) * HEAD_SIZE] = (
                    acc_out[g] / l_out[g]
                ).astype(o_ref.dtype)


def long_attention_chunk(b_arr, q_long, kv_chunk, state, chunk_rows, chunk_start, first, last):
    rows, q_cols = q_long.shape
    kv_cols = kv_chunk.shape[1] // 2
    heads_kv = kv_cols // HEAD_SIZE
    group = q_cols // kv_cols
    total = kv_chunk.shape[0]
    tk = chunk_rows * max(1, LONG_DEV // chunk_rows)
    per_tile = tk // chunk_rows
    tq = LONG_DEV
    kernel = functools.partial(
        flash_kernel, group=group, tq=tq, tk=tk, chunk_rows=chunk_rows, chunk_start=chunk_start,
        first=first, last=last,
    )
    state_shape = jax.ShapeDtypeStruct((heads_kv, group, rows, HEAD_SIZE), jnp.float32)
    state_spec = pl.BlockSpec((None, group, tq, HEAD_SIZE), lambda h, i, t, b: (h, 0, i, 0))
    kv_spec_k = pl.BlockSpec((tk, HEAD_SIZE), lambda h, i, t, b: (jnp.minimum(t, b[0] // per_tile), h))
    kv_spec_v = pl.BlockSpec(
        (tk, HEAD_SIZE), lambda h, i, t, b: (jnp.minimum(t, b[0] // per_tile), heads_kv + h)
    )
    q_spec = pl.BlockSpec((tq, group * HEAD_SIZE), lambda h, i, t, b: (i, h))
    in_specs = [q_spec, kv_spec_k, kv_spec_v]
    operands = [b_arr, q_long, kv_chunk, kv_chunk]
    aliases = {}
    if not first:
        in_specs += [state_spec] * 3
        operands += list(state)
    if last:
        out_specs = q_spec
        out_shape = jax.ShapeDtypeStruct((rows, q_cols), jnp.bfloat16)
    else:
        out_specs = [state_spec] * 3
        out_shape = [state_shape] * 3
        if not first:
            aliases = {4: 0, 5: 1, 6: 2}
    grid_spec = pltpu.PrefetchScalarGridSpec(
        num_scalar_prefetch=1,
        grid=(heads_kv, rows // tq, total // tk),
        in_specs=in_specs,
        out_specs=out_specs,
    )
    return pl.pallas_call(
        kernel,
        grid_spec=grid_spec,
        out_shape=out_shape,
        input_output_aliases=aliases,
        compiler_params=pltpu.CompilerParams(
            dimension_semantics=("arbitrary", "arbitrary", "arbitrary")
        ),
    )(*operands)


def long_attention(my_index, q_long, k_long, v_long):
    b_arr = jnp.reshape(my_index, (1,)).astype(jnp.int32)
    state = None
    start = 0
    for c, rows in enumerate(LONG_CHUNK_ROWS):
        kv = jnp.concatenate(
            [k_long[start:start + rows], v_long[start:start + rows]], axis=1
        )
        kv = lax.all_gather(kv, "req", axis=0, tiled=True)
        state = long_attention_chunk(
            b_arr, q_long, kv, state, rows, start, c == 0, c == len(LONG_CHUNK_ROWS) - 1
        )
        start += rows
    return state


def short_attention(my_index, req_count, q_short, k_short, v_short, short_pages, short_fill):
    heads_kv = k_short.shape[1] // HEAD_SIZE
    group = q_short.shape[1] // k_short.shape[1]
    perm = [(s, s + 1) for s in range(req_count - 1)]
    k_prev = lax.ppermute(k_short, "req", perm)
    v_prev = lax.ppermute(v_short, "req", perm)
    own_off = my_index * SHORT_DEV + jnp.arange(SHORT_DEV, dtype=jnp.int32)
    key_off = (my_index - 1) * SHORT_DEV + jnp.arange(2 * SHORT_DEV, dtype=jnp.int32)
    q_seg, q_pos, q_live = short_layout(own_off, short_pages, short_fill)
    k_seg, k_pos, k_live = short_layout(key_off, short_pages, short_fill)
    k_live = k_live & (key_off >= 0)
    allowed = (q_seg[:, None] == k_seg[None, :]) & (k_pos[None, :] <= q_pos[:, None]) & k_live[None, :]
    keys = jnp.concatenate([k_prev, k_short]).reshape(2 * SHORT_DEV, heads_kv, HEAD_SIZE)
    values = jnp.concatenate([v_prev, v_short]).reshape(2 * SHORT_DEV, heads_kv, HEAD_SIZE)
    qs = q_short.reshape(SHORT_DEV, heads_kv, group, HEAD_SIZE)
    scores = jnp.einsum(
        "qhgd,khd->hgqk", qs, keys, preferred_element_type=jnp.float32
    ) * HEAD_SIZE ** (-0.5)
    scores = jnp.where(allowed[None, None], scores, NEGATIVE_FILL)
    row_max = jnp.max(scores, axis=-1, keepdims=True)
    weights = jnp.exp(scores - row_max)
    denom = jnp.sum(weights, axis=-1)
    weighted = jnp.einsum(
        "hgqk,khd->qhgd", weights.astype(jnp.bfloat16), values, preferred_element_type=jnp.float32
    )
    attended = weighted / jnp.transpose(denom, (2, 0, 1))[..., None]
    attended = jnp.where(q_live[:, None, None, None], attended, 0.0)
    return attended.reshape(SHORT_DEV, -1).astype(jnp.bfloat16)


def local(
    queries,
    rotated_key_rows,
    stream_value_rows,
    out_weight,
    short_pages,
    short_fill,
    stream_page_table,
):
    req_count = lax.axis_size("req")
    my_index = lax.axis_index("req")
    tok_rows = queries.shape[0]
    pages_per = tok_rows // PAGE_ROWS
    capacity = (pages_per + req_count - 1) // req_count
    slot_count = capacity * req_count
    width = rotated_key_rows.shape[1]
    own_off = my_index * SHORT_DEV + jnp.arange(SHORT_DEV, dtype=jnp.int32)
    short_live = short_layout(own_off, short_pages, short_fill)[2]
    own_live = jnp.concatenate([jnp.ones((LONG_DEV,), bool), short_live])
    kv_rows = jnp.stack([rotated_key_rows, stream_value_rows])
    kv_rows = jnp.where(own_live[None, :, None], kv_rows, jnp.zeros_like(kv_rows))
    kv_pages = kv_rows.reshape(2, pages_per, PAGE_ROWS * width)
    page_map = stream_page_table.reshape(req_count, pages_per)
    owners = page_map // slot_count
    earlier = (
        jnp.arange(pages_per, dtype=jnp.int32)[:, None]
        > jnp.arange(pages_per, dtype=jnp.int32)[None, :]
    )
    matching = owners[:, :, None] == owners[:, None, :]
    order_in = jnp.sum((matching & earlier[None]).astype(jnp.int32), axis=2)
    my_owner = owners[my_index]
    my_order = order_in[my_index]
    send_map = (
        (my_owner * capacity + my_order)[:, None]
        == jnp.arange(slot_count, dtype=jnp.int32)[None, :]
    ).astype(jnp.bfloat16)
    outgoing = jnp.einsum(
        "ks,xkr->xsr", send_map, kv_pages, preferred_element_type=jnp.float32
    ).astype(jnp.bfloat16)
    outgoing = outgoing.reshape(2, req_count, capacity, PAGE_ROWS * width)
    incoming = lax.all_to_all(outgoing, "req", split_axis=1, concat_axis=1, tiled=True)
    mine_mask = owners == my_index
    placing = mine_mask[:, :, None] & (
        order_in[:, :, None] == jnp.arange(capacity, dtype=jnp.int32)[None, None, :]
    )
    target = (page_map % slot_count)[:, :, None] == jnp.arange(slot_count, dtype=jnp.int32)[
        None, None, :
    ]
    routing = jnp.einsum(
        "skc,skt->sct",
        placing.astype(jnp.bfloat16),
        target.astype(jnp.bfloat16),
        preferred_element_type=jnp.float32,
    ).astype(jnp.bfloat16)
    incoming, queries = lax.optimization_barrier((incoming, queries))
    att_long = long_attention(
        my_index, queries[:LONG_DEV], rotated_key_rows[:LONG_DEV], stream_value_rows[:LONG_DEV]
    )
    att_short = short_attention(
        my_index,
        req_count,
        queries[LONG_DEV:],
        rotated_key_rows[LONG_DEV:],
        stream_value_rows[LONG_DEV:],
        short_pages,
        short_fill,
    )
    attended = jnp.concatenate([att_long, att_short])
    tp_count = lax.axis_size("tp")
    if tp_count == 2:
        tp_index = lax.axis_index("tp")
        half_rows = tok_rows // 2
        theirs = lax.dynamic_slice_in_dim(attended, (1 - tp_index) * half_rows, half_rows, 0)
        sent = jnp.dot(theirs, out_weight, preferred_element_type=jnp.float32).astype(jnp.bfloat16)
        received = lax.ppermute(sent, "tp", [(0, 1), (1, 0)])
        mine = lax.dynamic_slice_in_dim(attended, tp_index * half_rows, half_rows, 0)
        own = jnp.dot(mine, out_weight, preferred_element_type=jnp.float32).astype(jnp.bfloat16)
        first_group = jnp.where(tp_index == 0, own, received).astype(jnp.float32)
        second_group = jnp.where(tp_index == 0, received, own).astype(jnp.float32)
        mixed_out = (first_group + second_group).astype(jnp.bfloat16)
    else:
        mixed_out = lax.psum_scatter(
            jnp.dot(attended, out_weight, preferred_element_type=jnp.float32).astype(jnp.bfloat16),
            "tp",
            scatter_dimension=0,
            tiled=True,
        )
    written_cache = jnp.einsum(
        "sct,xscr->xtr", routing, incoming, preferred_element_type=jnp.float32
    ).astype(jnp.bfloat16)
    written_cache = written_cache.reshape(2, slot_count, PAGE_ROWS, width)
    return (mixed_out, written_cache)


def solution(mesh):
    in_specs = (P("req", "tp"), P("req", "tp"), P("req", "tp"), P("tp", None), P(), P(), P())
    out_specs = (P(("req", "tp"), None), P(None, "req", None, "tp"))
    return jax.shard_map(local, mesh=mesh, in_specs=in_specs, out_specs=out_specs, check_vma=False)
```

```python
import functools

import jax
import jax.numpy as jnp
from jax import lax
from jax.experimental import pallas as pl
from jax.experimental.pallas import tpu as pltpu
from jax.sharding import PartitionSpec as P

HEAD_SIZE = 128
LONG_DEV = 512
SHORT_DEV = 128
PAGE_ROWS = 16
BLOCK_TOKENS = 640
LONG_CHUNKS = 2


NEGATIVE_FILL = -1e30
LOG2_E = 1.4426950408889634


def short_layout(offset, short_pages, short_fill):
    page_id = offset // PAGE_ROWS
    page_ends = jnp.cumsum(short_pages)
    page_starts = page_ends - short_pages
    limits = page_starts * PAGE_ROWS + (short_pages - 1) * PAGE_ROWS + short_fill
    owner_hit = page_ends[None, :] <= page_id[:, None]
    prompt = jnp.sum(owner_hit.astype(jnp.int32), axis=1)
    select = jnp.arange(short_pages.shape[0], dtype=jnp.int32)[None, :] == prompt[:, None]
    begin_at = jnp.sum(jnp.where(select, page_starts[None, :], 0), axis=1) * PAGE_ROWS
    limit_at = jnp.sum(jnp.where(select, limits[None, :], 0), axis=1)
    return (prompt, offset - begin_at, offset < limit_at)


def flash_kernel(b_ref, q_ref, k_ref, v_ref, *refs, group, tq, tk, chunk_rows, chunk, first, last):
    if first:
        m_out, l_out, acc_out = refs[-3:]
        m_in, l_in, acc_in = m_out, l_out, acc_out
    elif last:
        m_in, l_in, acc_in, o_ref = refs
        m_out, l_out, acc_out = m_in, l_in, acc_in
    else:
        m_in, l_in, acc_in, m_out, l_out, acc_out = refs
    i = pl.program_id(1)
    t = pl.program_id(2)
    b = b_ref[0]
    per_tile = tk // chunk_rows
    scale = HEAD_SIZE ** (-0.5)
    log2_scale = scale * LOG2_E

    @pl.when(t == 0)
    def _init():
        if first:
            m_out[...] = jnp.full(m_out.shape, NEGATIVE_FILL, jnp.float32)
            l_out[...] = jnp.zeros(l_out.shape, jnp.float32)
            acc_out[...] = jnp.zeros(acc_out.shape, jnp.float32)
        elif not last:
            m_out[...] = m_in[...]
            l_out[...] = l_in[...]
            acc_out[...] = acc_in[...]

    def step(masked):
        k = k_ref[...]
        v = v_ref[...]
        v_ext = jnp.concatenate([v, jnp.ones(v.shape, v.dtype)], axis=1)
        if masked:
            rows = i * tq + lax.broadcasted_iota(jnp.int32, (tq, tk), 0)
            cols = lax.broadcasted_iota(jnp.int32, (tq, tk), 1)
            src = t * per_tile + cols // chunk_rows
            key_pos = chunk * chunk_rows + cols % chunk_rows
            allowed = (src < b) | ((src == b) & (key_pos <= rows))
        for g in range(group):
            qg = q_ref[:, g * HEAD_SIZE:(g + 1) * HEAD_SIZE]
            s = lax.dot_general(
                qg, k, (((1,), (1,)), ((), ())), preferred_element_type=jnp.float32
            )
            if masked:
                s = jnp.where(allowed, s, NEGATIVE_FILL)
            m_prev = m_out[g]
            m_new = jnp.maximum(m_prev, jnp.max(s, axis=1, keepdims=True) * scale)
            p = jnp.exp2(s * log2_scale - m_new[:, :1] * LOG2_E)
            alpha = jnp.exp2((m_prev - m_new) * LOG2_E)
            pv = lax.dot_general(
                p.astype(jnp.bfloat16), v_ext, (((1,), (0,)), ((), ())),
                preferred_element_type=jnp.float32,
            )
            l_out[g] = alpha * l_out[g] + pv[:, HEAD_SIZE:]
            acc_out[g] = acc_out[g] * alpha + pv[:, :HEAD_SIZE]
            m_out[g] = m_new

    @pl.when(t * per_tile + per_tile - 1 < b)
    def _full():
        step(False)

    @pl.when((t * per_tile + per_tile - 1 >= b) & (t * per_tile <= b))
    def _diag():
        step(True)

    if last:
        @pl.when(t == pl.num_programs(2) - 1)
        def _fin():
            for g in range(group):
                o_ref[:, g * HEAD_SIZE:(g + 1) * HEAD_SIZE] = (
                    acc_out[g] / l_out[g]
                ).astype(o_ref.dtype)


def long_attention_chunk(b_arr, q_long, kv_chunk, state, chunk, first, last):
    rows, q_cols = q_long.shape
    kv_cols = kv_chunk.shape[1] // 2
    heads_kv = kv_cols // HEAD_SIZE
    group = q_cols // kv_cols
    chunk_rows = LONG_DEV // LONG_CHUNKS
    total = kv_chunk.shape[0]
    tk = min(512, total)
    per_tile = tk // chunk_rows
    tq = LONG_DEV
    kernel = functools.partial(
        flash_kernel, group=group, tq=tq, tk=tk, chunk_rows=chunk_rows, chunk=chunk,
        first=first, last=last,
    )
    state_shape = jax.ShapeDtypeStruct((heads_kv, group, rows, HEAD_SIZE), jnp.float32)
    state_spec = pl.BlockSpec((None, group, tq, HEAD_SIZE), lambda h, i, t, b: (h, 0, i, 0))
    kv_spec_k = pl.BlockSpec((tk, HEAD_SIZE), lambda h, i, t, b: (jnp.minimum(t, b[0] // per_tile), h))
    kv_spec_v = pl.BlockSpec(
        (tk, HEAD_SIZE), lambda h, i, t, b: (jnp.minimum(t, b[0] // per_tile), heads_kv + h)
    )
    q_spec = pl.BlockSpec((tq, group * HEAD_SIZE), lambda h, i, t, b: (i, h))
    in_specs = [q_spec, kv_spec_k, kv_spec_v]
    operands = [b_arr, q_long, kv_chunk, kv_chunk]
    aliases = {}
    if not first:
        in_specs += [state_spec] * 3
        operands += list(state)
    if last:
        out_specs = q_spec
        out_shape = jax.ShapeDtypeStruct((rows, q_cols), jnp.bfloat16)
    else:
        out_specs = [state_spec] * 3
        out_shape = [state_shape] * 3
        if not first:
            aliases = {4: 0, 5: 1, 6: 2}
    grid_spec = pltpu.PrefetchScalarGridSpec(
        num_scalar_prefetch=1,
        grid=(heads_kv, rows // tq, total // tk),
        in_specs=in_specs,
        out_specs=out_specs,
    )
    return pl.pallas_call(
        kernel,
        grid_spec=grid_spec,
        out_shape=out_shape,
        input_output_aliases=aliases,
        compiler_params=pltpu.CompilerParams(
            dimension_semantics=("arbitrary", "arbitrary", "arbitrary")
        ),
    )(*operands)


def long_attention(my_index, q_long, k_long, v_long, outgoing):
    b_arr = jnp.reshape(my_index, (1,)).astype(jnp.int32)
    chunk_rows = LONG_DEV // LONG_CHUNKS
    state = None
    for c in range(LONG_CHUNKS):
        kv = jnp.concatenate(
            [k_long[c * chunk_rows:(c + 1) * chunk_rows], v_long[c * chunk_rows:(c + 1) * chunk_rows]],
            axis=1,
        )
        kv = lax.all_gather(kv, "req", axis=0, tiled=True)
        if c == LONG_CHUNKS - 1:
            outgoing, kv, state = lax.optimization_barrier((outgoing, kv, state))
            incoming = lax.all_to_all(outgoing, "req", split_axis=1, concat_axis=1, tiled=True)
        state = long_attention_chunk(
            b_arr, q_long, kv, state, c, c == 0, c == LONG_CHUNKS - 1
        )
    return state, incoming


def short_attention(my_index, req_count, q_short, k_short, v_short, short_pages, short_fill):
    heads_kv = k_short.shape[1] // HEAD_SIZE
    group = q_short.shape[1] // k_short.shape[1]
    perm = [(s, s + 1) for s in range(req_count - 1)]
    k_prev = lax.ppermute(k_short, "req", perm)
    v_prev = lax.ppermute(v_short, "req", perm)
    own_off = my_index * SHORT_DEV + jnp.arange(SHORT_DEV, dtype=jnp.int32)
    key_off = (my_index - 1) * SHORT_DEV + jnp.arange(2 * SHORT_DEV, dtype=jnp.int32)
    q_seg, q_pos, q_live = short_layout(own_off, short_pages, short_fill)
    k_seg, k_pos, k_live = short_layout(key_off, short_pages, short_fill)
    k_live = k_live & (key_off >= 0)
    allowed = (q_seg[:, None] == k_seg[None, :]) & (k_pos[None, :] <= q_pos[:, None]) & k_live[None, :]
    keys = jnp.concatenate([k_prev, k_short]).reshape(2 * SHORT_DEV, heads_kv, HEAD_SIZE)
    values = jnp.concatenate([v_prev, v_short]).reshape(2 * SHORT_DEV, heads_kv, HEAD_SIZE)
    qs = q_short.reshape(SHORT_DEV, heads_kv, group, HEAD_SIZE)
    scores = jnp.einsum(
        "qhgd,khd->hgqk", qs, keys, preferred_element_type=jnp.float32
    ) * HEAD_SIZE ** (-0.5)
    scores = jnp.where(allowed[None, None], scores, NEGATIVE_FILL)
    row_max = jnp.max(scores, axis=-1, keepdims=True)
    weights = jnp.exp(scores - row_max)
    denom = jnp.sum(weights, axis=-1)
    weighted = jnp.einsum(
        "hgqk,khd->qhgd", weights.astype(jnp.bfloat16), values, preferred_element_type=jnp.float32
    )
    attended = weighted / jnp.transpose(denom, (2, 0, 1))[..., None]
    attended = jnp.where(q_live[:, None, None, None], attended, 0.0)
    return attended.reshape(SHORT_DEV, -1).astype(jnp.bfloat16)


def local(
    queries,
    rotated_key_rows,
    stream_value_rows,
    out_weight,
    short_pages,
    short_fill,
    stream_page_table,
):
    req_count = lax.axis_size("req")
    my_index = lax.axis_index("req")
    tok_rows = queries.shape[0]
    pages_per = tok_rows // PAGE_ROWS
    capacity = (pages_per + req_count - 1) // req_count
    slot_count = capacity * req_count
    width = rotated_key_rows.shape[1]
    own_off = my_index * SHORT_DEV + jnp.arange(SHORT_DEV, dtype=jnp.int32)
    short_live = short_layout(own_off, short_pages, short_fill)[2]
    own_live = jnp.concatenate([jnp.ones((LONG_DEV,), bool), short_live])
    kv_rows = jnp.stack([rotated_key_rows, stream_value_rows])
    kv_rows = jnp.where(own_live[None, :, None], kv_rows, jnp.zeros_like(kv_rows))
    kv_pages = kv_rows.reshape(2, pages_per, PAGE_ROWS * width)
    page_map = stream_page_table.reshape(req_count, pages_per)
    owners = page_map // slot_count
    earlier = (
        jnp.arange(pages_per, dtype=jnp.int32)[:, None]
        > jnp.arange(pages_per, dtype=jnp.int32)[None, :]
    )
    matching = owners[:, :, None] == owners[:, None, :]
    order_in = jnp.sum((matching & earlier[None]).astype(jnp.int32), axis=2)
    my_owner = owners[my_index]
    my_order = order_in[my_index]
    send_map = (
        (my_owner * capacity + my_order)[:, None]
        == jnp.arange(slot_count, dtype=jnp.int32)[None, :]
    ).astype(jnp.bfloat16)
    outgoing = jnp.einsum(
        "ks,xkr->xsr", send_map, kv_pages, preferred_element_type=jnp.float32
    ).astype(jnp.bfloat16)
    outgoing = outgoing.reshape(2, req_count, capacity, PAGE_ROWS * width)
    mine_mask = owners == my_index
    placing = mine_mask[:, :, None] & (
        order_in[:, :, None] == jnp.arange(capacity, dtype=jnp.int32)[None, None, :]
    )
    target = (page_map % slot_count)[:, :, None] == jnp.arange(slot_count, dtype=jnp.int32)[
        None, None, :
    ]
    routing = jnp.einsum(
        "skc,skt->sct",
        placing.astype(jnp.bfloat16),
        target.astype(jnp.bfloat16),
        preferred_element_type=jnp.float32,
    ).astype(jnp.bfloat16)
    att_long, incoming = long_attention(
        my_index, queries[:LONG_DEV], rotated_key_rows[:LONG_DEV], stream_value_rows[:LONG_DEV],
        outgoing,
    )
    att_short = short_attention(
        my_index,
        req_count,
        queries[LONG_DEV:],
        rotated_key_rows[LONG_DEV:],
        stream_value_rows[LONG_DEV:],
        short_pages,
        short_fill,
    )
    attended = jnp.concatenate([att_long, att_short])
    tp_count = lax.axis_size("tp")
    if tp_count == 2:
        tp_index = lax.axis_index("tp")
        half_rows = tok_rows // 2
        theirs = lax.dynamic_slice_in_dim(attended, (1 - tp_index) * half_rows, half_rows, 0)
        sent = jnp.dot(theirs, out_weight, preferred_element_type=jnp.float32).astype(jnp.bfloat16)
        received = lax.ppermute(sent, "tp", [(0, 1), (1, 0)])
        mine = lax.dynamic_slice_in_dim(attended, tp_index * half_rows, half_rows, 0)
        own = jnp.dot(mine, out_weight, preferred_element_type=jnp.float32).astype(jnp.bfloat16)
        first_group = jnp.where(tp_index == 0, own, received).astype(jnp.float32)
        second_group = jnp.where(tp_index == 0, received, own).astype(jnp.float32)
        mixed_out = (first_group + second_group).astype(jnp.bfloat16)
    else:
        mixed_out = lax.psum_scatter(
            jnp.dot(attended, out_weight, preferred_element_type=jnp.float32).astype(jnp.bfloat16),
            "tp",
            scatter_dimension=0,
            tiled=True,
        )
    written_cache = jnp.einsum(
        "sct,xscr->xtr", routing, incoming, preferred_element_type=jnp.float32
    ).astype(jnp.bfloat16)
    written_cache = written_cache.reshape(2, slot_count, PAGE_ROWS, width)
    return (mixed_out, written_cache)


def solution(mesh):
    in_specs = (P("req", "tp"), P("req", "tp"), P("req", "tp"), P("tp", None), P(), P(), P())
    out_specs = (P(("req", "tp"), None), P(None, "req", None, "tp"))
    return jax.shard_map(local, mesh=mesh, in_specs=in_specs, out_specs=out_specs, check_vma=False)
```

```python
import functools

import jax
import jax.numpy as jnp
from jax import lax
from jax.experimental import pallas as pl
from jax.experimental.pallas import tpu as pltpu
from jax.sharding import PartitionSpec as P

HEAD_SIZE = 128
LONG_DEV = 512
SHORT_DEV = 128
PAGE_ROWS = 16
BLOCK_TOKENS = 640
LONG_CHUNKS = 2


NEGATIVE_FILL = -1e30
LOG2_E = 1.4426950408889634


def short_layout(offset, short_pages, short_fill):
    page_id = offset // PAGE_ROWS
    page_ends = jnp.cumsum(short_pages)
    page_starts = page_ends - short_pages
    limits = page_starts * PAGE_ROWS + (short_pages - 1) * PAGE_ROWS + short_fill
    owner_hit = page_ends[None, :] <= page_id[:, None]
    prompt = jnp.sum(owner_hit.astype(jnp.int32), axis=1)
    select = jnp.arange(short_pages.shape[0], dtype=jnp.int32)[None, :] == prompt[:, None]
    begin_at = jnp.sum(jnp.where(select, page_starts[None, :], 0), axis=1) * PAGE_ROWS
    limit_at = jnp.sum(jnp.where(select, limits[None, :], 0), axis=1)
    return (prompt, offset - begin_at, offset < limit_at)


def flash_kernel(b_ref, q_ref, k_ref, v_ref, *refs, group, tq, tk, chunk_rows, chunk, first, last):
    if first:
        m_out, l_out, acc_out = refs[-3:]
        m_in, l_in, acc_in = m_out, l_out, acc_out
    elif last:
        m_in, l_in, acc_in, o_ref = refs
        m_out, l_out, acc_out = m_in, l_in, acc_in
    else:
        m_in, l_in, acc_in, m_out, l_out, acc_out = refs
    i = pl.program_id(1)
    t = pl.program_id(2)
    b = b_ref[0]
    per_tile = tk // chunk_rows
    scale = HEAD_SIZE ** (-0.5)
    log2_scale = scale * LOG2_E

    @pl.when(t == 0)
    def _init():
        if first:
            m_out[...] = jnp.full(m_out.shape, NEGATIVE_FILL, jnp.float32)
            l_out[...] = jnp.zeros(l_out.shape, jnp.float32)
            acc_out[...] = jnp.zeros(acc_out.shape, jnp.float32)
        elif not last:
            m_out[...] = m_in[...]
            l_out[...] = l_in[...]
            acc_out[...] = acc_in[...]

    def step(masked):
        k = k_ref[...]
        v = v_ref[...]
        v_ext = jnp.concatenate([v, jnp.ones(v.shape, v.dtype)], axis=1)
        s = lax.dot_general(
            q_ref[...], k, (((1,), (1,)), ((), ())), preferred_element_type=jnp.float32
        )
        if masked:
            shape = (group * tq, k.shape[0])
            rows = i * tq + lax.broadcasted_iota(jnp.int32, shape, 0) % tq
            cols = lax.broadcasted_iota(jnp.int32, shape, 1)
            src = t * per_tile + cols // chunk_rows
            key_pos = chunk * chunk_rows + cols % chunk_rows
            allowed = (src < b) | ((src == b) & (key_pos <= rows))
            s = jnp.where(allowed, s, NEGATIVE_FILL)
        m_prev = m_out[...].reshape(group * tq, HEAD_SIZE)
        m_new = jnp.maximum(m_prev, jnp.max(s, axis=1, keepdims=True) * scale)
        p = jnp.exp2(s * log2_scale - m_new[:, :1] * LOG2_E)
        alpha = jnp.exp2((m_prev - m_new) * LOG2_E)
        pv = lax.dot_general(
            p.astype(jnp.bfloat16), v_ext, (((1,), (0,)), ((), ())),
            preferred_element_type=jnp.float32,
        )
        l_new = alpha * l_out[...].reshape(group * tq, HEAD_SIZE) + pv[:, HEAD_SIZE:]
        acc_new = acc_out[...].reshape(group * tq, HEAD_SIZE) * alpha + pv[:, :HEAD_SIZE]
        l_out[...] = l_new.reshape(group, tq, HEAD_SIZE)
        acc_out[...] = acc_new.reshape(group, tq, HEAD_SIZE)
        m_out[...] = m_new.reshape(group, tq, HEAD_SIZE)

    @pl.when(t * per_tile + per_tile - 1 < b)
    def _full():
        step(False)

    @pl.when((t * per_tile + per_tile - 1 >= b) & (t * per_tile <= b))
    def _diag():
        step(True)

    if last:
        @pl.when(t == pl.num_programs(2) - 1)
        def _fin():
            for g in range(group):
                o_ref[:, g * HEAD_SIZE:(g + 1) * HEAD_SIZE] = (
                    acc_out[g] / l_out[g]
                ).astype(o_ref.dtype)


def long_attention_chunk(b_arr, q_long, kv_chunk, state, chunk, first, last):
    rows, q_cols = q_long.shape
    kv_cols = kv_chunk.shape[1] // 2
    heads_kv = kv_cols // HEAD_SIZE
    group = q_cols // kv_cols
    chunk_rows = LONG_DEV // LONG_CHUNKS
    total = kv_chunk.shape[0]
    tk = min(512, total)
    per_tile = tk // chunk_rows
    tq = LONG_DEV
    kernel = functools.partial(
        flash_kernel, group=group, tq=tq, tk=tk, chunk_rows=chunk_rows, chunk=chunk,
        first=first, last=last,
    )
    state_shape = jax.ShapeDtypeStruct((heads_kv, group, rows, HEAD_SIZE), jnp.float32)
    state_spec = pl.BlockSpec((None, group, tq, HEAD_SIZE), lambda h, i, t, b: (h, 0, i, 0))
    kv_spec_k = pl.BlockSpec((tk, HEAD_SIZE), lambda h, i, t, b: (jnp.minimum(t, b[0] // per_tile), h))
    kv_spec_v = pl.BlockSpec(
        (tk, HEAD_SIZE), lambda h, i, t, b: (jnp.minimum(t, b[0] // per_tile), heads_kv + h)
    )
    q_spec = pl.BlockSpec((tq, group * HEAD_SIZE), lambda h, i, t, b: (i, h))
    stacked_spec = pl.BlockSpec((None, group * tq, HEAD_SIZE), lambda h, i, t, b: (h, i, 0))
    q_stacked = q_long.reshape(rows, heads_kv, group, HEAD_SIZE).transpose(1, 2, 0, 3).reshape(
        heads_kv, group * rows, HEAD_SIZE
    )
    in_specs = [stacked_spec, kv_spec_k, kv_spec_v]
    operands = [b_arr, q_stacked, kv_chunk, kv_chunk]
    aliases = {}
    if not first:
        in_specs += [state_spec] * 3
        operands += list(state)
    if last:
        out_specs = q_spec
        out_shape = jax.ShapeDtypeStruct((rows, q_cols), jnp.bfloat16)
    else:
        out_specs = [state_spec] * 3
        out_shape = [state_shape] * 3
        if not first:
            aliases = {4: 0, 5: 1, 6: 2}
    grid_spec = pltpu.PrefetchScalarGridSpec(
        num_scalar_prefetch=1,
        grid=(heads_kv, rows // tq, total // tk),
        in_specs=in_specs,
        out_specs=out_specs,
    )
    return pl.pallas_call(
        kernel,
        grid_spec=grid_spec,
        out_shape=out_shape,
        input_output_aliases=aliases,
        compiler_params=pltpu.CompilerParams(
            dimension_semantics=("arbitrary", "arbitrary", "arbitrary")
        ),
    )(*operands)


def long_attention(my_index, q_long, k_long, v_long):
    b_arr = jnp.reshape(my_index, (1,)).astype(jnp.int32)
    chunk_rows = LONG_DEV // LONG_CHUNKS
    state = None
    for c in range(LONG_CHUNKS):
        kv = jnp.concatenate(
            [k_long[c * chunk_rows:(c + 1) * chunk_rows], v_long[c * chunk_rows:(c + 1) * chunk_rows]],
            axis=1,
        )
        kv = lax.all_gather(kv, "req", axis=0, tiled=True)
        state = long_attention_chunk(
            b_arr, q_long, kv, state, c, c == 0, c == LONG_CHUNKS - 1
        )
    return state


def short_attention(my_index, req_count, q_short, k_short, v_short, short_pages, short_fill):
    heads_kv = k_short.shape[1] // HEAD_SIZE
    group = q_short.shape[1] // k_short.shape[1]
    perm = [(s, s + 1) for s in range(req_count - 1)]
    k_prev = lax.ppermute(k_short, "req", perm)
    v_prev = lax.ppermute(v_short, "req", perm)
    own_off = my_index * SHORT_DEV + jnp.arange(SHORT_DEV, dtype=jnp.int32)
    key_off = (my_index - 1) * SHORT_DEV + jnp.arange(2 * SHORT_DEV, dtype=jnp.int32)
    q_seg, q_pos, q_live = short_layout(own_off, short_pages, short_fill)
    k_seg, k_pos, k_live = short_layout(key_off, short_pages, short_fill)
    k_live = k_live & (key_off >= 0)
    allowed = (q_seg[:, None] == k_seg[None, :]) & (k_pos[None, :] <= q_pos[:, None]) & k_live[None, :]
    keys = jnp.concatenate([k_prev, k_short]).reshape(2 * SHORT_DEV, heads_kv, HEAD_SIZE)
    values = jnp.concatenate([v_prev, v_short]).reshape(2 * SHORT_DEV, heads_kv, HEAD_SIZE)
    qs = q_short.reshape(SHORT_DEV, heads_kv, group, HEAD_SIZE)
    scores = jnp.einsum(
        "qhgd,khd->hgqk", qs, keys, preferred_element_type=jnp.float32
    ) * HEAD_SIZE ** (-0.5)
    scores = jnp.where(allowed[None, None], scores, NEGATIVE_FILL)
    row_max = jnp.max(scores, axis=-1, keepdims=True)
    weights = jnp.exp(scores - row_max)
    denom = jnp.sum(weights, axis=-1)
    weighted = jnp.einsum(
        "hgqk,khd->qhgd", weights.astype(jnp.bfloat16), values, preferred_element_type=jnp.float32
    )
    attended = weighted / jnp.transpose(denom, (2, 0, 1))[..., None]
    attended = jnp.where(q_live[:, None, None, None], attended, 0.0)
    return attended.reshape(SHORT_DEV, -1).astype(jnp.bfloat16)


def local(
    queries,
    rotated_key_rows,
    stream_value_rows,
    out_weight,
    short_pages,
    short_fill,
    stream_page_table,
):
    req_count = lax.axis_size("req")
    my_index = lax.axis_index("req")
    tok_rows = queries.shape[0]
    pages_per = tok_rows // PAGE_ROWS
    capacity = (pages_per + req_count - 1) // req_count
    slot_count = capacity * req_count
    width = rotated_key_rows.shape[1]
    own_off = my_index * SHORT_DEV + jnp.arange(SHORT_DEV, dtype=jnp.int32)
    short_live = short_layout(own_off, short_pages, short_fill)[2]
    own_live = jnp.concatenate([jnp.ones((LONG_DEV,), bool), short_live])
    kv_rows = jnp.stack([rotated_key_rows, stream_value_rows])
    kv_rows = jnp.where(own_live[None, :, None], kv_rows, jnp.zeros_like(kv_rows))
    kv_pages = kv_rows.reshape(2, pages_per, PAGE_ROWS * width)
    page_map = stream_page_table.reshape(req_count, pages_per)
    owners = page_map // slot_count
    earlier = (
        jnp.arange(pages_per, dtype=jnp.int32)[:, None]
        > jnp.arange(pages_per, dtype=jnp.int32)[None, :]
    )
    matching = owners[:, :, None] == owners[:, None, :]
    order_in = jnp.sum((matching & earlier[None]).astype(jnp.int32), axis=2)
    my_owner = owners[my_index]
    my_order = order_in[my_index]
    send_map = (
        (my_owner * capacity + my_order)[:, None]
        == jnp.arange(slot_count, dtype=jnp.int32)[None, :]
    ).astype(jnp.bfloat16)
    outgoing = jnp.einsum(
        "ks,xkr->xsr", send_map, kv_pages, preferred_element_type=jnp.float32
    ).astype(jnp.bfloat16)
    outgoing = outgoing.reshape(2, req_count, capacity, PAGE_ROWS * width)
    incoming = lax.all_to_all(outgoing, "req", split_axis=1, concat_axis=1, tiled=True)
    mine_mask = owners == my_index
    placing = mine_mask[:, :, None] & (
        order_in[:, :, None] == jnp.arange(capacity, dtype=jnp.int32)[None, None, :]
    )
    target = (page_map % slot_count)[:, :, None] == jnp.arange(slot_count, dtype=jnp.int32)[
        None, None, :
    ]
    routing = jnp.einsum(
        "skc,skt->sct",
        placing.astype(jnp.bfloat16),
        target.astype(jnp.bfloat16),
        preferred_element_type=jnp.float32,
    ).astype(jnp.bfloat16)
    incoming, queries = lax.optimization_barrier((incoming, queries))
    att_long = long_attention(
        my_index, queries[:LONG_DEV], rotated_key_rows[:LONG_DEV], stream_value_rows[:LONG_DEV]
    )
    att_short = short_attention(
        my_index,
        req_count,
        queries[LONG_DEV:],
        rotated_key_rows[LONG_DEV:],
        stream_value_rows[LONG_DEV:],
        short_pages,
        short_fill,
    )
    attended = jnp.concatenate([att_long, att_short])
    tp_count = lax.axis_size("tp")
    if tp_count == 2:
        tp_index = lax.axis_index("tp")
        half_rows = tok_rows // 2
        theirs = lax.dynamic_slice_in_dim(attended, (1 - tp_index) * half_rows, half_rows, 0)
        sent = jnp.dot(theirs, out_weight, preferred_element_type=jnp.float32).astype(jnp.bfloat16)
        received = lax.ppermute(sent, "tp", [(0, 1), (1, 0)])
        mine = lax.dynamic_slice_in_dim(attended, tp_index * half_rows, half_rows, 0)
        own = jnp.dot(mine, out_weight, preferred_element_type=jnp.float32).astype(jnp.bfloat16)
        first_group = jnp.where(tp_index == 0, own, received).astype(jnp.float32)
        second_group = jnp.where(tp_index == 0, received, own).astype(jnp.float32)
        mixed_out = (first_group + second_group).astype(jnp.bfloat16)
    else:
        mixed_out = lax.psum_scatter(
            jnp.dot(attended, out_weight, preferred_element_type=jnp.float32).astype(jnp.bfloat16),
            "tp",
            scatter_dimension=0,
            tiled=True,
        )
    written_cache = jnp.einsum(
        "sct,xscr->xtr", routing, incoming, preferred_element_type=jnp.float32
    ).astype(jnp.bfloat16)
    written_cache = written_cache.reshape(2, slot_count, PAGE_ROWS, width)
    return (mixed_out, written_cache)


def solution(mesh):
    in_specs = (P("req", "tp"), P("req", "tp"), P("req", "tp"), P("tp", None), P(), P(), P())
    out_specs = (P(("req", "tp"), None), P(None, "req", None, "tp"))
    return jax.shard_map(local, mesh=mesh, in_specs=in_specs, out_specs=out_specs, check_vma=False)
```

```python
import functools

import jax
import jax.numpy as jnp
from jax import lax
from jax.experimental import pallas as pl
from jax.experimental.pallas import tpu as pltpu
from jax.sharding import PartitionSpec as P

HEAD_SIZE = 128
LONG_DEV = 512
SHORT_DEV = 128
PAGE_ROWS = 16
BLOCK_TOKENS = 640
LONG_CHUNKS = 2


NEGATIVE_FILL = -1e30
LOG2_E = 1.4426950408889634


def short_layout(offset, short_pages, short_fill):
    page_id = offset // PAGE_ROWS
    page_ends = jnp.cumsum(short_pages)
    page_starts = page_ends - short_pages
    limits = page_starts * PAGE_ROWS + (short_pages - 1) * PAGE_ROWS + short_fill
    owner_hit = page_ends[None, :] <= page_id[:, None]
    prompt = jnp.sum(owner_hit.astype(jnp.int32), axis=1)
    select = jnp.arange(short_pages.shape[0], dtype=jnp.int32)[None, :] == prompt[:, None]
    begin_at = jnp.sum(jnp.where(select, page_starts[None, :], 0), axis=1) * PAGE_ROWS
    limit_at = jnp.sum(jnp.where(select, limits[None, :], 0), axis=1)
    return (prompt, offset - begin_at, offset < limit_at)


def flash_kernel(b_ref, q_ref, k_ref, v_ref, *refs, group, tq, tk, chunk_rows, chunk, first, last):
    if first:
        m_out, l_out, acc_out = refs[-3:]
        m_in, l_in, acc_in = m_out, l_out, acc_out
    elif last:
        m_in, l_in, acc_in, o_ref = refs
        m_out, l_out, acc_out = m_in, l_in, acc_in
    else:
        m_in, l_in, acc_in, m_out, l_out, acc_out = refs
    i = pl.program_id(1)
    t = pl.program_id(2)
    b = b_ref[0]
    per_tile = tk // chunk_rows
    scale = HEAD_SIZE ** (-0.5)
    log2_scale = scale * LOG2_E

    @pl.when(t == 0)
    def _init():
        if first:
            m_out[...] = jnp.full(m_out.shape, NEGATIVE_FILL, jnp.float32)
            l_out[...] = jnp.zeros(l_out.shape, jnp.float32)
            acc_out[...] = jnp.zeros(acc_out.shape, jnp.float32)
        elif not last:
            m_out[...] = m_in[...]
            l_out[...] = l_in[...]
            acc_out[...] = acc_in[...]

    def step(masked):
        k = k_ref[...]
        v = v_ref[...]
        v_ext = jnp.concatenate([v, jnp.ones(v.shape, v.dtype)], axis=1)
        if masked:
            rows = i * tq + lax.broadcasted_iota(jnp.int32, (tq, tk), 0)
            cols = lax.broadcasted_iota(jnp.int32, (tq, tk), 1)
            src = t * per_tile + cols // chunk_rows
            key_pos = chunk * chunk_rows + cols % chunk_rows
            allowed = (src < b) | ((src == b) & (key_pos <= rows))
        for g in range(group):
            qg = q_ref[:, g * HEAD_SIZE:(g + 1) * HEAD_SIZE]
            s = lax.dot_general(
                qg, k, (((1,), (1,)), ((), ())), preferred_element_type=jnp.float32
            )
            if masked:
                s = jnp.where(allowed, s, NEGATIVE_FILL)
            m_prev = m_out[g]
            m_new = jnp.maximum(m_prev, jnp.max(s, axis=1, keepdims=True) * scale)
            p = jnp.exp2(s * log2_scale - m_new[:, :1] * LOG2_E)
            alpha = jnp.exp2((m_prev - m_new) * LOG2_E)
            pv = lax.dot_general(
                p.astype(jnp.bfloat16), v_ext, (((1,), (0,)), ((), ())),
                preferred_element_type=jnp.float32,
            )
            l_out[g] = alpha * l_out[g] + pv[:, HEAD_SIZE:]
            acc_out[g] = acc_out[g] * alpha + pv[:, :HEAD_SIZE]
            m_out[g] = m_new

    @pl.when(t * per_tile + per_tile - 1 < b)
    def _full():
        step(False)

    @pl.when((t * per_tile + per_tile - 1 >= b) & (t * per_tile <= b))
    def _diag():
        step(True)

    if last:
        @pl.when(t == pl.num_programs(2) - 1)
        def _fin():
            for g in range(group):
                o_ref[:, g * HEAD_SIZE:(g + 1) * HEAD_SIZE] = (
                    acc_out[g] / l_out[g]
                ).astype(o_ref.dtype)


def long_attention_chunk(b_arr, q_long, kv_chunk, state, chunk, first, last):
    rows, q_cols = q_long.shape
    kv_cols = kv_chunk.shape[1] // 2
    heads_kv = kv_cols // HEAD_SIZE
    group = q_cols // kv_cols
    chunk_rows = LONG_DEV // LONG_CHUNKS
    total = kv_chunk.shape[0]
    tk = min(512, total)
    per_tile = tk // chunk_rows
    tq = LONG_DEV // 2
    kernel = functools.partial(
        flash_kernel, group=group, tq=tq, tk=tk, chunk_rows=chunk_rows, chunk=chunk,
        first=first, last=last,
    )
    state_shape = jax.ShapeDtypeStruct((heads_kv, group, rows, HEAD_SIZE), jnp.float32)
    state_spec = pl.BlockSpec((None, group, tq, HEAD_SIZE), lambda h, i, t, b: (h, 0, i, 0))
    kv_spec_k = pl.BlockSpec((tk, HEAD_SIZE), lambda h, i, t, b: (jnp.minimum(t, b[0] // per_tile), h))
    kv_spec_v = pl.BlockSpec(
        (tk, HEAD_SIZE), lambda h, i, t, b: (jnp.minimum(t, b[0] // per_tile), heads_kv + h)
    )
    q_spec = pl.BlockSpec((tq, group * HEAD_SIZE), lambda h, i, t, b: (i, h))
    in_specs = [q_spec, kv_spec_k, kv_spec_v]
    operands = [b_arr, q_long, kv_chunk, kv_chunk]
    aliases = {}
    if not first:
        in_specs += [state_spec] * 3
        operands += list(state)
    if last:
        out_specs = q_spec
        out_shape = jax.ShapeDtypeStruct((rows, q_cols), jnp.bfloat16)
    else:
        out_specs = [state_spec] * 3
        out_shape = [state_shape] * 3
        if not first:
            aliases = {4: 0, 5: 1, 6: 2}
    grid_spec = pltpu.PrefetchScalarGridSpec(
        num_scalar_prefetch=1,
        grid=(heads_kv, rows // tq, total // tk),
        in_specs=in_specs,
        out_specs=out_specs,
    )
    return pl.pallas_call(
        kernel,
        grid_spec=grid_spec,
        out_shape=out_shape,
        input_output_aliases=aliases,
        compiler_params=pltpu.CompilerParams(
            dimension_semantics=("arbitrary", "arbitrary", "arbitrary")
        ),
    )(*operands)


def long_attention(my_index, q_long, k_long, v_long):
    b_arr = jnp.reshape(my_index, (1,)).astype(jnp.int32)
    chunk_rows = LONG_DEV // LONG_CHUNKS
    state = None
    for c in range(LONG_CHUNKS):
        kv = jnp.concatenate(
            [k_long[c * chunk_rows:(c + 1) * chunk_rows], v_long[c * chunk_rows:(c + 1) * chunk_rows]],
            axis=1,
        )
        kv = lax.all_gather(kv, "req", axis=0, tiled=True)
        state = long_attention_chunk(
            b_arr, q_long, kv, state, c, c == 0, c == LONG_CHUNKS - 1
        )
    return state


def short_attention(my_index, req_count, q_short, k_short, v_short, short_pages, short_fill):
    heads_kv = k_short.shape[1] // HEAD_SIZE
    group = q_short.shape[1] // k_short.shape[1]
    perm = [(s, s + 1) for s in range(req_count - 1)]
    k_prev = lax.ppermute(k_short, "req", perm)
    v_prev = lax.ppermute(v_short, "req", perm)
    own_off = my_index * SHORT_DEV + jnp.arange(SHORT_DEV, dtype=jnp.int32)
    key_off = (my_index - 1) * SHORT_DEV + jnp.arange(2 * SHORT_DEV, dtype=jnp.int32)
    q_seg, q_pos, q_live = short_layout(own_off, short_pages, short_fill)
    k_seg, k_pos, k_live = short_layout(key_off, short_pages, short_fill)
    k_live = k_live & (key_off >= 0)
    allowed = (q_seg[:, None] == k_seg[None, :]) & (k_pos[None, :] <= q_pos[:, None]) & k_live[None, :]
    keys = jnp.concatenate([k_prev, k_short]).reshape(2 * SHORT_DEV, heads_kv, HEAD_SIZE)
    values = jnp.concatenate([v_prev, v_short]).reshape(2 * SHORT_DEV, heads_kv, HEAD_SIZE)
    qs = q_short.reshape(SHORT_DEV, heads_kv, group, HEAD_SIZE)
    scores = jnp.einsum(
        "qhgd,khd->hgqk", qs, keys, preferred_element_type=jnp.float32
    ) * HEAD_SIZE ** (-0.5)
    scores = jnp.where(allowed[None, None], scores, NEGATIVE_FILL)
    row_max = jnp.max(scores, axis=-1, keepdims=True)
    weights = jnp.exp(scores - row_max)
    denom = jnp.sum(weights, axis=-1)
    weighted = jnp.einsum(
        "hgqk,khd->qhgd", weights.astype(jnp.bfloat16), values, preferred_element_type=jnp.float32
    )
    attended = weighted / jnp.transpose(denom, (2, 0, 1))[..., None]
    attended = jnp.where(q_live[:, None, None, None], attended, 0.0)
    return attended.reshape(SHORT_DEV, -1).astype(jnp.bfloat16)


def local(
    queries,
    rotated_key_rows,
    stream_value_rows,
    out_weight,
    short_pages,
    short_fill,
    stream_page_table,
):
    req_count = lax.axis_size("req")
    my_index = lax.axis_index("req")
    tok_rows = queries.shape[0]
    pages_per = tok_rows // PAGE_ROWS
    capacity = (pages_per + req_count - 1) // req_count
    slot_count = capacity * req_count
    width = rotated_key_rows.shape[1]
    own_off = my_index * SHORT_DEV + jnp.arange(SHORT_DEV, dtype=jnp.int32)
    short_live = short_layout(own_off, short_pages, short_fill)[2]
    own_live = jnp.concatenate([jnp.ones((LONG_DEV,), bool), short_live])
    kv_rows = jnp.stack([rotated_key_rows, stream_value_rows])
    kv_rows = jnp.where(own_live[None, :, None], kv_rows, jnp.zeros_like(kv_rows))
    kv_pages = kv_rows.reshape(2, pages_per, PAGE_ROWS * width)
    page_map = stream_page_table.reshape(req_count, pages_per)
    owners = page_map // slot_count
    earlier = (
        jnp.arange(pages_per, dtype=jnp.int32)[:, None]
        > jnp.arange(pages_per, dtype=jnp.int32)[None, :]
    )
    matching = owners[:, :, None] == owners[:, None, :]
    order_in = jnp.sum((matching & earlier[None]).astype(jnp.int32), axis=2)
    my_owner = owners[my_index]
    my_order = order_in[my_index]
    send_map = (
        (my_owner * capacity + my_order)[:, None]
        == jnp.arange(slot_count, dtype=jnp.int32)[None, :]
    ).astype(jnp.bfloat16)
    outgoing = jnp.einsum(
        "ks,xkr->xsr", send_map, kv_pages, preferred_element_type=jnp.float32
    ).astype(jnp.bfloat16)
    outgoing = outgoing.reshape(2, req_count, capacity, PAGE_ROWS * width)
    incoming = lax.all_to_all(outgoing, "req", split_axis=1, concat_axis=1, tiled=True)
    mine_mask = owners == my_index
    placing = mine_mask[:, :, None] & (
        order_in[:, :, None] == jnp.arange(capacity, dtype=jnp.int32)[None, None, :]
    )
    target = (page_map % slot_count)[:, :, None] == jnp.arange(slot_count, dtype=jnp.int32)[
        None, None, :
    ]
    routing = jnp.einsum(
        "skc,skt->sct",
        placing.astype(jnp.bfloat16),
        target.astype(jnp.bfloat16),
        preferred_element_type=jnp.float32,
    ).astype(jnp.bfloat16)
    incoming, queries = lax.optimization_barrier((incoming, queries))
    att_long = long_attention(
        my_index, queries[:LONG_DEV], rotated_key_rows[:LONG_DEV], stream_value_rows[:LONG_DEV]
    )
    att_short = short_attention(
        my_index,
        req_count,
        queries[LONG_DEV:],
        rotated_key_rows[LONG_DEV:],
        stream_value_rows[LONG_DEV:],
        short_pages,
        short_fill,
    )
    attended = jnp.concatenate([att_long, att_short])
    tp_count = lax.axis_size("tp")
    if tp_count == 2:
        tp_index = lax.axis_index("tp")
        half_rows = tok_rows // 2
        theirs = lax.dynamic_slice_in_dim(attended, (1 - tp_index) * half_rows, half_rows, 0)
        sent = jnp.dot(theirs, out_weight, preferred_element_type=jnp.float32).astype(jnp.bfloat16)
        received = lax.ppermute(sent, "tp", [(0, 1), (1, 0)])
        mine = lax.dynamic_slice_in_dim(attended, tp_index * half_rows, half_rows, 0)
        own = jnp.dot(mine, out_weight, preferred_element_type=jnp.float32).astype(jnp.bfloat16)
        first_group = jnp.where(tp_index == 0, own, received).astype(jnp.float32)
        second_group = jnp.where(tp_index == 0, received, own).astype(jnp.float32)
        mixed_out = (first_group + second_group).astype(jnp.bfloat16)
    else:
        mixed_out = lax.psum_scatter(
            jnp.dot(attended, out_weight, preferred_element_type=jnp.float32).astype(jnp.bfloat16),
            "tp",
            scatter_dimension=0,
            tiled=True,
        )
    written_cache = jnp.einsum(
        "sct,xscr->xtr", routing, incoming, preferred_element_type=jnp.float32
    ).astype(jnp.bfloat16)
    written_cache = written_cache.reshape(2, slot_count, PAGE_ROWS, width)
    return (mixed_out, written_cache)


def solution(mesh):
    in_specs = (P("req", "tp"), P("req", "tp"), P("req", "tp"), P("tp", None), P(), P(), P())
    out_specs = (P(("req", "tp"), None), P(None, "req", None, "tp"))
    return jax.shard_map(local, mesh=mesh, in_specs=in_specs, out_specs=out_specs, check_vma=False)
```

```python
import functools

import jax
import jax.numpy as jnp
from jax import lax
from jax.experimental import pallas as pl
from jax.experimental.pallas import tpu as pltpu
from jax.sharding import PartitionSpec as P

HEAD_SIZE = 128
LONG_DEV = 512
SHORT_DEV = 128
PAGE_ROWS = 16
BLOCK_TOKENS = 640
LONG_CHUNKS = 2


NEGATIVE_FILL = -1e30
LOG2_E = 1.4426950408889634


def short_layout(offset, short_pages, short_fill):
    page_id = offset // PAGE_ROWS
    page_ends = jnp.cumsum(short_pages)
    page_starts = page_ends - short_pages
    limits = page_starts * PAGE_ROWS + (short_pages - 1) * PAGE_ROWS + short_fill
    owner_hit = page_ends[None, :] <= page_id[:, None]
    prompt = jnp.sum(owner_hit.astype(jnp.int32), axis=1)
    select = jnp.arange(short_pages.shape[0], dtype=jnp.int32)[None, :] == prompt[:, None]
    begin_at = jnp.sum(jnp.where(select, page_starts[None, :], 0), axis=1) * PAGE_ROWS
    limit_at = jnp.sum(jnp.where(select, limits[None, :], 0), axis=1)
    return (prompt, offset - begin_at, offset < limit_at)


def flash_kernel(b_ref, q_ref, k_ref, v_ref, *refs, group, tq, tk, chunk_rows, chunk, first, last):
    if first:
        m_out, l_out, acc_out = refs[-3:]
        m_in, l_in, acc_in = m_out, l_out, acc_out
    elif last:
        m_in, l_in, acc_in, o_ref = refs
        m_out, l_out, acc_out = m_in, l_in, acc_in
    else:
        m_in, l_in, acc_in, m_out, l_out, acc_out = refs
    i = pl.program_id(1)
    t = pl.program_id(2)
    b = b_ref[0]
    per_tile = tk // chunk_rows
    scale = HEAD_SIZE ** (-0.5)
    log2_scale = scale * LOG2_E

    @pl.when(t == 0)
    def _init():
        if first:
            m_out[...] = jnp.full(m_out.shape, NEGATIVE_FILL, jnp.float32)
            l_out[...] = jnp.zeros(l_out.shape, jnp.float32)
            acc_out[...] = jnp.zeros(acc_out.shape, jnp.float32)
        elif not last:
            m_out[...] = m_in[...]
            l_out[...] = l_in[...]
            acc_out[...] = acc_in[...]

    def step(masked):
        k = k_ref[...]
        v = v_ref[...]
        v_ext = jnp.concatenate([v, jnp.ones(v.shape, v.dtype)], axis=1)
        if masked:
            rows = i * tq + lax.broadcasted_iota(jnp.int32, (tq, tk), 0)
            cols = lax.broadcasted_iota(jnp.int32, (tq, tk), 1)
            src = t * per_tile + cols // chunk_rows
            key_pos = chunk * chunk_rows + cols % chunk_rows
            allowed = (src < b) | ((src == b) & (key_pos <= rows))
        for g in range(group):
            qg = q_ref[:, g * HEAD_SIZE:(g + 1) * HEAD_SIZE]
            s = lax.dot_general(
                qg, k, (((1,), (1,)), ((), ())), preferred_element_type=jnp.float32
            )
            if masked:
                s = jnp.where(allowed, s, NEGATIVE_FILL)
            m_prev = m_out[g]
            m_new = jnp.maximum(m_prev, jnp.max(s, axis=1, keepdims=True) * scale)
            p = jnp.exp2(s * log2_scale - m_new[:, :1] * LOG2_E)
            alpha = jnp.exp2((m_prev - m_new) * LOG2_E)
            pv = lax.dot_general(
                p.astype(jnp.bfloat16), v_ext, (((1,), (0,)), ((), ())),
                preferred_element_type=jnp.float32,
            )
            l_out[g] = alpha * l_out[g] + pv[:, HEAD_SIZE:]
            acc_out[g] = acc_out[g] * alpha + pv[:, :HEAD_SIZE]
            m_out[g] = m_new

    @pl.when(t * per_tile + per_tile - 1 < b)
    def _full():
        step(False)

    @pl.when((t * per_tile + per_tile - 1 >= b) & (t * per_tile <= b))
    def _diag():
        step(True)

    if last:
        @pl.when(t == pl.num_programs(2) - 1)
        def _fin():
            for g in range(group):
                o_ref[:, g * HEAD_SIZE:(g + 1) * HEAD_SIZE] = (
                    acc_out[g] / l_out[g]
                ).astype(o_ref.dtype)


def long_attention_chunk(b_arr, q_long, kv_chunk, state, chunk, first, last):
    rows, q_cols = q_long.shape
    kv_cols = kv_chunk.shape[1] // 2
    heads_kv = kv_cols // HEAD_SIZE
    group = q_cols // kv_cols
    chunk_rows = LONG_DEV // LONG_CHUNKS
    total = kv_chunk.shape[0]
    tk = min(1024, total)
    per_tile = tk // chunk_rows
    tq = LONG_DEV
    kernel = functools.partial(
        flash_kernel, group=group, tq=tq, tk=tk, chunk_rows=chunk_rows, chunk=chunk,
        first=first, last=last,
    )
    state_shape = jax.ShapeDtypeStruct((heads_kv, group, rows, HEAD_SIZE), jnp.float32)
    state_spec = pl.BlockSpec((None, group, tq, HEAD_SIZE), lambda h, i, t, b: (h, 0, i, 0))
    kv_spec_k = pl.BlockSpec((tk, HEAD_SIZE), lambda h, i, t, b: (jnp.minimum(t, b[0] // per_tile), h))
    kv_spec_v = pl.BlockSpec(
        (tk, HEAD_SIZE), lambda h, i, t, b: (jnp.minimum(t, b[0] // per_tile), heads_kv + h)
    )
    q_spec = pl.BlockSpec((tq, group * HEAD_SIZE), lambda h, i, t, b: (i, h))
    in_specs = [q_spec, kv_spec_k, kv_spec_v]
    operands = [b_arr, q_long, kv_chunk, kv_chunk]
    aliases = {}
    if not first:
        in_specs += [state_spec] * 3
        operands += list(state)
    if last:
        out_specs = q_spec
        out_shape = jax.ShapeDtypeStruct((rows, q_cols), jnp.bfloat16)
    else:
        out_specs = [state_spec] * 3
        out_shape = [state_shape] * 3
        if not first:
            aliases = {4: 0, 5: 1, 6: 2}
    grid_spec = pltpu.PrefetchScalarGridSpec(
        num_scalar_prefetch=1,
        grid=(heads_kv, rows // tq, total // tk),
        in_specs=in_specs,
        out_specs=out_specs,
    )
    return pl.pallas_call(
        kernel,
        grid_spec=grid_spec,
        out_shape=out_shape,
        input_output_aliases=aliases,
        compiler_params=pltpu.CompilerParams(
            dimension_semantics=("arbitrary", "arbitrary", "arbitrary")
        ),
    )(*operands)


def long_attention(my_index, q_long, k_long, v_long):
    b_arr = jnp.reshape(my_index, (1,)).astype(jnp.int32)
    chunk_rows = LONG_DEV // LONG_CHUNKS
    state = None
    for c in range(LONG_CHUNKS):
        kv = jnp.concatenate(
            [k_long[c * chunk_rows:(c + 1) * chunk_rows], v_long[c * chunk_rows:(c + 1) * chunk_rows]],
            axis=1,
        )
        kv = lax.all_gather(kv, "req", axis=0, tiled=True)
        state = long_attention_chunk(
            b_arr, q_long, kv, state, c, c == 0, c == LONG_CHUNKS - 1
        )
    return state


def short_attention(my_index, req_count, q_short, k_short, v_short, short_pages, short_fill):
    heads_kv = k_short.shape[1] // HEAD_SIZE
    group = q_short.shape[1] // k_short.shape[1]
    perm = [(s, s + 1) for s in range(req_count - 1)]
    k_prev = lax.ppermute(k_short, "req", perm)
    v_prev = lax.ppermute(v_short, "req", perm)
    own_off = my_index * SHORT_DEV + jnp.arange(SHORT_DEV, dtype=jnp.int32)
    key_off = (my_index - 1) * SHORT_DEV + jnp.arange(2 * SHORT_DEV, dtype=jnp.int32)
    q_seg, q_pos, q_live = short_layout(own_off, short_pages, short_fill)
    k_seg, k_pos, k_live = short_layout(key_off, short_pages, short_fill)
    k_live = k_live & (key_off >= 0)
    allowed = (q_seg[:, None] == k_seg[None, :]) & (k_pos[None, :] <= q_pos[:, None]) & k_live[None, :]
    keys = jnp.concatenate([k_prev, k_short]).reshape(2 * SHORT_DEV, heads_kv, HEAD_SIZE)
    values = jnp.concatenate([v_prev, v_short]).reshape(2 * SHORT_DEV, heads_kv, HEAD_SIZE)
    qs = q_short.reshape(SHORT_DEV, heads_kv, group, HEAD_SIZE)
    scores = jnp.einsum(
        "qhgd,khd->hgqk", qs, keys, preferred_element_type=jnp.float32
    ) * HEAD_SIZE ** (-0.5)
    scores = jnp.where(allowed[None, None], scores, NEGATIVE_FILL)
    row_max = jnp.max(scores, axis=-1, keepdims=True)
    weights = jnp.exp(scores - row_max)
    denom = jnp.sum(weights, axis=-1)
    weighted = jnp.einsum(
        "hgqk,khd->qhgd", weights.astype(jnp.bfloat16), values, preferred_element_type=jnp.float32
    )
    attended = weighted / jnp.transpose(denom, (2, 0, 1))[..., None]
    attended = jnp.where(q_live[:, None, None, None], attended, 0.0)
    return attended.reshape(SHORT_DEV, -1).astype(jnp.bfloat16)


def local(
    queries,
    rotated_key_rows,
    stream_value_rows,
    out_weight,
    short_pages,
    short_fill,
    stream_page_table,
):
    req_count = lax.axis_size("req")
    my_index = lax.axis_index("req")
    tok_rows = queries.shape[0]
    pages_per = tok_rows // PAGE_ROWS
    capacity = (pages_per + req_count - 1) // req_count
    slot_count = capacity * req_count
    width = rotated_key_rows.shape[1]
    own_off = my_index * SHORT_DEV + jnp.arange(SHORT_DEV, dtype=jnp.int32)
    short_live = short_layout(own_off, short_pages, short_fill)[2]
    own_live = jnp.concatenate([jnp.ones((LONG_DEV,), bool), short_live])
    kv_rows = jnp.stack([rotated_key_rows, stream_value_rows])
    kv_rows = jnp.where(own_live[None, :, None], kv_rows, jnp.zeros_like(kv_rows))
    kv_pages = kv_rows.reshape(2, pages_per, PAGE_ROWS * width)
    page_map = stream_page_table.reshape(req_count, pages_per)
    owners = page_map // slot_count
    earlier = (
        jnp.arange(pages_per, dtype=jnp.int32)[:, None]
        > jnp.arange(pages_per, dtype=jnp.int32)[None, :]
    )
    matching = owners[:, :, None] == owners[:, None, :]
    order_in = jnp.sum((matching & earlier[None]).astype(jnp.int32), axis=2)
    my_owner = owners[my_index]
    my_order = order_in[my_index]
    send_map = (
        (my_owner * capacity + my_order)[:, None]
        == jnp.arange(slot_count, dtype=jnp.int32)[None, :]
    ).astype(jnp.bfloat16)
    outgoing = jnp.einsum(
        "ks,xkr->xsr", send_map, kv_pages, preferred_element_type=jnp.float32
    ).astype(jnp.bfloat16)
    outgoing = outgoing.reshape(2, req_count, capacity, PAGE_ROWS * width)
    incoming = lax.all_to_all(outgoing, "req", split_axis=1, concat_axis=1, tiled=True)
    mine_mask = owners == my_index
    placing = mine_mask[:, :, None] & (
        order_in[:, :, None] == jnp.arange(capacity, dtype=jnp.int32)[None, None, :]
    )
    target = (page_map % slot_count)[:, :, None] == jnp.arange(slot_count, dtype=jnp.int32)[
        None, None, :
    ]
    routing = jnp.einsum(
        "skc,skt->sct",
        placing.astype(jnp.bfloat16),
        target.astype(jnp.bfloat16),
        preferred_element_type=jnp.float32,
    ).astype(jnp.bfloat16)
    incoming, queries = lax.optimization_barrier((incoming, queries))
    att_long = long_attention(
        my_index, queries[:LONG_DEV], rotated_key_rows[:LONG_DEV], stream_value_rows[:LONG_DEV]
    )
    att_short = short_attention(
        my_index,
        req_count,
        queries[LONG_DEV:],
        rotated_key_rows[LONG_DEV:],
        stream_value_rows[LONG_DEV:],
        short_pages,
        short_fill,
    )
    attended = jnp.concatenate([att_long, att_short])
    tp_count = lax.axis_size("tp")
    if tp_count == 2:
        tp_index = lax.axis_index("tp")
        half_rows = tok_rows // 2
        theirs = lax.dynamic_slice_in_dim(attended, (1 - tp_index) * half_rows, half_rows, 0)
        sent = jnp.dot(theirs, out_weight, preferred_element_type=jnp.float32).astype(jnp.bfloat16)
        received = lax.ppermute(sent, "tp", [(0, 1), (1, 0)])
        mine = lax.dynamic_slice_in_dim(attended, tp_index * half_rows, half_rows, 0)
        own = jnp.dot(mine, out_weight, preferred_element_type=jnp.float32).astype(jnp.bfloat16)
        first_group = jnp.where(tp_index == 0, own, received).astype(jnp.float32)
        second_group = jnp.where(tp_index == 0, received, own).astype(jnp.float32)
        mixed_out = (first_group + second_group).astype(jnp.bfloat16)
    else:
        mixed_out = lax.psum_scatter(
            jnp.dot(attended, out_weight, preferred_element_type=jnp.float32).astype(jnp.bfloat16),
            "tp",
            scatter_dimension=0,
            tiled=True,
        )
    written_cache = jnp.einsum(
        "sct,xscr->xtr", routing, incoming, preferred_element_type=jnp.float32
    ).astype(jnp.bfloat16)
    written_cache = written_cache.reshape(2, slot_count, PAGE_ROWS, width)
    return (mixed_out, written_cache)


def solution(mesh):
    in_specs = (P("req", "tp"), P("req", "tp"), P("req", "tp"), P("tp", None), P(), P(), P())
    out_specs = (P(("req", "tp"), None), P(None, "req", None, "tp"))
    return jax.shard_map(local, mesh=mesh, in_specs=in_specs, out_specs=out_specs, check_vma=False)
```

```python
import functools

import jax
import jax.numpy as jnp
from jax import lax
from jax.experimental import pallas as pl
from jax.experimental.pallas import tpu as pltpu
from jax.sharding import PartitionSpec as P

HEAD_SIZE = 128
LONG_DEV = 512
SHORT_DEV = 128
PAGE_ROWS = 16
BLOCK_TOKENS = 640
LONG_CHUNKS = 2


NEGATIVE_FILL = -1e30
LOG2_E = 1.4426950408889634


def short_layout(offset, short_pages, short_fill):
    page_id = offset // PAGE_ROWS
    page_ends = jnp.cumsum(short_pages)
    page_starts = page_ends - short_pages
    limits = page_starts * PAGE_ROWS + (short_pages - 1) * PAGE_ROWS + short_fill
    owner_hit = page_ends[None, :] <= page_id[:, None]
    prompt = jnp.sum(owner_hit.astype(jnp.int32), axis=1)
    select = jnp.arange(short_pages.shape[0], dtype=jnp.int32)[None, :] == prompt[:, None]
    begin_at = jnp.sum(jnp.where(select, page_starts[None, :], 0), axis=1) * PAGE_ROWS
    limit_at = jnp.sum(jnp.where(select, limits[None, :], 0), axis=1)
    return (prompt, offset - begin_at, offset < limit_at)


def flash_kernel(b_ref, q_ref, k_ref, v_ref, *refs, group, tq, tk, chunk_rows, chunk, first, last):
    if first:
        m_out, l_out, acc_out = refs[-3:]
        m_in, l_in, acc_in = m_out, l_out, acc_out
    elif last:
        m_in, l_in, acc_in, o_ref = refs
        m_out, l_out, acc_out = m_in, l_in, acc_in
    else:
        m_in, l_in, acc_in, m_out, l_out, acc_out = refs
    i = pl.program_id(1)
    t = pl.program_id(2)
    b = b_ref[0]
    per_tile = tk // chunk_rows
    scale = HEAD_SIZE ** (-0.5)
    log2_scale = scale * LOG2_E

    @pl.when(t == 0)
    def _init():
        if first:
            m_out[...] = jnp.full(m_out.shape, NEGATIVE_FILL, jnp.float32)
            l_out[...] = jnp.zeros(l_out.shape, jnp.float32)
            acc_out[...] = jnp.zeros(acc_out.shape, jnp.float32)
        elif not last:
            m_out[...] = m_in[...]
            l_out[...] = l_in[...]
            acc_out[...] = acc_in[...]

    def step(masked):
        k = k_ref[...]
        v = v_ref[...]
        v_ext = jnp.concatenate([v, jnp.ones(v.shape, v.dtype)], axis=1)
        if masked:
            rows = i * tq + lax.broadcasted_iota(jnp.int32, (tq, tk), 0)
            cols = lax.broadcasted_iota(jnp.int32, (tq, tk), 1)
            src = t * per_tile + cols // chunk_rows
            key_pos = chunk * chunk_rows + cols % chunk_rows
            allowed = (src < b) | ((src == b) & (key_pos <= rows))
        for g in range(group):
            qg = q_ref[:, g * HEAD_SIZE:(g + 1) * HEAD_SIZE]
            s = lax.dot_general(
                qg, k, (((1,), (1,)), ((), ())), preferred_element_type=jnp.float32
            )
            if masked:
                s = jnp.where(allowed, s, NEGATIVE_FILL)
            m_prev = m_out[g]
            m_new = jnp.maximum(m_prev, jnp.max(s, axis=1, keepdims=True) * scale)
            p = jnp.exp2(s * log2_scale - m_new[:, :1] * LOG2_E)
            alpha = jnp.exp2((m_prev - m_new) * LOG2_E)
            pv = lax.dot_general(
                p.astype(jnp.bfloat16), v_ext, (((1,), (0,)), ((), ())),
                preferred_element_type=jnp.float32,
            )
            l_out[g] = alpha * l_out[g] + pv[:, HEAD_SIZE:]
            acc_out[g] = acc_out[g] * alpha + pv[:, :HEAD_SIZE]
            m_out[g] = m_new

    @pl.when(t * per_tile + per_tile - 1 < b)
    def _full():
        step(False)

    @pl.when((t * per_tile + per_tile - 1 >= b) & (t * per_tile <= b))
    def _diag():
        step(True)

    if last:
        @pl.when(t == pl.num_programs(2) - 1)
        def _fin():
            for g in range(group):
                o_ref[:, g * HEAD_SIZE:(g + 1) * HEAD_SIZE] = (
                    acc_out[g] / l_out[g]
                ).astype(o_ref.dtype)


def long_attention_chunk(b_arr, q_long, kv_chunk, state, chunk, first, last):
    rows, q_cols = q_long.shape
    kv_cols = kv_chunk.shape[1] // 2
    heads_kv = kv_cols // HEAD_SIZE
    group = q_cols // kv_cols
    chunk_rows = LONG_DEV // LONG_CHUNKS
    total = kv_chunk.shape[0]
    tk = min(2048, total)
    per_tile = tk // chunk_rows
    tq = LONG_DEV
    kernel = functools.partial(
        flash_kernel, group=group, tq=tq, tk=tk, chunk_rows=chunk_rows, chunk=chunk,
        first=first, last=last,
    )
    state_shape = jax.ShapeDtypeStruct((heads_kv, group, rows, HEAD_SIZE), jnp.float32)
    state_spec = pl.BlockSpec((None, group, tq, HEAD_SIZE), lambda h, i, t, b: (h, 0, i, 0))
    kv_spec_k = pl.BlockSpec((tk, HEAD_SIZE), lambda h, i, t, b: (jnp.minimum(t, b[0] // per_tile), h))
    kv_spec_v = pl.BlockSpec(
        (tk, HEAD_SIZE), lambda h, i, t, b: (jnp.minimum(t, b[0] // per_tile), heads_kv + h)
    )
    q_spec = pl.BlockSpec((tq, group * HEAD_SIZE), lambda h, i, t, b: (i, h))
    in_specs = [q_spec, kv_spec_k, kv_spec_v]
    operands = [b_arr, q_long, kv_chunk, kv_chunk]
    aliases = {}
    if not first:
        in_specs += [state_spec] * 3
        operands += list(state)
    if last:
        out_specs = q_spec
        out_shape = jax.ShapeDtypeStruct((rows, q_cols), jnp.bfloat16)
    else:
        out_specs = [state_spec] * 3
        out_shape = [state_shape] * 3
        if not first:
            aliases = {4: 0, 5: 1, 6: 2}
    grid_spec = pltpu.PrefetchScalarGridSpec(
        num_scalar_prefetch=1,
        grid=(heads_kv, rows // tq, total // tk),
        in_specs=in_specs,
        out_specs=out_specs,
    )
    return pl.pallas_call(
        kernel,
        grid_spec=grid_spec,
        out_shape=out_shape,
        input_output_aliases=aliases,
        compiler_params=pltpu.CompilerParams(
            dimension_semantics=("arbitrary", "arbitrary", "arbitrary")
        ),
    )(*operands)


def long_attention(my_index, q_long, k_long, v_long):
    b_arr = jnp.reshape(my_index, (1,)).astype(jnp.int32)
    chunk_rows = LONG_DEV // LONG_CHUNKS
    state = None
    for c in range(LONG_CHUNKS):
        kv = jnp.concatenate(
            [k_long[c * chunk_rows:(c + 1) * chunk_rows], v_long[c * chunk_rows:(c + 1) * chunk_rows]],
            axis=1,
        )
        kv = lax.all_gather(kv, "req", axis=0, tiled=True)
        state = long_attention_chunk(
            b_arr, q_long, kv, state, c, c == 0, c == LONG_CHUNKS - 1
        )
    return state


def short_attention(my_index, req_count, q_short, k_short, v_short, short_pages, short_fill):
    heads_kv = k_short.shape[1] // HEAD_SIZE
    group = q_short.shape[1] // k_short.shape[1]
    perm = [(s, s + 1) for s in range(req_count - 1)]
    k_prev = lax.ppermute(k_short, "req", perm)
    v_prev = lax.ppermute(v_short, "req", perm)
    own_off = my_index * SHORT_DEV + jnp.arange(SHORT_DEV, dtype=jnp.int32)
    key_off = (my_index - 1) * SHORT_DEV + jnp.arange(2 * SHORT_DEV, dtype=jnp.int32)
    q_seg, q_pos, q_live = short_layout(own_off, short_pages, short_fill)
    k_seg, k_pos, k_live = short_layout(key_off, short_pages, short_fill)
    k_live = k_live & (key_off >= 0)
    allowed = (q_seg[:, None] == k_seg[None, :]) & (k_pos[None, :] <= q_pos[:, None]) & k_live[None, :]
    keys = jnp.concatenate([k_prev, k_short]).reshape(2 * SHORT_DEV, heads_kv, HEAD_SIZE)
    values = jnp.concatenate([v_prev, v_short]).reshape(2 * SHORT_DEV, heads_kv, HEAD_SIZE)
    qs = q_short.reshape(SHORT_DEV, heads_kv, group, HEAD_SIZE)
    scores = jnp.einsum(
        "qhgd,khd->hgqk", qs, keys, preferred_element_type=jnp.float32
    ) * HEAD_SIZE ** (-0.5)
    scores = jnp.where(allowed[None, None], scores, NEGATIVE_FILL)
    row_max = jnp.max(scores, axis=-1, keepdims=True)
    weights = jnp.exp(scores - row_max)
    denom = jnp.sum(weights, axis=-1)
    weighted = jnp.einsum(
        "hgqk,khd->qhgd", weights.astype(jnp.bfloat16), values, preferred_element_type=jnp.float32
    )
    attended = weighted / jnp.transpose(denom, (2, 0, 1))[..., None]
    attended = jnp.where(q_live[:, None, None, None], attended, 0.0)
    return attended.reshape(SHORT_DEV, -1).astype(jnp.bfloat16)


def local(
    queries,
    rotated_key_rows,
    stream_value_rows,
    out_weight,
    short_pages,
    short_fill,
    stream_page_table,
):
    req_count = lax.axis_size("req")
    my_index = lax.axis_index("req")
    tok_rows = queries.shape[0]
    pages_per = tok_rows // PAGE_ROWS
    capacity = (pages_per + req_count - 1) // req_count
    slot_count = capacity * req_count
    width = rotated_key_rows.shape[1]
    own_off = my_index * SHORT_DEV + jnp.arange(SHORT_DEV, dtype=jnp.int32)
    short_live = short_layout(own_off, short_pages, short_fill)[2]
    own_live = jnp.concatenate([jnp.ones((LONG_DEV,), bool), short_live])
    kv_rows = jnp.stack([rotated_key_rows, stream_value_rows])
    kv_rows = jnp.where(own_live[None, :, None], kv_rows, jnp.zeros_like(kv_rows))
    kv_pages = kv_rows.reshape(2, pages_per, PAGE_ROWS * width)
    page_map = stream_page_table.reshape(req_count, pages_per)
    owners = page_map // slot_count
    earlier = (
        jnp.arange(pages_per, dtype=jnp.int32)[:, None]
        > jnp.arange(pages_per, dtype=jnp.int32)[None, :]
    )
    matching = owners[:, :, None] == owners[:, None, :]
    order_in = jnp.sum((matching & earlier[None]).astype(jnp.int32), axis=2)
    my_owner = owners[my_index]
    my_order = order_in[my_index]
    send_map = (
        (my_owner * capacity + my_order)[:, None]
        == jnp.arange(slot_count, dtype=jnp.int32)[None, :]
    ).astype(jnp.bfloat16)
    outgoing = jnp.einsum(
        "ks,xkr->xsr", send_map, kv_pages, preferred_element_type=jnp.float32
    ).astype(jnp.bfloat16)
    outgoing = outgoing.reshape(2, req_count, capacity, PAGE_ROWS * width)
    incoming = lax.all_to_all(outgoing, "req", split_axis=1, concat_axis=1, tiled=True)
    mine_mask = owners == my_index
    placing = mine_mask[:, :, None] & (
        order_in[:, :, None] == jnp.arange(capacity, dtype=jnp.int32)[None, None, :]
    )
    target = (page_map % slot_count)[:, :, None] == jnp.arange(slot_count, dtype=jnp.int32)[
        None, None, :
    ]
    routing = jnp.einsum(
        "skc,skt->sct",
        placing.astype(jnp.bfloat16),
        target.astype(jnp.bfloat16),
        preferred_element_type=jnp.float32,
    ).astype(jnp.bfloat16)
    incoming, queries = lax.optimization_barrier((incoming, queries))
    att_long = long_attention(
        my_index, queries[:LONG_DEV], rotated_key_rows[:LONG_DEV], stream_value_rows[:LONG_DEV]
    )
    att_short = short_attention(
        my_index,
        req_count,
        queries[LONG_DEV:],
        rotated_key_rows[LONG_DEV:],
        stream_value_rows[LONG_DEV:],
        short_pages,
        short_fill,
    )
    attended = jnp.concatenate([att_long, att_short])
    tp_count = lax.axis_size("tp")
    if tp_count == 2:
        tp_index = lax.axis_index("tp")
        half_rows = tok_rows // 2
        theirs = lax.dynamic_slice_in_dim(attended, (1 - tp_index) * half_rows, half_rows, 0)
        sent = jnp.dot(theirs, out_weight, preferred_element_type=jnp.float32).astype(jnp.bfloat16)
        received = lax.ppermute(sent, "tp", [(0, 1), (1, 0)])
        mine = lax.dynamic_slice_in_dim(attended, tp_index * half_rows, half_rows, 0)
        own = jnp.dot(mine, out_weight, preferred_element_type=jnp.float32).astype(jnp.bfloat16)
        first_group = jnp.where(tp_index == 0, own, received).astype(jnp.float32)
        second_group = jnp.where(tp_index == 0, received, own).astype(jnp.float32)
        mixed_out = (first_group + second_group).astype(jnp.bfloat16)
    else:
        mixed_out = lax.psum_scatter(
            jnp.dot(attended, out_weight, preferred_element_type=jnp.float32).astype(jnp.bfloat16),
            "tp",
            scatter_dimension=0,
            tiled=True,
        )
    written_cache = jnp.einsum(
        "sct,xscr->xtr", routing, incoming, preferred_element_type=jnp.float32
    ).astype(jnp.bfloat16)
    written_cache = written_cache.reshape(2, slot_count, PAGE_ROWS, width)
    return (mixed_out, written_cache)


def solution(mesh):
    in_specs = (P("req", "tp"), P("req", "tp"), P("req", "tp"), P("tp", None), P(), P(), P())
    out_specs = (P(("req", "tp"), None), P(None, "req", None, "tp"))
    return jax.shard_map(local, mesh=mesh, in_specs=in_specs, out_specs=out_specs, check_vma=False)
```
